32 devices in a mesh: lat: 8 (over z, core), lon: 4 (over y, x).
Axes of the slice: x: 2, y: 2, z: 4, core: 2. Of those that a mesh axis runs over, the one named last changes fastest.
Arguments:
- elem_codes: int32 [128, 32, 256], P('lat', 'lon'), may hold values from 32 to 207, as said below
- block_exps: int32 [128, 32, 8], P('lat', 'lon'), may hold values from -2 to 1
- up_kernel: bfloat16 [4, 4, 256, 128], replicated, may hold values from -0.1875 to 0.1875
- up_bias: float32 [128], replicated, may hold values from -3 to 3
- mix_kernel: bfloat16 [3, 3, 128, 128], replicated, may hold values from -0.1875 to 0.1875
- cotangent: bfloat16 [256, 64, 128], P('lat', 'lon'), may hold values from -6 to 6
Outputs:
- section_out: bfloat16 [256, 64, 128], P('lat', 'lon')
- input_grad: float32 [128, 32, 256], P('lat', 'lon')
- up_grad: float32 [4, 4, 256, 128], P(None, None, 'lon')
- mix_grad: float32 [3, 3, 128, 128], P(None, None, 'lon')
The draws below stay inside these ranges and needn't reach their ends.
Inputs may be any that keep to these rules, and one draw needn't show every extreme that they name: `elem_codes`: every code has a sign bit of weight 128, a four-bit exponent field from 4 to 9 and a three-bit mantissa.
All inputs are finite; a program needn't handle non-finite values.
Results may differ from the reference program's by a relative error of at most 0.012.
Values may be sent and summed in bfloat16 or wider, within the bound.
No kernel may reach another device: no remote copies, remote signals or barrier semaphores. Data moves between devices by JAX's collectives and lax.ppermute only.
A program may use at most 64 MiB of HBM per device.

```python
import math
import jax
import jax.numpy as jnp
from jax import lax

CIN = 256
COUT = 128
BLOCK = 32
IN_ROWS = 128
IN_COLS = 32
OUT_ROWS = 256
OUT_COLS = 64
SB = 8


def draw_elem_codes(key, part):
    sign_key, exponent_key, mantissa_key = jax.random.split(key, 3)
    shape = (IN_ROWS, IN_COLS, CIN)
    sign_bit = jax.random.randint(sign_key, shape, 0, 2)
    exponent = jax.random.randint(exponent_key, shape, 4, 10)
    mantissa = jax.random.randint(mantissa_key, shape, 0, 8)
    return (sign_bit * 128 + exponent * 8 + mantissa).astype(jnp.int32)


def with_ends(array, key, smallest, top_value):
    longest = array.shape.index(max(array.shape))
    spots = []
    for shift in (0, 1):
        where = [jax.random.randint(jax.random.fold_in(key, axis), (), 0, length) for axis, length in enumerate(array.shape)]
        where[longest] = (where[longest] + shift) % array.shape[longest]
        spots.append(tuple(where))
    return array.at[spots[0]].set(smallest).at[spots[1]].set(top_value)


def levels(own_key, extent, pieces, low, top_value):
    def one(dim, blocks):
        steps = jax.random.uniform(jax.random.fold_in(jax.random.fold_in(own_key, 6), dim), (blocks,), jnp.float32, low / len(pieces), top_value / len(pieces))
        return jnp.repeat(jnp.exp(steps), extent[dim] // blocks).reshape((-1,) + (1,) * (len(extent) - dim - 1))

    level = one(*pieces[0])
    for cut in pieces[1:]:
        level = level * one(*cut)
    return level


def centred(stream_key, extent, width, limit, shards=(), dtype=jnp.bfloat16):
    entries = width * jax.random.normal(stream_key, extent, jnp.float32)
    if shards:
        entries = entries * levels(stream_key, extent, shards, -0.22, 0.18)
    return jnp.clip(entries, -limit, limit).astype(dtype)


def setup_inputs(seed: int = 0) -> dict:
    seeds = jax.random.split(jax.random.key(seed), 7)
    elem_codes = draw_elem_codes(jax.random.fold_in(seeds[6], 71), 0)
    block_exps = with_ends(jax.random.randint(seeds[1], (IN_ROWS, IN_COLS, SB), -2, 2), jax.random.fold_in(seeds[1], 1), -2, 1).astype(jnp.int32)
    up_kernel = centred(seeds[2], (4, 4, CIN, COUT), (4 * CIN) ** -0.5, 0.1875)
    up_bias = centred(seeds[3], (COUT,), 0.5, 3.0, (), jnp.float32)
    mix_kernel = centred(seeds[4], (3, 3, COUT, COUT), (9 * COUT) ** -0.5, 0.1875)
    cotangent = centred(seeds[5], (OUT_ROWS, OUT_COLS, COUT), 1.0, 6.0, ((0, 8), (1, 4)))
    return {"elem_codes": elem_codes, "block_exps": block_exps, "up_kernel": up_kernel, "up_bias": up_bias, "mix_kernel": mix_kernel, "cotangent": cotangent}


row_taps = (((1, 0), (3, -1)), ((0, 1), (2, 0)))

def decode(elem_codes, block_exps):
    sign_bit = elem_codes // 128
    exponent = elem_codes // 8 % 16
    mantissa = elem_codes % 8
    magnitude = jnp.exp2((exponent - 7).astype(jnp.float32)) * (1.0 + mantissa.astype(jnp.float32) / 8.0)
    signed = jnp.where(sign_bit == 1, -magnitude, magnitude)
    factor = jnp.repeat(jnp.exp2(block_exps.astype(jnp.float32)), BLOCK, axis=2)
    return (signed * factor).astype(jnp.bfloat16)

def extend(field, margin):
    widened = jnp.concatenate([field[:, -margin:], field, field[:, :margin]], axis=1)
    return jnp.pad(widened, ((margin, margin), (0, 0), (0, 0)))

def slope(pre_act):
    plain = pre_act.astype(jnp.float32)
    sigmoid_v = jax.nn.sigmoid(plain)
    return sigmoid_v * (1.0 + plain * (1.0 - sigmoid_v))

def matmul(left, right):
    return jnp.einsum('rcm,mn->rcn', left, right, precision=lax.Precision.HIGHEST)

def reference(elem_codes, block_exps, up_kernel, up_bias, mix_kernel, cotangent):
    inputs = decode(elem_codes, block_exps).astype(jnp.float32)
    up_wide = up_kernel.astype(jnp.float32)
    mix_wide = mix_kernel.astype(jnp.float32)
    grad_wide = cotangent.astype(jnp.float32)
    in_rows, in_cols = (inputs.shape[0], inputs.shape[1])
    out_rows, out_cols = (2 * in_rows, 2 * in_cols)
    padded_in = extend(inputs, 1)
    halves = []
    for row_par in range(2):
        lane_list = []
        for col_par in range(2):
            total = jnp.zeros((in_rows, in_cols, COUT), jnp.float32)
            for row_tap, row_off in row_taps[row_par]:
                for col_tap, col_off in row_taps[col_par]:
                    window = padded_in[1 + row_off:1 + row_off + in_rows, 1 + col_off:1 + col_off + in_cols]
                    total = total + matmul(window, up_wide[row_tap, col_tap])
            lane_list.append(total)
        halves.append(jnp.stack(lane_list, axis=2))
    raw = jnp.stack(halves, axis=1).reshape(out_rows, out_cols, COUT)
    pre_act = (raw + up_bias).astype(jnp.bfloat16)
    activated = jax.nn.silu(pre_act.astype(jnp.float32)).astype(jnp.bfloat16)
    act_pad = extend(activated.astype(jnp.float32), 1)
    grad_pad = extend(grad_wide, 1)
    grad_scale = 1.0 / math.sqrt(OUT_ROWS * OUT_COLS)
    total = jnp.zeros((out_rows, out_cols, COUT), jnp.float32)
    act_grad = jnp.zeros((out_rows, out_cols, COUT), jnp.float32)
    mix_list = []
    for row_tap in range(3):
        for col_tap in range(3):
            window = act_pad[row_tap:row_tap + out_rows, col_tap:col_tap + out_cols]
            total = total + matmul(window, mix_wide[row_tap, col_tap])
            flipped = grad_pad[2 - row_tap:2 - row_tap + out_rows, 2 - col_tap:2 - col_tap + out_cols]
            act_grad = act_grad + matmul(flipped, mix_wide[row_tap, col_tap].T)
            mix_list.append(jnp.einsum('rcm,rcn->mn', window, grad_wide, precision=lax.Precision.HIGHEST))
    section_out = total.astype(jnp.bfloat16)
    mix_grad = jnp.stack(mix_list, axis=0).reshape(3, 3, COUT, COUT) * grad_scale
    pre_grad = (act_grad * slope(pre_act)).astype(jnp.bfloat16)
    pre_pad = extend(pre_grad.astype(jnp.float32), 1)
    input_grad = jnp.zeros((in_rows, in_cols, CIN), jnp.float32)
    up_list = []
    for row_tap in range(4):
        for col_tap in range(4):
            window = pre_pad[row_tap:row_tap + 2 * in_rows:2, col_tap:col_tap + 2 * in_cols:2]
            input_grad = input_grad + matmul(window, up_wide[row_tap, col_tap].T)
            up_list.append(jnp.einsum('rcm,rcn->mn', inputs, window, precision=lax.Precision.HIGHEST))
    up_grad = jnp.stack(up_list, axis=0).reshape(4, 4, CIN, COUT) * grad_scale
    return (section_out, input_grad, up_grad, mix_grad)
```

```python
import math

import jax
import jax.numpy as jnp
from jax import lax
from jax.sharding import PartitionSpec as P

CIN = 256
COUT = 128
BLOCK = 32


row_taps = (((1, 0), (3, -1)), ((0, 1), (2, 0)))


def padded_2(array, sides, width, wrap):
    for axis, dim in sides:
        size, length = (lax.axis_size(axis), array.shape[dim])
        up = [(i, (i + 1) % size) for i in range(size if wrap else size - 1)]
        down = [(j, i) for i, j in up]
        last = lax.slice_in_dim(array, length - width, length, axis=dim)
        leading = lax.slice_in_dim(array, 0, width, axis=dim)
        before = lax.ppermute(last, axis, up)
        after = lax.ppermute(leading, axis, down)
        array = jnp.concatenate([before, array, after], axis=dim)
    return array


def decode(elem_codes, block_exps):
    sign_bit = elem_codes // 128
    exponent = elem_codes // 8 % 16
    mantissa = elem_codes % 8
    magnitude = jnp.exp2((exponent - 7).astype(jnp.float32)) * (
        1.0 + mantissa.astype(jnp.float32) / 8.0
    )
    signed = jnp.where(sign_bit == 1, -magnitude, magnitude)
    factor = jnp.repeat(jnp.exp2(block_exps.astype(jnp.float32)), BLOCK, axis=2)
    return (signed * factor).astype(jnp.bfloat16)


def extend(field, margin):
    widened = padded_2(field, (("lon", 1),), margin, True)
    return padded_2(widened, (("lat", 0),), margin, False)


def slope(pre_act):
    plain = pre_act.astype(jnp.float32)
    sigmoid_v = jax.nn.sigmoid(plain)
    return sigmoid_v * (1.0 + plain * (1.0 - sigmoid_v))


def upsample(padded, up_kernel, row_count, col_count):
    halves = []
    for row_par in range(2):
        lane_list = []
        for col_par in range(2):
            pieces = []
            kernels = []
            for row_tap, row_off in row_taps[row_par]:
                for col_tap, col_off in row_taps[col_par]:
                    pieces.append(
                        padded[
                            1 + row_off : 1 + row_off + row_count,
                            1 + col_off : 1 + col_off + col_count,
                        ]
                    )
                    kernels.append(up_kernel[row_tap, col_tap])
            stacked = jnp.concatenate(pieces, axis=2)
            kernel = jnp.concatenate(kernels, axis=0)
            lane_list.append(
                jnp.einsum("rck,kn->rcn", stacked, kernel, preferred_element_type=jnp.float32)
            )
        halves.append(jnp.stack(lane_list, axis=2))
    merged = jnp.stack(halves, axis=1)
    return merged.reshape(2 * row_count, 2 * col_count, merged.shape[-1])


def neighbours(padded, row_count, col_count, flipped):
    pieces = []
    for row_tap in range(3):
        for col_tap in range(3):
            row_at = 2 - row_tap if flipped else row_tap
            col_at = 2 - col_tap if flipped else col_tap
            pieces.append(padded[row_at : row_at + row_count, col_at : col_at + col_count])
    return jnp.concatenate(pieces, axis=2)


def strided(padded, row_count, col_count):
    pieces = []
    for row_tap in range(4):
        for col_tap in range(4):
            pieces.append(
                padded[row_tap : row_tap + 2 * row_count : 2, col_tap : col_tap + 2 * col_count : 2]
            )
    return jnp.concatenate(pieces, axis=2)


def shards(elem_codes, block_exps, up_kernel, up_bias, mix_kernel, cotangent):
    inputs = decode(elem_codes, block_exps)
    in_rows, in_cols = (inputs.shape[0], inputs.shape[1])
    out_rows, out_cols = (2 * in_rows, 2 * in_cols)
    lat_count = lax.axis_size("lat")
    lon_count = lax.axis_size("lon")
    back_mix = mix_kernel.transpose(0, 1, 3, 2).reshape(9 * COUT, COUT)
    padded_in = extend(inputs, 1)
    raw = upsample(padded_in, up_kernel, in_rows, in_cols)
    pre_act = (raw + up_bias).astype(jnp.bfloat16)
    act_pad = extend(jax.nn.silu(pre_act.astype(jnp.float32)).astype(jnp.bfloat16), 1)
    grad_pad = extend(cotangent, 1)
    act_grad = jnp.einsum(
        "rck,kn->rcn",
        neighbours(grad_pad, out_rows, out_cols, True),
        back_mix,
        preferred_element_type=jnp.float32,
    )
    pre_grad_pad = extend((act_grad * slope(pre_act)).astype(jnp.bfloat16), 1)
    patches = neighbours(act_pad, out_rows, out_cols, False)
    mix_flat = mix_kernel.reshape(9 * COUT, COUT)
    section_out = jnp.einsum(
        "rck,kn->rcn", patches, mix_flat, preferred_element_type=jnp.float32
    ).astype(jnp.bfloat16)
    grad_scale = 1.0 / math.sqrt(out_rows * lat_count * out_cols * lon_count)
    mix_flat_grad = jnp.einsum(
        "rctm,rcn->mtn",
        patches.reshape(out_rows, out_cols, 9, COUT),
        cotangent,
        preferred_element_type=jnp.float32,
    )
    grad_patches = strided(pre_grad_pad, in_rows, in_cols)
    back_up = up_kernel.transpose(0, 1, 3, 2).reshape(16 * COUT, CIN)
    input_grad = jnp.einsum(
        "rck,kn->rcn", grad_patches, back_up, preferred_element_type=jnp.float32
    )
    up_flat = jnp.einsum("rcm,rck->mk", inputs, grad_patches, preferred_element_type=jnp.float32)
    up_span = CIN // lon_count
    mix_span = COUT // lon_count
    up_size = up_span * 16 * COUT
    terms = jnp.concatenate(
        [up_flat.reshape(lon_count, up_size), mix_flat_grad.reshape(lon_count, -1)], axis=1
    )
    summed = reduce_terms(terms) * grad_scale
    up_part = summed[:up_size].reshape(up_span, 4, 4, COUT).transpose(1, 2, 0, 3)
    mix_part = summed[up_size:].reshape(mix_span, 3, 3, COUT).transpose(1, 2, 0, 3)
    return (section_out, input_grad, up_part, mix_part)


def exchange(part, axis, step):
    size = lax.axis_size(axis)
    return lax.ppermute(part, axis, [(i, i ^ step) for i in range(size)])


def halve(buffer, axis, step, dim):
    own = lax.axis_index(axis) // step % 2
    keep = lax.dynamic_index_in_dim(buffer, own, dim, keepdims=False)
    send = lax.dynamic_index_in_dim(buffer, 1 - own, dim, keepdims=False)
    return keep + exchange(send, axis, step)


def double(part, axis, step):
    own = lax.axis_index(axis) // step % 2
    got = exchange(part, axis, step)
    low = jnp.where(own == 0, part, got)
    high = jnp.where(own == 0, got, part)
    return jnp.concatenate([low, high])


def steps_of(size):
    count = size.bit_length() - 1
    return [1 << k for k in range(count)] if size == 1 << count else None


def scatter_lon(rows, order):
    lon_count = rows.shape[0]
    steps = steps_of(lon_count)
    width = len(steps)
    grid = rows.reshape((2,) * width + rows.shape[1:])
    held = list(reversed(steps))
    for step in order:
        dim = held.index(step)
        grid = halve(grid, "lon", step, dim)
        held.pop(dim)
    return grid


def reduce_lat(flat):
    steps = steps_of(lax.axis_size("lat"))
    if steps is None or flat.shape[0] % (1 << len(steps)):
        return lax.psum(flat, "lat")
    for step in steps:
        flat = halve(flat.reshape(2, -1), "lat", step, 0)
    for step in reversed(steps):
        flat = double(flat, "lat", step)
    return flat


def reduce_terms(rows):
    lon_count = rows.shape[0]
    steps = steps_of(lon_count)
    if steps is None or rows.shape[1] % 2:
        own = lax.axis_index("lon")
        mine = lax.dynamic_index_in_dim(lax.psum(rows, "lon"), own, 0, keepdims=False)
        return reduce_lat(mine)
    half = rows.shape[1] // 2
    first = scatter_lon(rows[:, :half], steps)
    second = scatter_lon(rows[:, half:], list(reversed(steps)))
    return jnp.concatenate([reduce_lat(first), reduce_lat(second)])


def solution(mesh):
    placed = (P("lat", "lon", None), P("lat", "lon", None), P(), P(), P(), P("lat", "lon", None))
    return jax.shard_map(
        shards,
        mesh=mesh,
        in_specs=placed,
        out_specs=(
            P("lat", "lon", None),
            P("lat", "lon", None),
            P(None, None, "lon", None),
            P(None, None, "lon", None),
        ),
        check_vma=False,
    )
```

```python
import math

import jax
import jax.numpy as jnp
from jax import lax
from jax.sharding import PartitionSpec as P

CIN = 256
COUT = 128
BLOCK = 32


row_taps = (((1, 0), (3, -1)), ((0, 1), (2, 0)))


def swap_edges(fields, margins, axis, dim, wrap):
    size = lax.axis_size(axis)
    up = [(i, (i + 1) % size) for i in range(size if wrap else size - 1)]
    down = [(j, i) for i, j in up]
    lasts, leads = [], []
    for field, width in zip(fields, margins):
        length = field.shape[dim]
        lasts.append(lax.slice_in_dim(field, length - width, length, axis=dim))
        leads.append(lax.slice_in_dim(field, 0, width, axis=dim))
    before = lax.ppermute(jnp.concatenate([p.reshape(-1) for p in lasts]), axis, up)
    after = lax.ppermute(jnp.concatenate([p.reshape(-1) for p in leads]), axis, down)
    joined, at = [], 0
    for field, last, lead in zip(fields, lasts, leads):
        count = last.size
        head = before[at : at + count].reshape(last.shape)
        tail = after[at : at + count].reshape(lead.shape)
        joined.append(jnp.concatenate([head, field, tail], axis=dim))
        at += count
    return joined


def extend_all(fields, margins):
    widened = swap_edges(fields, margins, "lon", 1, True)
    return swap_edges(widened, margins, "lat", 0, False)


def decode(elem_codes, block_exps):
    sign_bit = elem_codes // 128
    exponent = elem_codes // 8 % 16
    mantissa = elem_codes % 8
    magnitude = jnp.exp2((exponent - 7).astype(jnp.float32)) * (
        1.0 + mantissa.astype(jnp.float32) / 8.0
    )
    signed = jnp.where(sign_bit == 1, -magnitude, magnitude)
    factor = jnp.repeat(jnp.exp2(block_exps.astype(jnp.float32)), BLOCK, axis=2)
    return (signed * factor).astype(jnp.bfloat16)


def slope(pre_act):
    plain = pre_act.astype(jnp.float32)
    sigmoid_v = jax.nn.sigmoid(plain)
    return sigmoid_v * (1.0 + plain * (1.0 - sigmoid_v))


def upsample(padded, up_kernel, row_count, col_count):
    halves = []
    for row_par in (1, 0):
        lane_list = []
        for col_par in (1, 0):
            pieces = []
            kernels = []
            for row_tap, row_off in row_taps[row_par]:
                for col_tap, col_off in row_taps[col_par]:
                    row_at = 1 + row_off - row_par
                    col_at = 1 + col_off - col_par
                    pieces.append(
                        padded[row_at : row_at + row_count + 1, col_at : col_at + col_count + 1]
                    )
                    kernels.append(up_kernel[row_tap, col_tap])
            stacked = jnp.concatenate(pieces, axis=2)
            kernel = jnp.concatenate(kernels, axis=0)
            lane_list.append(
                jnp.einsum("rck,kn->rcn", stacked, kernel, preferred_element_type=jnp.float32)
            )
        halves.append(jnp.stack(lane_list, axis=2))
    merged = jnp.stack(halves, axis=1)
    return merged.reshape(2 * row_count + 2, 2 * col_count + 2, merged.shape[-1])


def neighbours(padded, row_count, col_count, flipped):
    pieces = []
    for row_tap in range(3):
        for col_tap in range(3):
            row_at = 2 - row_tap if flipped else row_tap
            col_at = 2 - col_tap if flipped else col_tap
            pieces.append(padded[row_at : row_at + row_count, col_at : col_at + col_count])
    return jnp.concatenate(pieces, axis=2)


def strided(padded, row_count, col_count):
    pieces = []
    for row_tap in range(4):
        for col_tap in range(4):
            pieces.append(
                padded[row_tap : row_tap + 2 * row_count : 2, col_tap : col_tap + 2 * col_count : 2]
            )
    return jnp.concatenate(pieces, axis=2)


def shards(elem_codes, block_exps, up_kernel, up_bias, mix_kernel, cotangent):
    inputs = decode(elem_codes, block_exps)
    in_rows, in_cols = (inputs.shape[0], inputs.shape[1])
    out_rows, out_cols = (2 * in_rows, 2 * in_cols)
    lat_count = lax.axis_size("lat")
    lon_count = lax.axis_size("lon")
    back_mix = mix_kernel.transpose(0, 1, 3, 2).reshape(9 * COUT, COUT)
    padded_in, grad_pad = extend_all((inputs, cotangent), (1, 2))
    raw = upsample(padded_in, up_kernel, in_rows, in_cols)
    pre_act = (raw + up_bias).astype(jnp.bfloat16)
    row_at = lax.axis_index("lat") * out_rows - 1 + lax.broadcasted_iota(jnp.int32, (out_rows + 2, 1, 1), 0)
    inside = (row_at >= 0) & (row_at < out_rows * lat_count)
    activated = jax.nn.silu(pre_act.astype(jnp.float32)).astype(jnp.bfloat16)
    act_pad = jnp.where(inside, activated, jnp.zeros_like(activated))
    act_grad = jnp.einsum(
        "rck,kn->rcn",
        neighbours(grad_pad, out_rows + 2, out_cols + 2, True),
        back_mix,
        preferred_element_type=jnp.float32,
    )
    pre_grad = (act_grad * slope(pre_act)).astype(jnp.bfloat16)
    pre_grad_pad = jnp.where(inside, pre_grad, jnp.zeros_like(pre_grad))
    patches = neighbours(act_pad, out_rows, out_cols, False)
    mix_flat = mix_kernel.reshape(9 * COUT, COUT)
    section_out = jnp.einsum(
        "rck,kn->rcn", patches, mix_flat, preferred_element_type=jnp.float32
    ).astype(jnp.bfloat16)
    grad_scale = 1.0 / math.sqrt(out_rows * lat_count * out_cols * lon_count)
    mix_flat_grad = jnp.einsum(
        "rctm,rcn->mtn",
        patches.reshape(out_rows, out_cols, 9, COUT),
        cotangent,
        preferred_element_type=jnp.float32,
    )
    grad_patches = strided(pre_grad_pad, in_rows, in_cols)
    back_up = up_kernel.transpose(0, 1, 3, 2).reshape(16 * COUT, CIN)
    input_grad = jnp.einsum(
        "rck,kn->rcn", grad_patches, back_up, preferred_element_type=jnp.float32
    )
    up_flat = jnp.einsum("rcm,rck->mk", inputs, grad_patches, preferred_element_type=jnp.float32)
    up_span = CIN // lon_count
    mix_span = COUT // lon_count
    up_size = up_span * 16 * COUT
    terms = jnp.concatenate(
        [up_flat.reshape(lon_count, up_size), mix_flat_grad.reshape(lon_count, -1)], axis=1
    )
    summed = reduce_terms(terms) * grad_scale
    up_part = summed[:up_size].reshape(up_span, 4, 4, COUT).transpose(1, 2, 0, 3)
    mix_part = summed[up_size:].reshape(mix_span, 3, 3, COUT).transpose(1, 2, 0, 3)
    return (section_out, input_grad, up_part, mix_part)


def exchange(part, axis, step):
    size = lax.axis_size(axis)
    return lax.ppermute(part, axis, [(i, i ^ step) for i in range(size)])


def halve(buffer, axis, step, dim):
    own = lax.axis_index(axis) // step % 2
    keep = lax.dynamic_index_in_dim(buffer, own, dim, keepdims=False)
    send = lax.dynamic_index_in_dim(buffer, 1 - own, dim, keepdims=False)
    return keep + exchange(send, axis, step)


def double(part, axis, step):
    own = lax.axis_index(axis) // step % 2
    got = exchange(part, axis, step)
    low = jnp.where(own == 0, part, got)
    high = jnp.where(own == 0, got, part)
    return jnp.concatenate([low, high])


def steps_of(size):
    count = size.bit_length() - 1
    return [1 << k for k in range(count)] if size == 1 << count else None


def scatter_lon(rows, order):
    lon_count = rows.shape[0]
    steps = steps_of(lon_count)
    width = len(steps)
    grid = rows.reshape((2,) * width + rows.shape[1:])
    held = list(reversed(steps))
    for step in order:
        dim = held.index(step)
        grid = halve(grid, "lon", step, dim)
        held.pop(dim)
    return grid


def reduce_lat(flat):
    steps = steps_of(lax.axis_size("lat"))
    if steps is None or flat.shape[0] % (1 << len(steps)):
        return lax.psum(flat, "lat")
    for step in steps:
        flat = halve(flat.reshape(2, -1), "lat", step, 0)
    for step in reversed(steps):
        flat = double(flat, "lat", step)
    return flat


def reduce_terms(rows):
    lon_count = rows.shape[0]
    steps = steps_of(lon_count)
    if steps is None or rows.shape[1] % 2:
        own = lax.axis_index("lon")
        mine = lax.dynamic_index_in_dim(lax.psum(rows, "lon"), own, 0, keepdims=False)
        return reduce_lat(mine)
    half = rows.shape[1] // 2
    first = scatter_lon(rows[:, :half], steps)
    second = scatter_lon(rows[:, half:], list(reversed(steps)))
    return jnp.concatenate([reduce_lat(first), reduce_lat(second)])


def solution(mesh):
    placed = (P("lat", "lon", None), P("lat", "lon", None), P(), P(), P(), P("lat", "lon", None))
    return jax.shard_map(
        shards,
        mesh=mesh,
        in_specs=placed,
        out_specs=(
            P("lat", "lon", None),
            P("lat", "lon", None),
            P(None, None, "lon", None),
            P(None, None, "lon", None),
        ),
        check_vma=False,
    )
```

```python
import math

import jax
import jax.numpy as jnp
from jax import lax
from jax.sharding import PartitionSpec as P

CIN = 256
COUT = 128
BLOCK = 32


row_taps = (((1, 0), (3, -1)), ((0, 1), (2, 0)))


def swap_edges(fields, margins, axis, dim, wrap):
    size = lax.axis_size(axis)
    up = [(i, (i + 1) % size) for i in range(size if wrap else size - 1)]
    down = [(j, i) for i, j in up]
    lasts, leads = [], []
    for field, width in zip(fields, margins):
        length = field.shape[dim]
        lasts.append(lax.slice_in_dim(field, length - width, length, axis=dim))
        leads.append(lax.slice_in_dim(field, 0, width, axis=dim))
    before = lax.ppermute(jnp.concatenate([p.reshape(-1) for p in lasts]), axis, up)
    after = lax.ppermute(jnp.concatenate([p.reshape(-1) for p in leads]), axis, down)
    joined, at = [], 0
    for field, last, lead in zip(fields, lasts, leads):
        count = last.size
        head = before[at : at + count].reshape(last.shape)
        tail = after[at : at + count].reshape(lead.shape)
        joined.append(jnp.concatenate([head, field, tail], axis=dim))
        at += count
    return joined


def extend_all(fields, margins):
    widened = swap_edges(fields, margins, "lon", 1, True)
    return swap_edges(widened, margins, "lat", 0, False)


def decode(elem_codes, block_exps):
    sign_bit = elem_codes // 128
    exponent = elem_codes // 8 % 16
    mantissa = elem_codes % 8
    magnitude = jnp.exp2((exponent - 7).astype(jnp.float32)) * (
        1.0 + mantissa.astype(jnp.float32) / 8.0
    )
    signed = jnp.where(sign_bit == 1, -magnitude, magnitude)
    factor = jnp.repeat(jnp.exp2(block_exps.astype(jnp.float32)), BLOCK, axis=2)
    return (signed * factor).astype(jnp.bfloat16)


def slope(pre_act):
    plain = pre_act.astype(jnp.float32)
    sigmoid_v = jax.nn.sigmoid(plain)
    return sigmoid_v * (1.0 + plain * (1.0 - sigmoid_v))


def upsample(padded, up_kernel, row_count, col_count):
    halves = []
    for row_par in (1, 0):
        lane_list = []
        for col_par in (1, 0):
            pieces = []
            kernels = []
            for row_tap, row_off in row_taps[row_par]:
                for col_tap, col_off in row_taps[col_par]:
                    row_at = 1 + row_off - row_par
                    col_at = 1 + col_off - col_par
                    pieces.append(
                        padded[row_at : row_at + row_count + 1, col_at : col_at + col_count + 1]
                    )
                    kernels.append(up_kernel[row_tap, col_tap])
            stacked = jnp.concatenate(pieces, axis=2)
            kernel = jnp.concatenate(kernels, axis=0)
            lane_list.append(
                jnp.einsum("rck,kn->rcn", stacked, kernel, preferred_element_type=jnp.float32)
            )
        halves.append(jnp.stack(lane_list, axis=2))
    merged = jnp.stack(halves, axis=1)
    return merged.reshape(2 * row_count + 2, 2 * col_count + 2, merged.shape[-1])


def neighbours(padded, row_count, col_count, flipped):
    pieces = []
    for row_tap in range(3):
        for col_tap in range(3):
            row_at = 2 - row_tap if flipped else row_tap
            col_at = 2 - col_tap if flipped else col_tap
            pieces.append(padded[row_at : row_at + row_count, col_at : col_at + col_count])
    return jnp.concatenate(pieces, axis=2)


def strided(padded, row_count, col_count):
    pieces = []
    for row_tap in range(4):
        for col_tap in range(4):
            pieces.append(
                padded[row_tap : row_tap + 2 * row_count : 2, col_tap : col_tap + 2 * col_count : 2]
            )
    return jnp.concatenate(pieces, axis=2)


def shards(elem_codes, block_exps, up_kernel, up_bias, mix_kernel, cotangent):
    inputs = decode(elem_codes, block_exps)
    in_rows, in_cols = (inputs.shape[0], inputs.shape[1])
    out_rows, out_cols = (2 * in_rows, 2 * in_cols)
    lat_count = lax.axis_size("lat")
    lon_count = lax.axis_size("lon")
    back_mix = mix_kernel.transpose(0, 1, 3, 2).reshape(9 * COUT, COUT)
    padded_in, grad_pad = extend_all((inputs, cotangent), (1, 2))
    raw = upsample(padded_in, up_kernel, in_rows, in_cols)
    pre_act = (raw + up_bias).astype(jnp.bfloat16)
    row_at = lax.axis_index("lat") * out_rows - 1 + lax.broadcasted_iota(jnp.int32, (out_rows + 2, 1, 1), 0)
    inside = (row_at >= 0) & (row_at < out_rows * lat_count)
    activated = jax.nn.silu(pre_act.astype(jnp.float32)).astype(jnp.bfloat16)
    act_pad = jnp.where(inside, activated, jnp.zeros_like(activated))
    act_grad = jnp.einsum(
        "rck,kn->rcn",
        neighbours(grad_pad, out_rows + 2, out_cols + 2, True),
        back_mix,
        preferred_element_type=jnp.float32,
    )
    pre_grad = (act_grad * slope(pre_act)).astype(jnp.bfloat16)
    pre_grad_pad = jnp.where(inside, pre_grad, jnp.zeros_like(pre_grad))
    patches = neighbours(act_pad, out_rows, out_cols, False)
    mix_flat = mix_kernel.reshape(9 * COUT, COUT)
    section_out = jnp.einsum(
        "rck,kn->rcn", patches, mix_flat, preferred_element_type=jnp.float32
    ).astype(jnp.bfloat16)
    grad_scale = 1.0 / math.sqrt(out_rows * lat_count * out_cols * lon_count)
    mix_flat_grad = jnp.einsum(
        "rctm,rcn->mtn",
        patches.reshape(out_rows, out_cols, 9, COUT),
        cotangent,
        preferred_element_type=jnp.float32,
    )
    grad_patches = strided(pre_grad_pad, in_rows, in_cols)
    back_up = up_kernel.transpose(0, 1, 3, 2).reshape(16 * COUT, CIN)
    input_grad = jnp.einsum(
        "rck,kn->rcn", grad_patches, back_up, preferred_element_type=jnp.float32
    )
    up_flat = jnp.einsum("rcm,rck->mk", inputs, grad_patches, preferred_element_type=jnp.float32)
    up_span = CIN // lon_count
    mix_span = COUT // lon_count
    up_size = up_span * 16 * COUT
    terms = jnp.concatenate(
        [up_flat.reshape(lon_count, up_size), mix_flat_grad.reshape(lon_count, -1)], axis=1
    )
    summed = reduce_terms(terms) * grad_scale
    up_part = summed[:up_size].reshape(up_span, 4, 4, COUT).transpose(1, 2, 0, 3)
    mix_part = summed[up_size:].reshape(mix_span, 3, 3, COUT).transpose(1, 2, 0, 3)
    return (section_out, input_grad, up_part, mix_part)


def exchange(part, axis, step):
    size = lax.axis_size(axis)
    return lax.ppermute(part, axis, [(i, i ^ step) for i in range(size)])


def halve(buffer, axis, step, dim):
    own = lax.axis_index(axis) // step % 2
    keep = lax.dynamic_index_in_dim(buffer, own, dim, keepdims=False)
    send = lax.dynamic_index_in_dim(buffer, 1 - own, dim, keepdims=False)
    return keep + exchange(send, axis, step)


def double(part, axis, step):
    own = lax.axis_index(axis) // step % 2
    got = exchange(part, axis, step)
    low = jnp.where(own == 0, part, got)
    high = jnp.where(own == 0, got, part)
    return jnp.concatenate([low, high])


def steps_of(size):
    count = size.bit_length() - 1
    return [1 << k for k in range(count)] if size == 1 << count else None


def scatter_lon(rows, order):
    lon_count = rows.shape[0]
    steps = steps_of(lon_count)
    width = len(steps)
    grid = rows.reshape((2,) * width + rows.shape[1:])
    held = list(reversed(steps))
    for step in order:
        dim = held.index(step)
        grid = halve(grid, "lon", step, dim)
        held.pop(dim)
    return grid


def reduce_lat(flat):
    steps = steps_of(lax.axis_size("lat"))
    if steps is None or flat.shape[0] % (1 << len(steps)):
        return lax.psum(flat, "lat")
    for step in steps:
        flat = halve(flat.reshape(2, -1), "lat", step, 0)
    for step in reversed(steps):
        flat = double(flat, "lat", step)
    return flat


def reduce_terms(rows):
    lon_count = rows.shape[0]
    steps = steps_of(lon_count)
    if steps is None or rows.shape[1] % 2:
        own = lax.axis_index("lon")
        mine = lax.dynamic_index_in_dim(lax.psum(rows, "lon"), own, 0, keepdims=False)
        return reduce_lat(mine)
    half = rows.shape[1] // 2
    first = scatter_lon(rows[:, :half], steps)
    second = scatter_lon(rows[:, half:], list(reversed(steps)))
    return reduce_lat(jnp.concatenate([first, second]))


def solution(mesh):
    placed = (P("lat", "lon", None), P("lat", "lon", None), P(), P(), P(), P("lat", "lon", None))
    return jax.shard_map(
        shards,
        mesh=mesh,
        in_specs=placed,
        out_specs=(
            P("lat", "lon", None),
            P("lat", "lon", None),
            P(None, None, "lon", None),
            P(None, None, "lon", None),
        ),
        check_vma=False,
    )
```

```python
import math

import jax
import jax.numpy as jnp
from jax import lax
from jax.sharding import PartitionSpec as P

CIN = 256
COUT = 128
BLOCK = 32


row_taps = (((1, 0), (3, -1)), ((0, 1), (2, 0)))


def swap_edges(fields, margins, axis, dim, wrap):
    size = lax.axis_size(axis)
    up = [(i, (i + 1) % size) for i in range(size if wrap else size - 1)]
    down = [(j, i) for i, j in up]
    lasts, leads = [], []
    for field, width in zip(fields, margins):
        length = field.shape[dim]
        lasts.append(lax.slice_in_dim(field, length - width, length, axis=dim))
        leads.append(lax.slice_in_dim(field, 0, width, axis=dim))
    before = lax.ppermute(jnp.concatenate([p.reshape(-1) for p in lasts]), axis, up)
    after = lax.ppermute(jnp.concatenate([p.reshape(-1) for p in leads]), axis, down)
    joined, at = [], 0
    for field, last, lead in zip(fields, lasts, leads):
        count = last.size
        head = before[at : at + count].reshape(last.shape)
        tail = after[at : at + count].reshape(lead.shape)
        joined.append(jnp.concatenate([head, field, tail], axis=dim))
        at += count
    return joined


def extend_all(fields, margins):
    widened = swap_edges(fields, margins, "lon", 1, True)
    return swap_edges(widened, margins, "lat", 0, False)


def decode(elem_codes, block_exps):
    sign_bit = elem_codes // 128
    exponent = elem_codes // 8 % 16
    mantissa = elem_codes % 8
    magnitude = jnp.exp2((exponent - 7).astype(jnp.float32)) * (
        1.0 + mantissa.astype(jnp.float32) / 8.0
    )
    signed = jnp.where(sign_bit == 1, -magnitude, magnitude)
    factor = jnp.repeat(jnp.exp2(block_exps.astype(jnp.float32)), BLOCK, axis=2)
    return (signed * factor).astype(jnp.bfloat16)


def slope(pre_act):
    plain = pre_act.astype(jnp.float32)
    sigmoid_v = jax.nn.sigmoid(plain)
    return sigmoid_v * (1.0 + plain * (1.0 - sigmoid_v))


def upsample(padded, up_kernel, row_count, col_count):
    halves = []
    for row_par in (1, 0):
        lane_list = []
        for col_par in (1, 0):
            pieces = []
            kernels = []
            for row_tap, row_off in row_taps[row_par]:
                for col_tap, col_off in row_taps[col_par]:
                    row_at = 1 + row_off - row_par
                    col_at = 1 + col_off - col_par
                    pieces.append(
                        padded[row_at : row_at + row_count + 1, col_at : col_at + col_count + 1]
                    )
                    kernels.append(up_kernel[row_tap, col_tap])
            stacked = jnp.concatenate(pieces, axis=2)
            kernel = jnp.concatenate(kernels, axis=0)
            lane_list.append(
                jnp.einsum("rck,kn->rcn", stacked, kernel, preferred_element_type=jnp.float32)
            )
        halves.append(jnp.stack(lane_list, axis=2))
    merged = jnp.stack(halves, axis=1)
    return merged.reshape(2 * row_count + 2, 2 * col_count + 2, merged.shape[-1])


def neighbours(padded, row_count, col_count, flipped):
    pieces = []
    for row_tap in range(3):
        for col_tap in range(3):
            row_at = 2 - row_tap if flipped else row_tap
            col_at = 2 - col_tap if flipped else col_tap
            pieces.append(padded[row_at : row_at + row_count, col_at : col_at + col_count])
    return jnp.concatenate(pieces, axis=2)


def strided(padded, row_count, col_count):
    pieces = []
    for row_tap in range(4):
        for col_tap in range(4):
            pieces.append(
                padded[row_tap : row_tap + 2 * row_count : 2, col_tap : col_tap + 2 * col_count : 2]
            )
    return jnp.concatenate(pieces, axis=2)


def shards(elem_codes, block_exps, up_kernel, up_bias, mix_kernel, cotangent):
    inputs = decode(elem_codes, block_exps)
    in_rows, in_cols = (inputs.shape[0], inputs.shape[1])
    out_rows, out_cols = (2 * in_rows, 2 * in_cols)
    lat_count = lax.axis_size("lat")
    lon_count = lax.axis_size("lon")
    back_mix = mix_kernel.transpose(0, 1, 3, 2).reshape(9 * COUT, COUT)
    padded_in, grad_pad = extend_all((inputs, cotangent), (1, 2))
    raw = upsample(padded_in, up_kernel, in_rows, in_cols)
    pre_act = (raw + up_bias).astype(jnp.bfloat16)
    row_at = lax.axis_index("lat") * out_rows - 1 + lax.broadcasted_iota(jnp.int32, (out_rows + 2, 1, 1), 0)
    inside = (row_at >= 0) & (row_at < out_rows * lat_count)
    activated = jax.nn.silu(pre_act.astype(jnp.float32)).astype(jnp.bfloat16)
    act_pad = jnp.where(inside, activated, jnp.zeros_like(activated))
    act_grad = jnp.einsum(
        "rck,kn->rcn",
        neighbours(grad_pad, out_rows + 2, out_cols + 2, True),
        back_mix,
        preferred_element_type=jnp.float32,
    )
    pre_grad = (act_grad * slope(pre_act)).astype(jnp.bfloat16)
    pre_grad_pad = jnp.where(inside, pre_grad, jnp.zeros_like(pre_grad))
    patches = neighbours(act_pad, out_rows, out_cols, False)
    mix_flat = mix_kernel.reshape(9 * COUT, COUT)
    section_out = jnp.einsum(
        "rck,kn->rcn", patches, mix_flat, preferred_element_type=jnp.float32
    ).astype(jnp.bfloat16)
    grad_scale = 1.0 / math.sqrt(out_rows * lat_count * out_cols * lon_count)
    mix_flat_grad = jnp.einsum(
        "rctm,rcn->mtn",
        patches.reshape(out_rows, out_cols, 9, COUT),
        cotangent,
        preferred_element_type=jnp.float32,
    )
    grad_patches = strided(pre_grad_pad, in_rows, in_cols)
    back_up = up_kernel.transpose(0, 1, 3, 2).reshape(16 * COUT, CIN)
    input_grad = jnp.einsum(
        "rck,kn->rcn", grad_patches, back_up, preferred_element_type=jnp.float32
    )
    up_flat = jnp.einsum("rcm,rck->mk", inputs, grad_patches, preferred_element_type=jnp.float32)
    up_span = CIN // lon_count
    mix_span = COUT // lon_count
    up_size = up_span * 16 * COUT
    terms = jnp.concatenate(
        [up_flat.reshape(lon_count, up_size), mix_flat_grad.reshape(lon_count, -1)], axis=1
    )
    summed = reduce_terms(terms) * grad_scale
    up_part = summed[:up_size].reshape(up_span, 4, 4, COUT).transpose(1, 2, 0, 3)
    mix_part = summed[up_size:].reshape(mix_span, 3, 3, COUT).transpose(1, 2, 0, 3)
    return (section_out, input_grad, up_part, mix_part)


def exchange(part, axis, step):
    size = lax.axis_size(axis)
    return lax.ppermute(part, axis, [(i, i ^ step) for i in range(size)])


def halve(buffer, axis, step, dim):
    own = lax.axis_index(axis) // step % 2
    keep = lax.dynamic_index_in_dim(buffer, own, dim, keepdims=False)
    send = lax.dynamic_index_in_dim(buffer, 1 - own, dim, keepdims=False)
    return keep + exchange(send.astype(jnp.bfloat16), axis, step).astype(keep.dtype)


def double(part, axis, step):
    own = lax.axis_index(axis) // step % 2
    got = exchange(part, axis, step)
    low = jnp.where(own == 0, part, got)
    high = jnp.where(own == 0, got, part)
    return jnp.concatenate([low, high])


def steps_of(size):
    count = size.bit_length() - 1
    return [1 << k for k in range(count)] if size == 1 << count else None


def scatter_lon(rows, order):
    lon_count = rows.shape[0]
    steps = steps_of(lon_count)
    width = len(steps)
    grid = rows.reshape((2,) * width + rows.shape[1:])
    held = list(reversed(steps))
    for step in order:
        dim = held.index(step)
        grid = halve(grid, "lon", step, dim)
        held.pop(dim)
    return grid


def reduce_lat(flat):
    steps = steps_of(lax.axis_size("lat"))
    if steps is None or flat.shape[0] % (1 << len(steps)):
        return lax.psum(flat, "lat")
    for step in steps:
        flat = halve(flat.reshape(2, -1), "lat", step, 0)
    flat = flat.astype(jnp.bfloat16)
    for step in reversed(steps):
        flat = double(flat, "lat", step)
    return flat.astype(jnp.float32)


def reduce_terms(rows):
    lon_count = rows.shape[0]
    steps = steps_of(lon_count)
    if steps is None or rows.shape[1] % 2:
        own = lax.axis_index("lon")
        mine = lax.dynamic_index_in_dim(lax.psum(rows, "lon"), own, 0, keepdims=False)
        return reduce_lat(mine)
    half = rows.shape[1] // 2
    first = scatter_lon(rows[:, :half], steps)
    second = scatter_lon(rows[:, half:], list(reversed(steps)))
    return jnp.concatenate([reduce_lat(first), reduce_lat(second)])


def solution(mesh):
    placed = (P("lat", "lon", None), P("lat", "lon", None), P(), P(), P(), P("lat", "lon", None))
    return jax.shard_map(
        shards,
        mesh=mesh,
        in_specs=placed,
        out_specs=(
            P("lat", "lon", None),
            P("lat", "lon", None),
            P(None, None, "lon", None),
            P(None, None, "lon", None),
        ),
        check_vma=False,
    )
```

```python
import math

import jax
import jax.numpy as jnp
from jax import lax
from jax.sharding import PartitionSpec as P

CIN = 256
COUT = 128
BLOCK = 32


row_taps = (((1, 0), (3, -1)), ((0, 1), (2, 0)))


def swap_edges(fields, margins, axis, dim, wrap):
    size = lax.axis_size(axis)
    up = [(i, (i + 1) % size) for i in range(size if wrap else size - 1)]
    down = [(j, i) for i, j in up]
    lasts, leads = [], []
    for field, width in zip(fields, margins):
        length = field.shape[dim]
        lasts.append(lax.slice_in_dim(field, length - width, length, axis=dim))
        leads.append(lax.slice_in_dim(field, 0, width, axis=dim))
    before = lax.ppermute(jnp.concatenate([p.reshape(-1) for p in lasts]), axis, up)
    after = lax.ppermute(jnp.concatenate([p.reshape(-1) for p in leads]), axis, down)
    joined, at = [], 0
    for field, last, lead in zip(fields, lasts, leads):
        count = last.size
        head = before[at : at + count].reshape(last.shape)
        tail = after[at : at + count].reshape(lead.shape)
        joined.append(jnp.concatenate([head, field, tail], axis=dim))
        at += count
    return joined


def extend_all(fields, margins):
    widened = swap_edges(fields, margins, "lon", 1, True)
    return swap_edges(widened, margins, "lat", 0, False)


def decode(elem_codes, block_exps):
    sign_bit = elem_codes // 128
    exponent = elem_codes // 8 % 16
    mantissa = elem_codes % 8
    magnitude = jnp.exp2((exponent - 7).astype(jnp.float32)) * (
        1.0 + mantissa.astype(jnp.float32) / 8.0
    )
    signed = jnp.where(sign_bit == 1, -magnitude, magnitude)
    factor = jnp.repeat(jnp.exp2(block_exps.astype(jnp.float32)), BLOCK, axis=2)
    return (signed * factor).astype(jnp.bfloat16)


def slope(pre_act):
    plain = pre_act.astype(jnp.float32)
    sigmoid_v = jax.nn.sigmoid(plain)
    return sigmoid_v * (1.0 + plain * (1.0 - sigmoid_v))


def upsample(padded, up_kernel, row_count, col_count):
    halves = []
    for row_par in (1, 0):
        lane_list = []
        for col_par in (1, 0):
            pieces = []
            kernels = []
            for row_tap, row_off in row_taps[row_par]:
                for col_tap, col_off in row_taps[col_par]:
                    row_at = 1 + row_off - row_par
                    col_at = 1 + col_off - col_par
                    pieces.append(
                        padded[row_at : row_at + row_count + 1, col_at : col_at + col_count + 1]
                    )
                    kernels.append(up_kernel[row_tap, col_tap])
            stacked = jnp.concatenate(pieces, axis=2)
            kernel = jnp.concatenate(kernels, axis=0)
            lane_list.append(
                jnp.einsum("rck,kn->rcn", stacked, kernel, preferred_element_type=jnp.float32)
            )
        halves.append(jnp.stack(lane_list, axis=2))
    merged = jnp.stack(halves, axis=1)
    return merged.reshape(2 * row_count + 2, 2 * col_count + 2, merged.shape[-1])


def neighbours(padded, row_count, col_count, flipped):
    pieces = []
    for row_tap in range(3):
        for col_tap in range(3):
            row_at = 2 - row_tap if flipped else row_tap
            col_at = 2 - col_tap if flipped else col_tap
            pieces.append(padded[row_at : row_at + row_count, col_at : col_at + col_count])
    return jnp.concatenate(pieces, axis=2)


def strided(padded, row_count, col_count):
    pieces = []
    for row_tap in range(4):
        for col_tap in range(4):
            pieces.append(
                padded[row_tap : row_tap + 2 * row_count : 2, col_tap : col_tap + 2 * col_count : 2]
            )
    return jnp.concatenate(pieces, axis=2)


def shards(elem_codes, block_exps, up_kernel, up_bias, mix_kernel, cotangent):
    inputs = decode(elem_codes, block_exps)
    in_rows, in_cols = (inputs.shape[0], inputs.shape[1])
    out_rows, out_cols = (2 * in_rows, 2 * in_cols)
    lat_count = lax.axis_size("lat")
    lon_count = lax.axis_size("lon")
    back_mix = mix_kernel.transpose(0, 1, 3, 2).reshape(9 * COUT, COUT)
    padded_in, grad_pad = extend_all((inputs, cotangent), (1, 2))
    raw = upsample(padded_in, up_kernel, in_rows, in_cols)
    pre_act = (raw + up_bias).astype(jnp.bfloat16)
    row_at = lax.axis_index("lat") * out_rows - 1 + lax.broadcasted_iota(jnp.int32, (out_rows + 2, 1, 1), 0)
    inside = (row_at >= 0) & (row_at < out_rows * lat_count)
    activated = jax.nn.silu(pre_act.astype(jnp.float32)).astype(jnp.bfloat16)
    act_pad = jnp.where(inside, activated, jnp.zeros_like(activated))
    act_grad = jnp.einsum(
        "rck,kn->rcn",
        neighbours(grad_pad, out_rows + 2, out_cols + 2, True),
        back_mix,
        preferred_element_type=jnp.float32,
    )
    pre_grad = (act_grad * slope(pre_act)).astype(jnp.bfloat16)
    pre_grad_pad = jnp.where(inside, pre_grad, jnp.zeros_like(pre_grad))
    patches = neighbours(act_pad, out_rows, out_cols, False)
    mix_flat = mix_kernel.reshape(9 * COUT, COUT)
    section_out = jnp.einsum(
        "rck,kn->rcn", patches, mix_flat, preferred_element_type=jnp.float32
    ).astype(jnp.bfloat16)
    grad_scale = 1.0 / math.sqrt(out_rows * lat_count * out_cols * lon_count)
    mix_flat_grad = jnp.einsum(
        "rctm,rcn->mtn",
        patches.reshape(out_rows, out_cols, 9, COUT),
        cotangent,
        preferred_element_type=jnp.float32,
    )
    grad_patches = strided(pre_grad_pad, in_rows, in_cols)
    back_up = up_kernel.transpose(0, 1, 3, 2).reshape(16 * COUT, CIN)
    input_grad = jnp.einsum(
        "rck,kn->rcn", grad_patches, back_up, preferred_element_type=jnp.float32
    )
    up_flat = jnp.einsum("rcm,rck->mk", inputs, grad_patches, preferred_element_type=jnp.float32)
    up_span = CIN // lon_count
    mix_span = COUT // lon_count
    up_size = up_span * 16 * COUT
    terms = jnp.concatenate(
        [up_flat.reshape(lon_count, up_size), mix_flat_grad.reshape(lon_count, -1)], axis=1
    )
    summed = reduce_terms(terms) * grad_scale
    up_part = summed[:up_size].reshape(up_span, 4, 4, COUT).transpose(1, 2, 0, 3)
    mix_part = summed[up_size:].reshape(mix_span, 3, 3, COUT).transpose(1, 2, 0, 3)
    return (section_out, input_grad, up_part, mix_part)


def exchange(part, axis, step):
    size = lax.axis_size(axis)
    return lax.ppermute(part, axis, [(i, i ^ step) for i in range(size)])


def halve(buffer, axis, step, dim):
    own = lax.axis_index(axis) // step % 2
    keep = lax.dynamic_index_in_dim(buffer, own, dim, keepdims=False)
    send = lax.dynamic_index_in_dim(buffer, 1 - own, dim, keepdims=False)
    return keep + exchange(send.astype(jnp.bfloat16), axis, step).astype(keep.dtype)


def double(part, axis, step):
    own = lax.axis_index(axis) // step % 2
    got = exchange(part, axis, step)
    low = jnp.where(own == 0, part, got)
    high = jnp.where(own == 0, got, part)
    return jnp.concatenate([low, high])


def steps_of(size):
    count = size.bit_length() - 1
    return [1 << k for k in range(count)] if size == 1 << count else None


def scatter_lon(rows, order):
    lon_count = rows.shape[0]
    steps = steps_of(lon_count)
    width = len(steps)
    grid = rows.reshape((2,) * width + rows.shape[1:])
    held = list(reversed(steps))
    for step in order:
        dim = held.index(step)
        grid = halve(grid, "lon", step, dim)
        held.pop(dim)
    return grid


def reduce_lat(flat):
    steps = steps_of(lax.axis_size("lat"))
    if steps is None or flat.shape[0] % 2:
        return lax.psum(flat, "lat")
    part = halve(flat.reshape(2, -1), "lat", steps[0], 0).astype(jnp.bfloat16)
    for step in steps[1:]:
        got = exchange(part, "lat", step)
        part = (part.astype(jnp.float32) + got.astype(jnp.float32)).astype(jnp.bfloat16)
    return double(part, "lat", steps[0]).astype(jnp.float32)


def reduce_terms(rows):
    lon_count = rows.shape[0]
    steps = steps_of(lon_count)
    if steps is None or rows.shape[1] % 2:
        own = lax.axis_index("lon")
        mine = lax.dynamic_index_in_dim(lax.psum(rows, "lon"), own, 0, keepdims=False)
        return reduce_lat(mine)
    half = rows.shape[1] // 2
    first = scatter_lon(rows[:, :half], steps)
    second = scatter_lon(rows[:, half:], list(reversed(steps)))
    return jnp.concatenate([reduce_lat(first), reduce_lat(second)])


def solution(mesh):
    placed = (P("lat", "lon", None), P("lat", "lon", None), P(), P(), P(), P("lat", "lon", None))
    return jax.shard_map(
        shards,
        mesh=mesh,
        in_specs=placed,
        out_specs=(
            P("lat", "lon", None),
            P("lat", "lon", None),
            P(None, None, "lon", None),
            P(None, None, "lon", None),
        ),
        check_vma=False,
    )
```

```python
import math

import jax
import jax.numpy as jnp
from jax import lax
from jax.sharding import PartitionSpec as P

CIN = 256
COUT = 128
BLOCK = 32


row_taps = (((1, 0), (3, -1)), ((0, 1), (2, 0)))


def swap_edges(fields, margins, axis, dim, wrap):
    size = lax.axis_size(axis)
    up = [(i, (i + 1) % size) for i in range(size if wrap else size - 1)]
    down = [(j, i) for i, j in up]
    lasts, leads = [], []
    for field, width in zip(fields, margins):
        length = field.shape[dim]
        lasts.append(lax.slice_in_dim(field, length - width, length, axis=dim))
        leads.append(lax.slice_in_dim(field, 0, width, axis=dim))
    before = lax.ppermute(jnp.concatenate([p.reshape(-1) for p in lasts]), axis, up)
    after = lax.ppermute(jnp.concatenate([p.reshape(-1) for p in leads]), axis, down)
    joined, at = [], 0
    for field, last, lead in zip(fields, lasts, leads):
        count = last.size
        head = before[at : at + count].reshape(last.shape)
        tail = after[at : at + count].reshape(lead.shape)
        joined.append(jnp.concatenate([head, field, tail], axis=dim))
        at += count
    return joined


def extend_all(fields, margins):
    widened = swap_edges(fields, margins, "lon", 1, True)
    return swap_edges(widened, margins, "lat", 0, False)


def decode(elem_codes, block_exps):
    sign_bit = elem_codes // 128
    exponent = elem_codes // 8 % 16
    mantissa = elem_codes % 8
    magnitude = jnp.exp2((exponent - 7).astype(jnp.float32)) * (
        1.0 + mantissa.astype(jnp.float32) / 8.0
    )
    signed = jnp.where(sign_bit == 1, -magnitude, magnitude)
    factor = jnp.repeat(jnp.exp2(block_exps.astype(jnp.float32)), BLOCK, axis=2)
    return (signed * factor).astype(jnp.bfloat16)


def slope(pre_act):
    plain = pre_act.astype(jnp.float32)
    sigmoid_v = jax.nn.sigmoid(plain)
    return sigmoid_v * (1.0 + plain * (1.0 - sigmoid_v))


def upsample(padded, up_kernel, row_count, col_count):
    halves = []
    for row_par in (1, 0):
        lane_list = []
        for col_par in (1, 0):
            pieces = []
            kernels = []
            for row_tap, row_off in row_taps[row_par]:
                for col_tap, col_off in row_taps[col_par]:
                    row_at = 1 + row_off - row_par
                    col_at = 1 + col_off - col_par
                    pieces.append(
                        padded[row_at : row_at + row_count + 1, col_at : col_at + col_count + 1]
                    )
                    kernels.append(up_kernel[row_tap, col_tap])
            stacked = jnp.concatenate(pieces, axis=2)
            kernel = jnp.concatenate(kernels, axis=0)
            lane_list.append(
                jnp.einsum("rck,kn->rcn", stacked, kernel, preferred_element_type=jnp.float32)
            )
        halves.append(jnp.stack(lane_list, axis=2))
    merged = jnp.stack(halves, axis=1)
    return merged.reshape(2 * row_count + 2, 2 * col_count + 2, merged.shape[-1])


def neighbours(padded, row_count, col_count, flipped):
    pieces = []
    for row_tap in range(3):
        for col_tap in range(3):
            row_at = 2 - row_tap if flipped else row_tap
            col_at = 2 - col_tap if flipped else col_tap
            pieces.append(padded[row_at : row_at + row_count, col_at : col_at + col_count])
    return jnp.concatenate(pieces, axis=2)


def strided(padded, row_count, col_count):
    pieces = []
    for row_tap in range(4):
        for col_tap in range(4):
            pieces.append(
                padded[row_tap : row_tap + 2 * row_count : 2, col_tap : col_tap + 2 * col_count : 2]
            )
    return jnp.concatenate(pieces, axis=2)


def shards(elem_codes, block_exps, up_kernel, up_bias, mix_kernel, cotangent):
    inputs = decode(elem_codes, block_exps)
    in_rows, in_cols = (inputs.shape[0], inputs.shape[1])
    out_rows, out_cols = (2 * in_rows, 2 * in_cols)
    lat_count = lax.axis_size("lat")
    lon_count = lax.axis_size("lon")
    back_mix = mix_kernel.transpose(0, 1, 3, 2).reshape(9 * COUT, COUT)
    padded_in, grad_pad = extend_all((inputs, cotangent), (1, 2))
    raw = upsample(padded_in, up_kernel, in_rows, in_cols)
    pre_act = (raw + up_bias).astype(jnp.bfloat16)
    row_at = lax.axis_index("lat") * out_rows - 1 + lax.broadcasted_iota(jnp.int32, (out_rows + 2, 1, 1), 0)
    inside = (row_at >= 0) & (row_at < out_rows * lat_count)
    activated = jax.nn.silu(pre_act.astype(jnp.float32)).astype(jnp.bfloat16)
    act_pad = jnp.where(inside, activated, jnp.zeros_like(activated))
    act_grad = jnp.einsum(
        "rck,kn->rcn",
        neighbours(grad_pad, out_rows + 2, out_cols + 2, True),
        back_mix,
        preferred_element_type=jnp.float32,
    )
    pre_grad = (act_grad * slope(pre_act)).astype(jnp.bfloat16)
    pre_grad_pad = jnp.where(inside, pre_grad, jnp.zeros_like(pre_grad))
    patches = neighbours(act_pad, out_rows, out_cols, False)
    mix_flat = mix_kernel.reshape(9 * COUT, COUT)
    section_out = jnp.einsum(
        "rck,kn->rcn", patches, mix_flat, preferred_element_type=jnp.float32
    ).astype(jnp.bfloat16)
    grad_scale = 1.0 / math.sqrt(out_rows * lat_count * out_cols * lon_count)
    mix_taps = jnp.einsum(
        "rctm,rcn->tmn",
        patches.reshape(out_rows, out_cols, 9, COUT),
        cotangent,
        preferred_element_type=jnp.float32,
    )
    grad_patches = strided(pre_grad_pad, in_rows, in_cols)
    back_up = up_kernel.transpose(0, 1, 3, 2).reshape(16 * COUT, CIN)
    input_grad = jnp.einsum(
        "rck,kn->rcn", grad_patches, back_up, preferred_element_type=jnp.float32
    )
    up_taps = jnp.einsum(
        "rctn,rcm->tmn",
        grad_patches.reshape(in_rows, in_cols, 16, COUT),
        inputs,
        preferred_element_type=jnp.float32,
    )
    up_span = CIN // lon_count
    mix_span = COUT // lon_count
    up_rows = 16 * up_span
    by_owner = [
        up_taps.reshape(16, lon_count, up_span, COUT).transpose(1, 0, 2, 3),
        mix_taps.reshape(9, lon_count, mix_span, COUT).transpose(1, 0, 2, 3),
    ]
    terms = jnp.concatenate([t.reshape(lon_count, -1, COUT) for t in by_owner], axis=1)
    summed = reduce_terms(terms) * grad_scale
    up_part = summed[:up_rows].reshape(4, 4, up_span, COUT)
    mix_part = summed[up_rows:].reshape(3, 3, mix_span, COUT)
    return (section_out, input_grad, up_part, mix_part)


def exchange(part, axis, step):
    size = lax.axis_size(axis)
    return lax.ppermute(part, axis, [(i, i ^ step) for i in range(size)])


def halve(buffer, axis, step, dim):
    own = lax.axis_index(axis) // step % 2
    keep = lax.dynamic_index_in_dim(buffer, own, dim, keepdims=False)
    send = lax.dynamic_index_in_dim(buffer, 1 - own, dim, keepdims=False)
    return keep + exchange(send.astype(jnp.bfloat16), axis, step).astype(keep.dtype)


def double(part, axis, step):
    own = lax.axis_index(axis) // step % 2
    got = exchange(part, axis, step)
    low = jnp.where(own == 0, part, got)
    high = jnp.where(own == 0, got, part)
    return jnp.concatenate([low, high])


def steps_of(size):
    count = size.bit_length() - 1
    return [1 << k for k in range(count)] if size == 1 << count else None


def scatter_lon(rows, order):
    lon_count = rows.shape[0]
    steps = steps_of(lon_count)
    width = len(steps)
    grid = rows.reshape((2,) * width + rows.shape[1:])
    held = list(reversed(steps))
    for step in order:
        dim = held.index(step)
        grid = halve(grid, "lon", step, dim)
        held.pop(dim)
    return grid


def reduce_lat(flat):
    steps = steps_of(lax.axis_size("lat"))
    if steps is None or flat.shape[0] % 2:
        return lax.psum(flat, "lat")
    pair = flat.reshape((2, flat.shape[0] // 2) + flat.shape[1:])
    part = halve(pair, "lat", steps[0], 0).astype(jnp.bfloat16)
    for step in steps[1:]:
        got = exchange(part, "lat", step)
        part = (part.astype(jnp.float32) + got.astype(jnp.float32)).astype(jnp.bfloat16)
    return double(part, "lat", steps[0]).astype(jnp.float32)


def reduce_terms(rows):
    lon_count = rows.shape[0]
    steps = steps_of(lon_count)
    if steps is None or rows.shape[1] % 2:
        own = lax.axis_index("lon")
        mine = lax.dynamic_index_in_dim(lax.psum(rows, "lon"), own, 0, keepdims=False)
        return reduce_lat(mine)
    half = rows.shape[1] // 2
    first = scatter_lon(rows[:, :half], steps)
    second = scatter_lon(rows[:, half:], list(reversed(steps)))
    return jnp.concatenate([reduce_lat(first), reduce_lat(second)])


def solution(mesh):
    placed = (P("lat", "lon", None), P("lat", "lon", None), P(), P(), P(), P("lat", "lon", None))
    return jax.shard_map(
        shards,
        mesh=mesh,
        in_specs=placed,
        out_specs=(
            P("lat", "lon", None),
            P("lat", "lon", None),
            P(None, None, "lon", None),
            P(None, None, "lon", None),
        ),
        check_vma=False,
    )
```

```python
import math

import jax
import jax.numpy as jnp
from jax import lax
from jax.sharding import PartitionSpec as P

CIN = 256
COUT = 128
BLOCK = 32


row_taps = (((1, 0), (3, -1)), ((0, 1), (2, 0)))


def swap_edges(fields, margins, axis, dim, wrap):
    size = lax.axis_size(axis)
    up = [(i, (i + 1) % size) for i in range(size if wrap else size - 1)]
    down = [(j, i) for i, j in up]
    lasts, leads = [], []
    for field, width in zip(fields, margins):
        length = field.shape[dim]
        lasts.append(lax.slice_in_dim(field, length - width, length, axis=dim))
        leads.append(lax.slice_in_dim(field, 0, width, axis=dim))
    before = lax.ppermute(jnp.concatenate([p.reshape(-1) for p in lasts]), axis, up)
    after = lax.ppermute(jnp.concatenate([p.reshape(-1) for p in leads]), axis, down)
    joined, at = [], 0
    for field, last, lead in zip(fields, lasts, leads):
        count = last.size
        head = before[at : at + count].reshape(last.shape)
        tail = after[at : at + count].reshape(lead.shape)
        joined.append(jnp.concatenate([head, field, tail], axis=dim))
        at += count
    return joined


def extend_all(fields, margins):
    widened = swap_edges(fields, margins, "lon", 1, True)
    return swap_edges(widened, margins, "lat", 0, False)


def decode(elem_codes, block_exps):
    sign_bit = elem_codes // 128
    exponent = elem_codes // 8 % 16
    mantissa = elem_codes % 8
    magnitude = jnp.exp2((exponent - 7).astype(jnp.float32)) * (
        1.0 + mantissa.astype(jnp.float32) / 8.0
    )
    signed = jnp.where(sign_bit == 1, -magnitude, magnitude)
    factor = jnp.repeat(jnp.exp2(block_exps.astype(jnp.float32)), BLOCK, axis=2)
    return (signed * factor).astype(jnp.bfloat16)


def slope(pre_act):
    plain = pre_act.astype(jnp.float32)
    sigmoid_v = jax.nn.sigmoid(plain)
    return sigmoid_v * (1.0 + plain * (1.0 - sigmoid_v))


def upsample(padded, up_kernel, row_count, col_count):
    halves = []
    for row_par in (1, 0):
        lane_list = []
        for col_par in (1, 0):
            pieces = []
            kernels = []
            for row_tap, row_off in row_taps[row_par]:
                for col_tap, col_off in row_taps[col_par]:
                    row_at = 1 + row_off - row_par
                    col_at = 1 + col_off - col_par
                    pieces.append(
                        padded[row_at : row_at + row_count + 1, col_at : col_at + col_count + 1]
                    )
                    kernels.append(up_kernel[row_tap, col_tap])
            stacked = jnp.concatenate(pieces, axis=2)
            kernel = jnp.concatenate(kernels, axis=0)
            lane_list.append(
                jnp.einsum("rck,kn->rcn", stacked, kernel, preferred_element_type=jnp.float32)
            )
        halves.append(jnp.stack(lane_list, axis=2))
    merged = jnp.stack(halves, axis=1)
    return merged.reshape(2 * row_count + 2, 2 * col_count + 2, merged.shape[-1])


def neighbours(padded, row_count, col_count, flipped):
    pieces = []
    for row_tap in range(3):
        for col_tap in range(3):
            row_at = 2 - row_tap if flipped else row_tap
            col_at = 2 - col_tap if flipped else col_tap
            pieces.append(padded[row_at : row_at + row_count, col_at : col_at + col_count])
    return jnp.concatenate(pieces, axis=2)


def strided(padded, row_count, col_count):
    pieces = []
    for row_tap in range(4):
        for col_tap in range(4):
            pieces.append(
                padded[row_tap : row_tap + 2 * row_count : 2, col_tap : col_tap + 2 * col_count : 2]
            )
    return jnp.concatenate(pieces, axis=2)


def shards(elem_codes, block_exps, up_kernel, up_bias, mix_kernel, cotangent):
    inputs = decode(elem_codes, block_exps)
    in_rows, in_cols = (inputs.shape[0], inputs.shape[1])
    out_rows, out_cols = (2 * in_rows, 2 * in_cols)
    lat_count = lax.axis_size("lat")
    lon_count = lax.axis_size("lon")
    back_mix = mix_kernel.transpose(0, 1, 3, 2).reshape(9 * COUT, COUT)
    padded_in, grad_pad = extend_all((inputs, cotangent), (1, 2))
    raw = upsample(padded_in, up_kernel, in_rows, in_cols)
    pre_act = (raw + up_bias).astype(jnp.bfloat16)
    row_at = lax.axis_index("lat") * out_rows - 1 + lax.broadcasted_iota(jnp.int32, (out_rows + 2, 1, 1), 0)
    inside = (row_at >= 0) & (row_at < out_rows * lat_count)
    activated = jax.nn.silu(pre_act.astype(jnp.float32)).astype(jnp.bfloat16)
    act_pad = jnp.where(inside, activated, jnp.zeros_like(activated))
    act_grad = jnp.einsum(
        "rck,kn->rcn",
        neighbours(grad_pad, out_rows + 2, out_cols + 2, True),
        back_mix,
        preferred_element_type=jnp.float32,
    )
    pre_grad = (act_grad * slope(pre_act)).astype(jnp.bfloat16)
    pre_grad_pad = jnp.where(inside, pre_grad, jnp.zeros_like(pre_grad))
    patches = neighbours(act_pad, out_rows, out_cols, False)
    mix_flat = mix_kernel.reshape(9 * COUT, COUT)
    section_out = jnp.einsum(
        "rck,kn->rcn", patches, mix_flat, preferred_element_type=jnp.float32
    ).astype(jnp.bfloat16)
    grad_scale = 1.0 / math.sqrt(out_rows * lat_count * out_cols * lon_count)
    mix_span = COUT // lon_count
    mix_owned = jnp.einsum(
        "rctm,rcn->mtn",
        patches.reshape(out_rows, out_cols, 9, COUT),
        cotangent,
        preferred_element_type=jnp.float32,
    ).reshape(lon_count, mix_span, 9, COUT).transpose(0, 2, 1, 3)
    grad_patches = strided(pre_grad_pad, in_rows, in_cols)
    back_up = up_kernel.transpose(0, 1, 3, 2).reshape(16 * COUT, CIN)
    input_grad = jnp.einsum(
        "rck,kn->rcn", grad_patches, back_up, preferred_element_type=jnp.float32
    )
    up_taps = jnp.einsum(
        "rctn,rcm->tmn",
        grad_patches.reshape(in_rows, in_cols, 16, COUT),
        inputs,
        preferred_element_type=jnp.float32,
    )
    up_span = CIN // lon_count
    up_rows = 16 * up_span
    by_owner = [
        up_taps.reshape(16, lon_count, up_span, COUT).transpose(1, 0, 2, 3),
        mix_owned,
    ]
    terms = jnp.concatenate([t.reshape(lon_count, -1, COUT) for t in by_owner], axis=1)
    summed = reduce_terms(terms) * grad_scale
    up_part = summed[:up_rows].reshape(4, 4, up_span, COUT)
    mix_part = summed[up_rows:].reshape(3, 3, mix_span, COUT)
    return (section_out, input_grad, up_part, mix_part)


def exchange(part, axis, step):
    size = lax.axis_size(axis)
    return lax.ppermute(part, axis, [(i, i ^ step) for i in range(size)])


def halve(buffer, axis, step, dim):
    own = lax.axis_index(axis) // step % 2
    keep = lax.dynamic_index_in_dim(buffer, own, dim, keepdims=False)
    send = lax.dynamic_index_in_dim(buffer, 1 - own, dim, keepdims=False)
    return keep + exchange(send.astype(jnp.bfloat16), axis, step).astype(keep.dtype)


def double(part, axis, step):
    own = lax.axis_index(axis) // step % 2
    got = exchange(part, axis, step)
    low = jnp.where(own == 0, part, got)
    high = jnp.where(own == 0, got, part)
    return jnp.concatenate([low, high])


def steps_of(size):
    count = size.bit_length() - 1
    return [1 << k for k in range(count)] if size == 1 << count else None


def scatter_lon(rows, order):
    lon_count = rows.shape[0]
    steps = steps_of(lon_count)
    width = len(steps)
    grid = rows.reshape((2,) * width + rows.shape[1:])
    held = list(reversed(steps))
    for step in order:
        dim = held.index(step)
        grid = halve(grid, "lon", step, dim)
        held.pop(dim)
    return grid


def reduce_lat(flat):
    steps = steps_of(lax.axis_size("lat"))
    if steps is None or flat.shape[0] % 2:
        return lax.psum(flat, "lat")
    pair = flat.reshape((2, flat.shape[0] // 2) + flat.shape[1:])
    part = halve(pair, "lat", steps[0], 0).astype(jnp.bfloat16)
    for step in steps[1:]:
        got = exchange(part, "lat", step)
        part = (part.astype(jnp.float32) + got.astype(jnp.float32)).astype(jnp.bfloat16)
    return double(part, "lat", steps[0]).astype(jnp.float32)


def reduce_terms(rows):
    lon_count = rows.shape[0]
    steps = steps_of(lon_count)
    if steps is None or rows.shape[1] % 2:
        own = lax.axis_index("lon")
        mine = lax.dynamic_index_in_dim(lax.psum(rows, "lon"), own, 0, keepdims=False)
        return reduce_lat(mine)
    half = rows.shape[1] // 2
    first = scatter_lon(rows[:, :half], steps)
    second = scatter_lon(rows[:, half:], list(reversed(steps)))
    return jnp.concatenate([reduce_lat(first), reduce_lat(second)])


def solution(mesh):
    placed = (P("lat", "lon", None), P("lat", "lon", None), P(), P(), P(), P("lat", "lon", None))
    return jax.shard_map(
        shards,
        mesh=mesh,
        in_specs=placed,
        out_specs=(
            P("lat", "lon", None),
            P("lat", "lon", None),
            P(None, None, "lon", None),
            P(None, None, "lon", None),
        ),
        check_vma=False,
    )
```

```python
import math

import jax
import jax.numpy as jnp
from jax import lax
from jax.sharding import PartitionSpec as P

CIN = 256
COUT = 128
BLOCK = 32


row_taps = (((1, 0), (3, -1)), ((0, 1), (2, 0)))


def swap_edges(fields, margins, axis, dim, wrap):
    size = lax.axis_size(axis)
    up = [(i, (i + 1) % size) for i in range(size if wrap else size - 1)]
    down = [(j, i) for i, j in up]
    lasts, leads = [], []
    for field, width in zip(fields, margins):
        length = field.shape[dim]
        lasts.append(lax.slice_in_dim(field, length - width, length, axis=dim))
        leads.append(lax.slice_in_dim(field, 0, width, axis=dim))
    before = lax.ppermute(jnp.concatenate([p.reshape(-1) for p in lasts]), axis, up)
    after = lax.ppermute(jnp.concatenate([p.reshape(-1) for p in leads]), axis, down)
    joined, at = [], 0
    for field, last, lead in zip(fields, lasts, leads):
        count = last.size
        head = before[at : at + count].reshape(last.shape)
        tail = after[at : at + count].reshape(lead.shape)
        joined.append(jnp.concatenate([head, field, tail], axis=dim))
        at += count
    return joined


def extend_all(fields, margins):
    widened = swap_edges(fields, margins, "lon", 1, True)
    return swap_edges(widened, margins, "lat", 0, False)


def decode(elem_codes, block_exps):
    sign_bit = elem_codes // 128
    exponent = elem_codes // 8 % 16
    mantissa = elem_codes % 8
    magnitude = jnp.exp2((exponent - 7).astype(jnp.float32)) * (
        1.0 + mantissa.astype(jnp.float32) / 8.0
    )
    signed = jnp.where(sign_bit == 1, -magnitude, magnitude)
    factor = jnp.repeat(jnp.exp2(block_exps.astype(jnp.float32)), BLOCK, axis=2)
    return (signed * factor).astype(jnp.bfloat16)


def slope(pre_act):
    plain = pre_act.astype(jnp.float32)
    sigmoid_v = jax.nn.sigmoid(plain)
    return sigmoid_v * (1.0 + plain * (1.0 - sigmoid_v))


def upsample(padded, up_kernel, row_count, col_count):
    halves = []
    for row_par in (1, 0):
        lane_list = []
        for col_par in (1, 0):
            pieces = []
            kernels = []
            for row_tap, row_off in row_taps[row_par]:
                for col_tap, col_off in row_taps[col_par]:
                    row_at = 1 + row_off - row_par
                    col_at = 1 + col_off - col_par
                    pieces.append(
                        padded[row_at : row_at + row_count + 1, col_at : col_at + col_count + 1]
                    )
                    kernels.append(up_kernel[row_tap, col_tap])
            stacked = jnp.concatenate(pieces, axis=2)
            kernel = jnp.concatenate(kernels, axis=0)
            lane_list.append(
                jnp.einsum("rck,kn->rcn", stacked, kernel, preferred_element_type=jnp.float32)
            )
        halves.append(jnp.stack(lane_list, axis=2))
    merged = jnp.stack(halves, axis=1)
    return merged.reshape(2 * row_count + 2, 2 * col_count + 2, merged.shape[-1])


def neighbours(padded, row_count, col_count, flipped):
    pieces = []
    for row_tap in range(3):
        for col_tap in range(3):
            row_at = 2 - row_tap if flipped else row_tap
            col_at = 2 - col_tap if flipped else col_tap
            pieces.append(padded[row_at : row_at + row_count, col_at : col_at + col_count])
    return jnp.concatenate(pieces, axis=2)


def strided(padded, row_count, col_count):
    split = padded.reshape(row_count + 1, 2, col_count + 1, 2, padded.shape[-1])
    pieces = []
    for row_tap in range(4):
        for col_tap in range(4):
            row_at, col_at = (row_tap // 2, col_tap // 2)
            pieces.append(
                split[
                    row_at : row_at + row_count,
                    row_tap % 2,
                    col_at : col_at + col_count,
                    col_tap % 2,
                ]
            )
    return jnp.concatenate(pieces, axis=2)


def shards(elem_codes, block_exps, up_kernel, up_bias, mix_kernel, cotangent):
    inputs = decode(elem_codes, block_exps)
    in_rows, in_cols = (inputs.shape[0], inputs.shape[1])
    out_rows, out_cols = (2 * in_rows, 2 * in_cols)
    lat_count = lax.axis_size("lat")
    lon_count = lax.axis_size("lon")
    back_mix = mix_kernel.transpose(0, 1, 3, 2).reshape(9 * COUT, COUT)
    padded_in, grad_pad = extend_all((inputs, cotangent), (1, 2))
    raw = upsample(padded_in, up_kernel, in_rows, in_cols)
    pre_act = (raw + up_bias).astype(jnp.bfloat16)
    row_at = lax.axis_index("lat") * out_rows - 1 + lax.broadcasted_iota(jnp.int32, (out_rows + 2, 1, 1), 0)
    inside = (row_at >= 0) & (row_at < out_rows * lat_count)
    activated = jax.nn.silu(pre_act.astype(jnp.float32)).astype(jnp.bfloat16)
    act_pad = jnp.where(inside, activated, jnp.zeros_like(activated))
    act_grad = jnp.einsum(
        "rck,kn->rcn",
        neighbours(grad_pad, out_rows + 2, out_cols + 2, True),
        back_mix,
        preferred_element_type=jnp.float32,
    )
    pre_grad = (act_grad * slope(pre_act)).astype(jnp.bfloat16)
    pre_grad_pad = jnp.where(inside, pre_grad, jnp.zeros_like(pre_grad))
    patches = neighbours(act_pad, out_rows, out_cols, False)
    mix_flat = mix_kernel.reshape(9 * COUT, COUT)
    section_out = jnp.einsum(
        "rck,kn->rcn", patches, mix_flat, preferred_element_type=jnp.float32
    ).astype(jnp.bfloat16)
    grad_scale = 1.0 / math.sqrt(out_rows * lat_count * out_cols * lon_count)
    mix_span = COUT // lon_count
    mix_owned = jnp.einsum(
        "rctm,rcn->mtn",
        patches.reshape(out_rows, out_cols, 9, COUT),
        cotangent,
        preferred_element_type=jnp.float32,
    ).reshape(lon_count, mix_span, 9, COUT).transpose(0, 2, 1, 3)
    grad_patches = strided(pre_grad_pad, in_rows, in_cols)
    back_up = up_kernel.transpose(0, 1, 3, 2).reshape(16 * COUT, CIN)
    input_grad = jnp.einsum(
        "rck,kn->rcn", grad_patches, back_up, preferred_element_type=jnp.float32
    )
    up_taps = jnp.einsum(
        "rctn,rcm->tmn",
        grad_patches.reshape(in_rows, in_cols, 16, COUT),
        inputs,
        preferred_element_type=jnp.float32,
    )
    up_span = CIN // lon_count
    up_rows = 16 * up_span
    by_owner = [
        up_taps.reshape(16, lon_count, up_span, COUT).transpose(1, 0, 2, 3),
        mix_owned,
    ]
    terms = jnp.concatenate([t.reshape(lon_count, -1, COUT) for t in by_owner], axis=1)
    summed = reduce_terms(terms) * grad_scale
    up_part = summed[:up_rows].reshape(4, 4, up_span, COUT)
    mix_part = summed[up_rows:].reshape(3, 3, mix_span, COUT)
    return (section_out, input_grad, up_part, mix_part)


def exchange(part, axis, step):
    size = lax.axis_size(axis)
    return lax.ppermute(part, axis, [(i, i ^ step) for i in range(size)])


def halve(buffer, axis, step, dim):
    own = lax.axis_index(axis) // step % 2
    keep = lax.dynamic_index_in_dim(buffer, own, dim, keepdims=False)
    send = lax.dynamic_index_in_dim(buffer, 1 - own, dim, keepdims=False)
    return keep + exchange(send.astype(jnp.bfloat16), axis, step).astype(keep.dtype)


def double(part, axis, step):
    own = lax.axis_index(axis) // step % 2
    got = exchange(part, axis, step)
    low = jnp.where(own == 0, part, got)
    high = jnp.where(own == 0, got, part)
    return jnp.concatenate([low, high])


def steps_of(size):
    count = size.bit_length() - 1
    return [1 << k for k in range(count)] if size == 1 << count else None


def scatter_lon(rows, order):
    lon_count = rows.shape[0]
    steps = steps_of(lon_count)
    width = len(steps)
    grid = rows.reshape((2,) * width + rows.shape[1:])
    held = list(reversed(steps))
    for step in order:
        dim = held.index(step)
        grid = halve(grid, "lon", step, dim)
        held.pop(dim)
    return grid


def reduce_lat(flat):
    steps = steps_of(lax.axis_size("lat"))
    if steps is None or flat.shape[0] % 2:
        return lax.psum(flat, "lat")
    pair = flat.reshape((2, flat.shape[0] // 2) + flat.shape[1:])
    part = halve(pair, "lat", steps[0], 0).astype(jnp.bfloat16)
    for step in steps[1:]:
        got = exchange(part, "lat", step)
        part = (part.astype(jnp.float32) + got.astype(jnp.float32)).astype(jnp.bfloat16)
    return double(part, "lat", steps[0]).astype(jnp.float32)


def reduce_terms(rows):
    lon_count = rows.shape[0]
    steps = steps_of(lon_count)
    if steps is None or rows.shape[1] % 2:
        own = lax.axis_index("lon")
        mine = lax.dynamic_index_in_dim(lax.psum(rows, "lon"), own, 0, keepdims=False)
        return reduce_lat(mine)
    half = rows.shape[1] // 2
    first = scatter_lon(rows[:, :half], steps)
    second = scatter_lon(rows[:, half:], list(reversed(steps)))
    return jnp.concatenate([reduce_lat(first), reduce_lat(second)])


def solution(mesh):
    placed = (P("lat", "lon", None), P("lat", "lon", None), P(), P(), P(), P("lat", "lon", None))
    return jax.shard_map(
        shards,
        mesh=mesh,
        in_specs=placed,
        out_specs=(
            P("lat", "lon", None),
            P("lat", "lon", None),
            P(None, None, "lon", None),
            P(None, None, "lon", None),
        ),
        check_vma=False,
    )
```

```python
import math

import jax
import jax.numpy as jnp
from jax import lax
from jax.sharding import PartitionSpec as P

CIN = 256
COUT = 128
BLOCK = 32


row_taps = (((1, 0), (3, -1)), ((0, 1), (2, 0)))


def swap_edges(fields, margins, axis, dim, wrap):
    size = lax.axis_size(axis)
    up = [(i, (i + 1) % size) for i in range(size if wrap else size - 1)]
    down = [(j, i) for i, j in up]
    lasts, leads = [], []
    for field, width in zip(fields, margins):
        length = field.shape[dim]
        lasts.append(lax.slice_in_dim(field, length - width, length, axis=dim))
        leads.append(lax.slice_in_dim(field, 0, width, axis=dim))
    before = lax.ppermute(jnp.concatenate([p.reshape(-1) for p in lasts]), axis, up)
    after = lax.ppermute(jnp.concatenate([p.reshape(-1) for p in leads]), axis, down)
    joined, at = [], 0
    for field, last, lead in zip(fields, lasts, leads):
        count = last.size
        head = before[at : at + count].reshape(last.shape)
        tail = after[at : at + count].reshape(lead.shape)
        joined.append(jnp.concatenate([head, field, tail], axis=dim))
        at += count
    return joined


def extend_all(fields, margins):
    widened = swap_edges(fields, margins, "lon", 1, True)
    return swap_edges(widened, margins, "lat", 0, False)


def decode(elem_codes, block_exps):
    sign_bit = elem_codes // 128
    exponent = elem_codes // 8 % 16
    mantissa = elem_codes % 8
    magnitude = jnp.exp2((exponent - 7).astype(jnp.float32)) * (
        1.0 + mantissa.astype(jnp.float32) / 8.0
    )
    signed = jnp.where(sign_bit == 1, -magnitude, magnitude)
    factor = jnp.repeat(jnp.exp2(block_exps.astype(jnp.float32)), BLOCK, axis=2)
    return (signed * factor).astype(jnp.bfloat16)


def slope(pre_act):
    plain = pre_act.astype(jnp.float32)
    sigmoid_v = jax.nn.sigmoid(plain)
    return sigmoid_v * (1.0 + plain * (1.0 - sigmoid_v))


def upsample(padded, up_kernel, row_count, col_count):
    halves = []
    for row_par in (1, 0):
        lane_list = []
        for col_par in (1, 0):
            pieces = []
            kernels = []
            for row_tap, row_off in row_taps[row_par]:
                for col_tap, col_off in row_taps[col_par]:
                    row_at = 1 + row_off - row_par
                    col_at = 1 + col_off - col_par
                    pieces.append(
                        padded[row_at : row_at + row_count + 1, col_at : col_at + col_count + 1]
                    )
                    kernels.append(up_kernel[row_tap, col_tap])
            stacked = jnp.concatenate(pieces, axis=2)
            kernel = jnp.concatenate(kernels, axis=0)
            lane_list.append(
                jnp.einsum("rck,kn->rcn", stacked, kernel, preferred_element_type=jnp.float32)
            )
        halves.append(jnp.stack(lane_list, axis=2))
    merged = jnp.stack(halves, axis=1)
    return merged.reshape(2 * row_count + 2, 2 * col_count + 2, merged.shape[-1])


def neighbours(padded, row_count, col_count, flipped):
    pieces = []
    for row_tap in range(3):
        for col_tap in range(3):
            row_at = 2 - row_tap if flipped else row_tap
            col_at = 2 - col_tap if flipped else col_tap
            pieces.append(padded[row_at : row_at + row_count, col_at : col_at + col_count])
    return jnp.concatenate(pieces, axis=2)


def strided(padded, row_count, col_count):
    split = padded.reshape(row_count + 1, 2, col_count + 1, 2, padded.shape[-1])
    pieces = []
    for row_tap in range(4):
        for col_tap in range(4):
            row_at, col_at = (row_tap // 2, col_tap // 2)
            pieces.append(
                split[
                    row_at : row_at + row_count,
                    row_tap % 2,
                    col_at : col_at + col_count,
                    col_tap % 2,
                ]
            )
    return jnp.concatenate(pieces, axis=2)


def shards(elem_codes, block_exps, up_kernel, up_bias, mix_kernel, cotangent):
    inputs = decode(elem_codes, block_exps)
    in_rows, in_cols = (inputs.shape[0], inputs.shape[1])
    out_rows, out_cols = (2 * in_rows, 2 * in_cols)
    lat_count = lax.axis_size("lat")
    lon_count = lax.axis_size("lon")
    back_mix = mix_kernel[::-1, ::-1].transpose(0, 1, 3, 2)
    padded_in, grad_pad = extend_all((inputs, cotangent), (1, 2))
    raw = upsample(padded_in, up_kernel, in_rows, in_cols)
    pre_act = (raw + up_bias).astype(jnp.bfloat16)
    row_at = lax.axis_index("lat") * out_rows - 1 + lax.broadcasted_iota(jnp.int32, (out_rows + 2, 1, 1), 0)
    inside = (row_at >= 0) & (row_at < out_rows * lat_count)
    activated = jax.nn.silu(pre_act.astype(jnp.float32)).astype(jnp.bfloat16)
    act_pad = jnp.where(inside, activated, jnp.zeros_like(activated))
    act_grad = lax.conv_general_dilated(
        grad_pad[None],
        back_mix,
        (1, 1),
        "VALID",
        dimension_numbers=("NHWC", "HWIO", "NHWC"),
        preferred_element_type=jnp.float32,
    )[0]
    pre_grad = (act_grad * slope(pre_act)).astype(jnp.bfloat16)
    pre_grad_pad = jnp.where(inside, pre_grad, jnp.zeros_like(pre_grad))
    patches = neighbours(act_pad, out_rows, out_cols, False)
    mix_flat = mix_kernel.reshape(9 * COUT, COUT)
    section_out = jnp.einsum(
        "rck,kn->rcn", patches, mix_flat, preferred_element_type=jnp.float32
    ).astype(jnp.bfloat16)
    grad_scale = 1.0 / math.sqrt(out_rows * lat_count * out_cols * lon_count)
    mix_span = COUT // lon_count
    mix_owned = jnp.einsum(
        "rctm,rcn->mtn",
        patches.reshape(out_rows, out_cols, 9, COUT),
        cotangent,
        preferred_element_type=jnp.float32,
    ).reshape(lon_count, mix_span, 9, COUT).transpose(0, 2, 1, 3)
    grad_patches = strided(pre_grad_pad, in_rows, in_cols)
    back_up = up_kernel.transpose(0, 1, 3, 2).reshape(16 * COUT, CIN)
    input_grad = jnp.einsum(
        "rck,kn->rcn", grad_patches, back_up, preferred_element_type=jnp.float32
    )
    up_taps = jnp.einsum(
        "rctn,rcm->tmn",
        grad_patches.reshape(in_rows, in_cols, 16, COUT),
        inputs,
        preferred_element_type=jnp.float32,
    )
    up_span = CIN // lon_count
    up_rows = 16 * up_span
    by_owner = [
        up_taps.reshape(16, lon_count, up_span, COUT).transpose(1, 0, 2, 3),
        mix_owned,
    ]
    terms = jnp.concatenate([t.reshape(lon_count, -1, COUT) for t in by_owner], axis=1)
    summed = reduce_terms(terms) * grad_scale
    up_part = summed[:up_rows].reshape(4, 4, up_span, COUT)
    mix_part = summed[up_rows:].reshape(3, 3, mix_span, COUT)
    return (section_out, input_grad, up_part, mix_part)


def exchange(part, axis, step):
    size = lax.axis_size(axis)
    return lax.ppermute(part, axis, [(i, i ^ step) for i in range(size)])


def halve(buffer, axis, step, dim):
    own = lax.axis_index(axis) // step % 2
    keep = lax.dynamic_index_in_dim(buffer, own, dim, keepdims=False)
    send = lax.dynamic_index_in_dim(buffer, 1 - own, dim, keepdims=False)
    return keep + exchange(send.astype(jnp.bfloat16), axis, step).astype(keep.dtype)


def double(part, axis, step):
    own = lax.axis_index(axis) // step % 2
    got = exchange(part, axis, step)
    low = jnp.where(own == 0, part, got)
    high = jnp.where(own == 0, got, part)
    return jnp.concatenate([low, high])


def steps_of(size):
    count = size.bit_length() - 1
    return [1 << k for k in range(count)] if size == 1 << count else None


def scatter_lon(rows, order):
    lon_count = rows.shape[0]
    steps = steps_of(lon_count)
    width = len(steps)
    grid = rows.reshape((2,) * width + rows.shape[1:])
    held = list(reversed(steps))
    for step in order:
        dim = held.index(step)
        grid = halve(grid, "lon", step, dim)
        held.pop(dim)
    return grid


def reduce_lat(flat):
    steps = steps_of(lax.axis_size("lat"))
    if steps is None or flat.shape[0] % 2:
        return lax.psum(flat, "lat")
    pair = flat.reshape((2, flat.shape[0] // 2) + flat.shape[1:])
    part = halve(pair, "lat", steps[0], 0).astype(jnp.bfloat16)
    for step in steps[1:]:
        got = exchange(part, "lat", step)
        part = (part.astype(jnp.float32) + got.astype(jnp.float32)).astype(jnp.bfloat16)
    return double(part, "lat", steps[0]).astype(jnp.float32)


def reduce_terms(rows):
    lon_count = rows.shape[0]
    steps = steps_of(lon_count)
    if steps is None or rows.shape[1] % 2:
        own = lax.axis_index("lon")
        mine = lax.dynamic_index_in_dim(lax.psum(rows, "lon"), own, 0, keepdims=False)
        return reduce_lat(mine)
    half = rows.shape[1] // 2
    first = scatter_lon(rows[:, :half], steps)
    second = scatter_lon(rows[:, half:], list(reversed(steps)))
    return jnp.concatenate([reduce_lat(first), reduce_lat(second)])


def solution(mesh):
    placed = (P("lat", "lon", None), P("lat", "lon", None), P(), P(), P(), P("lat", "lon", None))
    return jax.shard_map(
        shards,
        mesh=mesh,
        in_specs=placed,
        out_specs=(
            P("lat", "lon", None),
            P("lat", "lon", None),
            P(None, None, "lon", None),
            P(None, None, "lon", None),
        ),
        check_vma=False,
    )
```

```python
import math

import jax
import jax.numpy as jnp
from jax import lax
from jax.sharding import PartitionSpec as P

CIN = 256
COUT = 128
BLOCK = 32


row_taps = (((1, 0), (3, -1)), ((0, 1), (2, 0)))


def swap_edges(fields, margins, axis, dim, wrap):
    size = lax.axis_size(axis)
    up = [(i, (i + 1) % size) for i in range(size if wrap else size - 1)]
    down = [(j, i) for i, j in up]
    lasts, leads = [], []
    for field, width in zip(fields, margins):
        length = field.shape[dim]
        lasts.append(lax.slice_in_dim(field, length - width, length, axis=dim))
        leads.append(lax.slice_in_dim(field, 0, width, axis=dim))
    before = lax.ppermute(jnp.concatenate([p.reshape(-1) for p in lasts]), axis, up)
    after = lax.ppermute(jnp.concatenate([p.reshape(-1) for p in leads]), axis, down)
    joined, at = [], 0
    for field, last, lead in zip(fields, lasts, leads):
        count = last.size
        head = before[at : at + count].reshape(last.shape)
        tail = after[at : at + count].reshape(lead.shape)
        joined.append(jnp.concatenate([head, field, tail], axis=dim))
        at += count
    return joined


def extend_all(fields, margins):
    widened = swap_edges(fields, margins, "lon", 1, True)
    return swap_edges(widened, margins, "lat", 0, False)


def decode(elem_codes, block_exps):
    sign_bit = elem_codes // 128
    exponent = elem_codes // 8 % 16
    mantissa = elem_codes % 8
    magnitude = jnp.exp2((exponent - 7).astype(jnp.float32)) * (
        1.0 + mantissa.astype(jnp.float32) / 8.0
    )
    signed = jnp.where(sign_bit == 1, -magnitude, magnitude)
    factor = jnp.repeat(jnp.exp2(block_exps.astype(jnp.float32)), BLOCK, axis=2)
    return (signed * factor).astype(jnp.bfloat16)


def slope(pre_act):
    plain = pre_act.astype(jnp.float32)
    sigmoid_v = jax.nn.sigmoid(plain)
    return sigmoid_v * (1.0 + plain * (1.0 - sigmoid_v))


def upsample(padded, up_kernel, row_count, col_count):
    halves = []
    for row_par in (1, 0):
        lane_list = []
        for col_par in (1, 0):
            pieces = []
            kernels = []
            for row_tap, row_off in row_taps[row_par]:
                for col_tap, col_off in row_taps[col_par]:
                    row_at = 1 + row_off - row_par
                    col_at = 1 + col_off - col_par
                    pieces.append(
                        padded[row_at : row_at + row_count + 1, col_at : col_at + col_count + 1]
                    )
                    kernels.append(up_kernel[row_tap, col_tap])
            stacked = jnp.concatenate(pieces, axis=2)
            kernel = jnp.concatenate(kernels, axis=0)
            lane_list.append(
                jnp.einsum("rck,kn->rcn", stacked, kernel, preferred_element_type=jnp.float32)
            )
        halves.append(jnp.stack(lane_list, axis=2))
    merged = jnp.stack(halves, axis=1)
    return merged.reshape(2 * row_count + 2, 2 * col_count + 2, merged.shape[-1])


def neighbours(padded, row_count, col_count, flipped):
    pieces = []
    for row_tap in range(3):
        for col_tap in range(3):
            row_at = 2 - row_tap if flipped else row_tap
            col_at = 2 - col_tap if flipped else col_tap
            pieces.append(padded[row_at : row_at + row_count, col_at : col_at + col_count])
    return jnp.concatenate(pieces, axis=2)


def strided(padded, row_count, col_count):
    split = padded.reshape(row_count + 1, 2, col_count + 1, 2, padded.shape[-1])
    pieces = []
    for row_tap in range(4):
        for col_tap in range(4):
            row_at, col_at = (row_tap // 2, col_tap // 2)
            pieces.append(
                split[
                    row_at : row_at + row_count,
                    row_tap % 2,
                    col_at : col_at + col_count,
                    col_tap % 2,
                ]
            )
    return jnp.concatenate(pieces, axis=2)


def shards(elem_codes, block_exps, up_kernel, up_bias, mix_kernel, cotangent):
    inputs = decode(elem_codes, block_exps)
    in_rows, in_cols = (inputs.shape[0], inputs.shape[1])
    out_rows, out_cols = (2 * in_rows, 2 * in_cols)
    lat_count = lax.axis_size("lat")
    lon_count = lax.axis_size("lon")
    back_mix = mix_kernel[::-1, ::-1].transpose(0, 1, 3, 2)
    padded_in, grad_pad = extend_all((inputs, cotangent), (1, 2))
    raw = upsample(padded_in, up_kernel, in_rows, in_cols)
    pre_act = (raw + up_bias).astype(jnp.bfloat16)
    row_at = lax.axis_index("lat") * out_rows - 1 + lax.broadcasted_iota(jnp.int32, (out_rows + 2, 1, 1), 0)
    inside = (row_at >= 0) & (row_at < out_rows * lat_count)
    activated = jax.nn.silu(pre_act.astype(jnp.float32)).astype(jnp.bfloat16)
    act_pad = jnp.where(inside, activated, jnp.zeros_like(activated))
    act_grad = lax.conv_general_dilated(
        grad_pad[None],
        back_mix,
        (1, 1),
        "VALID",
        dimension_numbers=("NHWC", "HWIO", "NHWC"),
        preferred_element_type=jnp.float32,
    )[0]
    pre_grad = (act_grad * slope(pre_act)).astype(jnp.bfloat16)
    pre_grad_pad = jnp.where(inside, pre_grad, jnp.zeros_like(pre_grad))
    patches = neighbours(act_pad, out_rows, out_cols, False)
    mix_flat = mix_kernel.reshape(9 * COUT, COUT)
    section_out = jnp.einsum(
        "rck,kn->rcn", patches, mix_flat, preferred_element_type=jnp.float32
    ).astype(jnp.bfloat16)
    grad_scale = 1.0 / math.sqrt(out_rows * lat_count * out_cols * lon_count)
    mix_span = COUT // lon_count
    mix_owned = jnp.einsum(
        "rctm,rcn->mtn",
        patches.reshape(out_rows, out_cols, 9, COUT),
        cotangent,
        preferred_element_type=jnp.float32,
    ).reshape(lon_count, mix_span, 9, COUT).transpose(0, 2, 1, 3)
    grad_patches = strided(pre_grad_pad, in_rows, in_cols)
    back_up = up_kernel.transpose(0, 1, 3, 2).reshape(16 * COUT, CIN)
    input_grad = jnp.einsum(
        "rck,kn->rcn", grad_patches, back_up, preferred_element_type=jnp.float32
    )
    up_taps = jnp.einsum(
        "rctn,rcm->tmn",
        grad_patches.reshape(in_rows, in_cols, 16, COUT),
        inputs,
        preferred_element_type=jnp.float32,
    )
    up_span = CIN // lon_count
    up_rows = 16 * up_span
    by_owner = [
        up_taps.reshape(16, lon_count, up_span, COUT).transpose(1, 0, 2, 3),
        mix_owned,
    ]
    terms = jnp.concatenate([t.reshape(lon_count, -1, COUT) for t in by_owner], axis=1)
    summed = reduce_terms(terms) * grad_scale
    up_part = summed[:up_rows].reshape(4, 4, up_span, COUT)
    mix_part = summed[up_rows:].reshape(3, 3, mix_span, COUT)
    return (section_out, input_grad, up_part, mix_part)


def exchange(part, axis, step):
    size = lax.axis_size(axis)
    return lax.ppermute(part, axis, [(i, i ^ step) for i in range(size)])


def halve(buffer, axis, step, dim):
    own = lax.axis_index(axis) // step % 2
    keep = lax.dynamic_index_in_dim(buffer, own, dim, keepdims=False)
    send = lax.dynamic_index_in_dim(buffer, 1 - own, dim, keepdims=False)
    return keep + exchange(send.astype(jnp.bfloat16), axis, step).astype(keep.dtype)


def double(part, axis, step):
    own = lax.axis_index(axis) // step % 2
    got = exchange(part, axis, step)
    low = jnp.where(own == 0, part, got)
    high = jnp.where(own == 0, got, part)
    return jnp.concatenate([low, high])


def steps_of(size):
    count = size.bit_length() - 1
    return [1 << k for k in range(count)] if size == 1 << count else None


def scatter_lon(rows, order):
    lon_count = rows.shape[0]
    steps = steps_of(lon_count)
    width = len(steps)
    grid = rows.reshape((2,) * width + rows.shape[1:])
    held = list(reversed(steps))
    for step in order:
        dim = held.index(step)
        grid = halve(grid, "lon", step, dim)
        held.pop(dim)
    return grid


def reduce_lat(flat):
    steps = steps_of(lax.axis_size("lat"))
    if steps is None or flat.shape[0] % 2:
        return lax.psum(flat, "lat")
    pair = flat.reshape((2, flat.shape[0] // 2) + flat.shape[1:])
    part = halve(pair, "lat", steps[0], 0).astype(jnp.bfloat16)
    for step in steps[1:]:
        got = exchange(part, "lat", step)
        part = (part.astype(jnp.float32) + got.astype(jnp.float32)).astype(jnp.bfloat16)
    return double(part, "lat", steps[0]).astype(jnp.float32)


def reduce_terms(rows):
    lon_count = rows.shape[0]
    steps = steps_of(lon_count)
    if steps is None or rows.shape[1] % 2:
        own = lax.axis_index("lon")
        mine = lax.dynamic_index_in_dim(lax.psum(rows, "lon"), own, 0, keepdims=False)
        return reduce_lat(mine)
    half = rows.shape[1] // 2
    first = scatter_lon(rows[:, :half], steps)
    second = scatter_lon(rows[:, half:], list(reversed(steps)))
    return reduce_lat(jnp.concatenate([first, second]))


def solution(mesh):
    placed = (P("lat", "lon", None), P("lat", "lon", None), P(), P(), P(), P("lat", "lon", None))
    return jax.shard_map(
        shards,
        mesh=mesh,
        in_specs=placed,
        out_specs=(
            P("lat", "lon", None),
            P("lat", "lon", None),
            P(None, None, "lon", None),
            P(None, None, "lon", None),
        ),
        check_vma=False,
    )
```

```python
import math

import jax
import jax.numpy as jnp
from jax import lax
from jax.sharding import PartitionSpec as P

CIN = 256
COUT = 128
BLOCK = 32


row_taps = (((1, 0), (3, -1)), ((0, 1), (2, 0)))


def swap_edges(fields, margins, axis, dim, wrap):
    size = lax.axis_size(axis)
    up = [(i, (i + 1) % size) for i in range(size if wrap else size - 1)]
    down = [(j, i) for i, j in up]
    lasts, leads = [], []
    for field, width in zip(fields, margins):
        length = field.shape[dim]
        lasts.append(lax.slice_in_dim(field, length - width, length, axis=dim))
        leads.append(lax.slice_in_dim(field, 0, width, axis=dim))
    before = lax.ppermute(jnp.concatenate([p.reshape(-1) for p in lasts]), axis, up)
    after = lax.ppermute(jnp.concatenate([p.reshape(-1) for p in leads]), axis, down)
    joined, at = [], 0
    for field, last, lead in zip(fields, lasts, leads):
        count = last.size
        head = before[at : at + count].reshape(last.shape)
        tail = after[at : at + count].reshape(lead.shape)
        joined.append(jnp.concatenate([head, field, tail], axis=dim))
        at += count
    return joined


def extend_all(fields, margins):
    widened = swap_edges(fields, margins, "lon", 1, True)
    return swap_edges(widened, margins, "lat", 0, False)


def decode(elem_codes, block_exps):
    sign_bit = elem_codes // 128
    exponent = elem_codes // 8 % 16
    mantissa = elem_codes % 8
    magnitude = jnp.exp2((exponent - 7).astype(jnp.float32)) * (
        1.0 + mantissa.astype(jnp.float32) / 8.0
    )
    signed = jnp.where(sign_bit == 1, -magnitude, magnitude)
    factor = jnp.repeat(jnp.exp2(block_exps.astype(jnp.float32)), BLOCK, axis=2)
    return (signed * factor).astype(jnp.bfloat16)


def slope(pre_act):
    plain = pre_act.astype(jnp.float32)
    sigmoid_v = jax.nn.sigmoid(plain)
    return sigmoid_v * (1.0 + plain * (1.0 - sigmoid_v))


def upsample(padded, up_kernel, row_count, col_count):
    halves = []
    for row_par in (1, 0):
        lane_list = []
        for col_par in (1, 0):
            pieces = []
            kernels = []
            for row_tap, row_off in row_taps[row_par]:
                for col_tap, col_off in row_taps[col_par]:
                    row_at = 1 + row_off - row_par
                    col_at = 1 + col_off - col_par
                    pieces.append(
                        padded[row_at : row_at + row_count + 1, col_at : col_at + col_count + 1]
                    )
                    kernels.append(up_kernel[row_tap, col_tap])
            stacked = jnp.concatenate(pieces, axis=2)
            kernel = jnp.concatenate(kernels, axis=0)
            lane_list.append(
                jnp.einsum("rck,kn->rcn", stacked, kernel, preferred_element_type=jnp.float32)
            )
        halves.append(jnp.stack(lane_list, axis=2))
    merged = jnp.stack(halves, axis=1)
    return merged.reshape(2 * row_count + 2, 2 * col_count + 2, merged.shape[-1])


def neighbours(padded, row_count, col_count, flipped):
    pieces = []
    for row_tap in range(3):
        for col_tap in range(3):
            row_at = 2 - row_tap if flipped else row_tap
            col_at = 2 - col_tap if flipped else col_tap
            pieces.append(padded[row_at : row_at + row_count, col_at : col_at + col_count])
    return jnp.concatenate(pieces, axis=2)


def strided(padded, row_count, col_count):
    split = padded.reshape(row_count + 1, 2, col_count + 1, 2, padded.shape[-1])
    pieces = []
    for row_tap in range(4):
        for col_tap in range(4):
            row_at, col_at = (row_tap // 2, col_tap // 2)
            pieces.append(
                split[
                    row_at : row_at + row_count,
                    row_tap % 2,
                    col_at : col_at + col_count,
                    col_tap % 2,
                ]
            )
    return jnp.concatenate(pieces, axis=2)


def shards(elem_codes, block_exps, up_kernel, up_bias, mix_kernel, cotangent):
    inputs = decode(elem_codes, block_exps)
    in_rows, in_cols = (inputs.shape[0], inputs.shape[1])
    out_rows, out_cols = (2 * in_rows, 2 * in_cols)
    lat_count = lax.axis_size("lat")
    lon_count = lax.axis_size("lon")
    back_mix = mix_kernel[::-1, ::-1].transpose(0, 1, 3, 2)
    padded_in, grad_pad = extend_all((inputs, cotangent), (1, 2))
    raw = upsample(padded_in, up_kernel, in_rows, in_cols)
    pre_act = (raw + up_bias).astype(jnp.bfloat16)
    row_at = lax.axis_index("lat") * out_rows - 1 + lax.broadcasted_iota(jnp.int32, (out_rows + 2, 1, 1), 0)
    inside = (row_at >= 0) & (row_at < out_rows * lat_count)
    activated = jax.nn.silu(pre_act.astype(jnp.float32)).astype(jnp.bfloat16)
    act_pad = jnp.where(inside, activated, jnp.zeros_like(activated))
    act_grad = lax.conv_general_dilated(
        grad_pad[None],
        back_mix,
        (1, 1),
        "VALID",
        dimension_numbers=("NHWC", "HWIO", "NHWC"),
        preferred_element_type=jnp.float32,
    )[0]
    pre_grad = (act_grad * slope(pre_act)).astype(jnp.bfloat16)
    pre_grad_pad = jnp.where(inside, pre_grad, jnp.zeros_like(pre_grad))
    patches = neighbours(act_pad, out_rows, out_cols, False)
    mix_flat = mix_kernel.reshape(9 * COUT, COUT)
    section_out = jnp.einsum(
        "rck,kn->rcn", patches, mix_flat, preferred_element_type=jnp.float32
    ).astype(jnp.bfloat16)
    grad_scale = 1.0 / math.sqrt(out_rows * lat_count * out_cols * lon_count)
    mix_span = COUT // lon_count
    mix_owned = jnp.einsum(
        "rctm,rcn->mtn",
        patches.reshape(out_rows, out_cols, 9, COUT),
        cotangent,
        preferred_element_type=jnp.float32,
    ).reshape(lon_count, mix_span, 9, COUT).transpose(0, 2, 1, 3)
    grad_patches = strided(pre_grad_pad, in_rows, in_cols)
    back_up = up_kernel.transpose(0, 1, 3, 2).reshape(16 * COUT, CIN)
    input_grad = jnp.einsum(
        "rck,kn->rcn", grad_patches, back_up, preferred_element_type=jnp.float32
    )
    up_taps = jnp.einsum(
        "rctn,rcm->tmn",
        grad_patches.reshape(in_rows, in_cols, 16, COUT),
        inputs,
        preferred_element_type=jnp.float32,
    )
    up_span = CIN // lon_count
    up_rows = 16 * up_span
    by_owner = [
        up_taps.reshape(16, lon_count, up_span, COUT).transpose(1, 0, 2, 3),
        mix_owned,
    ]
    terms = jnp.concatenate([t.reshape(lon_count, -1, COUT) for t in by_owner], axis=1)
    summed = reduce_terms(terms) * grad_scale
    up_part = summed[:up_rows].reshape(4, 4, up_span, COUT)
    mix_part = summed[up_rows:].reshape(3, 3, mix_span, COUT)
    return (section_out, input_grad, up_part, mix_part)


def exchange(part, axis, step):
    size = lax.axis_size(axis)
    return lax.ppermute(part, axis, [(i, i ^ step) for i in range(size)])


def halve(buffer, axis, step, dim):
    own = lax.axis_index(axis) // step % 2
    keep = lax.dynamic_index_in_dim(buffer, own, dim, keepdims=False)
    send = lax.dynamic_index_in_dim(buffer, 1 - own, dim, keepdims=False)
    return keep + exchange(send.astype(jnp.bfloat16), axis, step).astype(keep.dtype)


def double(part, axis, step):
    own = lax.axis_index(axis) // step % 2
    got = exchange(part, axis, step)
    low = jnp.where(own == 0, part, got)
    high = jnp.where(own == 0, got, part)
    return jnp.concatenate([low, high])


def steps_of(size):
    count = size.bit_length() - 1
    return [1 << k for k in range(count)] if size == 1 << count else None


def scatter_lon(rows, order):
    lon_count = rows.shape[0]
    steps = steps_of(lon_count)
    width = len(steps)
    grid = rows.reshape((2,) * width + rows.shape[1:])
    held = list(reversed(steps))
    for step in order:
        dim = held.index(step)
        grid = halve(grid, "lon", step, dim)
        held.pop(dim)
    return grid


def reduce_lat(flat):
    steps = steps_of(lax.axis_size("lat"))
    if steps is None or flat.shape[0] % 2:
        return lax.psum(flat, "lat")
    pair = flat.reshape((2, flat.shape[0] // 2) + flat.shape[1:])
    part = halve(pair, "lat", steps[0], 0).astype(jnp.bfloat16)
    for step in steps[1:]:
        got = exchange(part, "lat", step)
        part = (part.astype(jnp.float32) + got.astype(jnp.float32)).astype(jnp.bfloat16)
    return double(part, "lat", steps[0]).astype(jnp.float32)


def butterfly(part, steps):
    part = part.astype(jnp.bfloat16)
    for step in steps:
        got = exchange(part, "lat", step)
        part = (part.astype(jnp.float32) + got.astype(jnp.float32)).astype(jnp.bfloat16)
    return part


def reduce_terms(rows):
    lon_count, count = rows.shape[:2]
    steps = steps_of(lon_count)
    lat_steps = steps_of(lax.axis_size("lat"))
    if steps is None or lat_steps is None or count % 4:
        own = lax.axis_index("lon")
        mine = lax.dynamic_index_in_dim(lax.psum(rows, "lon"), own, 0, keepdims=False)
        return reduce_lat(mine)
    pair = rows.reshape((lon_count, 2, count // 2) + rows.shape[2:])
    part = halve(pair, "lat", lat_steps[0], 1)
    half = count // 4
    first = scatter_lon(part[:, :half], steps)
    second = scatter_lon(part[:, half:], list(reversed(steps)))
    joined = jnp.concatenate([butterfly(first, lat_steps[1:]), butterfly(second, lat_steps[1:])])
    return double(joined, "lat", lat_steps[0]).astype(jnp.float32)


def solution(mesh):
    placed = (P("lat", "lon", None), P("lat", "lon", None), P(), P(), P(), P("lat", "lon", None))
    return jax.shard_map(
        shards,
        mesh=mesh,
        in_specs=placed,
        out_specs=(
            P("lat", "lon", None),
            P("lat", "lon", None),
            P(None, None, "lon", None),
            P(None, None, "lon", None),
        ),
        check_vma=False,
    )
```

```python
import math

import jax
import jax.numpy as jnp
from jax import lax
from jax.sharding import PartitionSpec as P

CIN = 256
COUT = 128
BLOCK = 32


row_taps = (((1, 0), (3, -1)), ((0, 1), (2, 0)))


def swap_edges(fields, margins, axis, dim, wrap):
    size = lax.axis_size(axis)
    up = [(i, (i + 1) % size) for i in range(size if wrap else size - 1)]
    down = [(j, i) for i, j in up]
    lasts, leads = [], []
    for field, width in zip(fields, margins):
        length = field.shape[dim]
        lasts.append(lax.slice_in_dim(field, length - width, length, axis=dim))
        leads.append(lax.slice_in_dim(field, 0, width, axis=dim))
    before = lax.ppermute(jnp.concatenate([p.reshape(-1) for p in lasts]), axis, up)
    after = lax.ppermute(jnp.concatenate([p.reshape(-1) for p in leads]), axis, down)
    joined, at = [], 0
    for field, last, lead in zip(fields, lasts, leads):
        count = last.size
        head = before[at : at + count].reshape(last.shape)
        tail = after[at : at + count].reshape(lead.shape)
        joined.append(jnp.concatenate([head, field, tail], axis=dim))
        at += count
    return joined


def extend_all(fields, margins):
    widened = swap_edges(fields, margins, "lon", 1, True)
    return swap_edges(widened, margins, "lat", 0, False)


def decode(elem_codes, block_exps):
    sign_bit = elem_codes // 128
    exponent = elem_codes // 8 % 16
    mantissa = elem_codes % 8
    magnitude = jnp.exp2((exponent - 7).astype(jnp.float32)) * (
        1.0 + mantissa.astype(jnp.float32) / 8.0
    )
    signed = jnp.where(sign_bit == 1, -magnitude, magnitude)
    factor = jnp.repeat(jnp.exp2(block_exps.astype(jnp.float32)), BLOCK, axis=2)
    return (signed * factor).astype(jnp.bfloat16)


def slope(pre_act):
    plain = pre_act.astype(jnp.float32)
    sigmoid_v = jax.nn.sigmoid(plain)
    return sigmoid_v * (1.0 + plain * (1.0 - sigmoid_v))


def upsample(padded, up_kernel, row_count, col_count):
    halves = []
    for row_par in (1, 0):
        lane_list = []
        for col_par in (1, 0):
            pieces = []
            kernels = []
            for row_tap, row_off in row_taps[row_par]:
                for col_tap, col_off in row_taps[col_par]:
                    row_at = 1 + row_off - row_par
                    col_at = 1 + col_off - col_par
                    pieces.append(
                        padded[row_at : row_at + row_count + 1, col_at : col_at + col_count + 1]
                    )
                    kernels.append(up_kernel[row_tap, col_tap])
            stacked = jnp.concatenate(pieces, axis=2)
            kernel = jnp.concatenate(kernels, axis=0)
            lane_list.append(
                jnp.einsum("rck,kn->rcn", stacked, kernel, preferred_element_type=jnp.float32)
            )
        halves.append(jnp.stack(lane_list, axis=2))
    merged = jnp.stack(halves, axis=1)
    return merged.reshape(2 * row_count + 2, 2 * col_count + 2, merged.shape[-1])


def neighbours(padded, row_count, col_count, flipped):
    pieces = []
    for row_tap in range(3):
        for col_tap in range(3):
            row_at = 2 - row_tap if flipped else row_tap
            col_at = 2 - col_tap if flipped else col_tap
            pieces.append(padded[row_at : row_at + row_count, col_at : col_at + col_count])
    return jnp.concatenate(pieces, axis=2)


def strided(padded, row_count, col_count):
    split = padded.reshape(row_count + 1, 2, col_count + 1, 2, padded.shape[-1])
    pieces = []
    for row_tap in range(4):
        for col_tap in range(4):
            row_at, col_at = (row_tap // 2, col_tap // 2)
            pieces.append(
                split[
                    row_at : row_at + row_count,
                    row_tap % 2,
                    col_at : col_at + col_count,
                    col_tap % 2,
                ]
            )
    return jnp.concatenate(pieces, axis=2)


def shards(elem_codes, block_exps, up_kernel, up_bias, mix_kernel, cotangent):
    inputs = decode(elem_codes, block_exps)
    in_rows, in_cols = (inputs.shape[0], inputs.shape[1])
    out_rows, out_cols = (2 * in_rows, 2 * in_cols)
    lat_count = lax.axis_size("lat")
    lon_count = lax.axis_size("lon")
    back_mix = mix_kernel[::-1, ::-1].transpose(0, 1, 3, 2)
    padded_in, grad_pad = extend_all((inputs, cotangent), (1, 2))
    raw = upsample(padded_in, up_kernel, in_rows, in_cols)
    pre_act = (raw + up_bias).astype(jnp.bfloat16)
    row_at = lax.axis_index("lat") * out_rows - 1 + lax.broadcasted_iota(jnp.int32, (out_rows + 2, 1, 1), 0)
    inside = (row_at >= 0) & (row_at < out_rows * lat_count)
    activated = jax.nn.silu(pre_act.astype(jnp.float32)).astype(jnp.bfloat16)
    act_pad = jnp.where(inside, activated, jnp.zeros_like(activated))
    act_grad = lax.conv_general_dilated(
        grad_pad[None],
        back_mix,
        (1, 1),
        "VALID",
        dimension_numbers=("NHWC", "HWIO", "NHWC"),
        preferred_element_type=jnp.float32,
    )[0]
    pre_grad = (act_grad * slope(pre_act)).astype(jnp.bfloat16)
    pre_grad_pad = jnp.where(inside, pre_grad, jnp.zeros_like(pre_grad))
    patches = neighbours(act_pad, out_rows, out_cols, False)
    mix_flat = mix_kernel.reshape(9 * COUT, COUT)
    section_out = jnp.einsum(
        "rck,kn->rcn", patches, mix_flat, preferred_element_type=jnp.float32
    ).astype(jnp.bfloat16)
    grad_scale = 1.0 / math.sqrt(out_rows * lat_count * out_cols * lon_count)
    mix_span = COUT // lon_count
    mix_owned = jnp.einsum(
        "rctm,rcn->mtn",
        patches.reshape(out_rows, out_cols, 9, COUT),
        cotangent,
        preferred_element_type=jnp.float32,
    ).reshape(lon_count, mix_span, 9, COUT).transpose(0, 2, 1, 3)
    grad_patches = strided(pre_grad_pad, in_rows, in_cols)
    back_up = up_kernel.transpose(0, 1, 3, 2).reshape(16 * COUT, CIN)
    input_grad = jnp.einsum(
        "rck,kn->rcn", grad_patches, back_up, preferred_element_type=jnp.float32
    )
    up_taps = jnp.einsum(
        "rctn,rcm->tmn",
        grad_patches.reshape(in_rows, in_cols, 16, COUT),
        inputs,
        preferred_element_type=jnp.float32,
    )
    up_span = CIN // lon_count
    up_rows = 16 * up_span
    by_owner = [
        up_taps.reshape(16, lon_count, up_span, COUT).transpose(1, 0, 2, 3),
        mix_owned,
    ]
    terms = jnp.concatenate([t.reshape(lon_count, -1, COUT) for t in by_owner], axis=1)
    summed = reduce_terms(terms) * grad_scale
    up_part = summed[:up_rows].reshape(4, 4, up_span, COUT)
    mix_part = summed[up_rows:].reshape(3, 3, mix_span, COUT)
    return (section_out, input_grad, up_part, mix_part)


def exchange(part, axis, step):
    size = lax.axis_size(axis)
    return lax.ppermute(part, axis, [(i, i ^ step) for i in range(size)])


def halve(buffer, axis, step, dim):
    own = lax.axis_index(axis) // step % 2
    keep = lax.dynamic_index_in_dim(buffer, own, dim, keepdims=False)
    send = lax.dynamic_index_in_dim(buffer, 1 - own, dim, keepdims=False)
    return keep + exchange(send.astype(jnp.bfloat16), axis, step).astype(keep.dtype)


def double(part, axis, step):
    own = lax.axis_index(axis) // step % 2
    got = exchange(part, axis, step)
    low = jnp.where(own == 0, part, got)
    high = jnp.where(own == 0, got, part)
    return jnp.concatenate([low, high])


def steps_of(size):
    count = size.bit_length() - 1
    return [1 << k for k in range(count)] if size == 1 << count else None


def scatter_lon(rows, order):
    lon_count = rows.shape[0]
    steps = steps_of(lon_count)
    width = len(steps)
    grid = rows.reshape((2,) * width + rows.shape[1:])
    held = list(reversed(steps))
    for step in order:
        dim = held.index(step)
        grid = halve(grid, "lon", step, dim)
        held.pop(dim)
    return grid


def reduce_lat(flat):
    steps = steps_of(lax.axis_size("lat"))
    if steps is None or flat.shape[0] % 2:
        return lax.psum(flat, "lat")
    pair = flat.reshape((2, flat.shape[0] // 2) + flat.shape[1:])
    part = halve(pair, "lat", steps[0], 0).astype(jnp.bfloat16)
    for step in steps[1:]:
        got = exchange(part, "lat", step)
        part = (part.astype(jnp.float32) + got.astype(jnp.float32)).astype(jnp.bfloat16)
    return double(part, "lat", steps[0]).astype(jnp.float32)


def butterfly(part, steps):
    part = part.astype(jnp.bfloat16)
    for step in steps:
        got = exchange(part, "lat", step)
        part = (part.astype(jnp.float32) + got.astype(jnp.float32)).astype(jnp.bfloat16)
    return part


def reduce_terms(rows):
    lon_count, count = rows.shape[:2]
    steps = steps_of(lon_count)
    lat_steps = steps_of(lax.axis_size("lat"))
    if steps is None or lat_steps is None or count % 4:
        own = lax.axis_index("lon")
        mine = lax.dynamic_index_in_dim(lax.psum(rows, "lon"), own, 0, keepdims=False)
        return reduce_lat(mine)
    pair = rows.reshape((lon_count, 2, count // 2) + rows.shape[2:])
    part = halve(pair, "lat", lat_steps[0], 1)
    half = count // 4
    first = scatter_lon(part[:, :half], steps)
    second = scatter_lon(part[:, half:], list(reversed(steps)))
    joined = butterfly(jnp.concatenate([first, second]), lat_steps[1:])
    return double(joined, "lat", lat_steps[0]).astype(jnp.float32)


def solution(mesh):
    placed = (P("lat", "lon", None), P("lat", "lon", None), P(), P(), P(), P("lat", "lon", None))
    return jax.shard_map(
        shards,
        mesh=mesh,
        in_specs=placed,
        out_specs=(
            P("lat", "lon", None),
            P("lat", "lon", None),
            P(None, None, "lon", None),
            P(None, None, "lon", None),
        ),
        check_vma=False,
    )
```

```python
import math

import jax
import jax.numpy as jnp
from jax import lax
from jax.sharding import PartitionSpec as P

CIN = 256
COUT = 128
BLOCK = 32


row_taps = (((1, 0), (3, -1)), ((0, 1), (2, 0)))


def swap_edges(fields, margins, axis, dim, wrap):
    size = lax.axis_size(axis)
    up = [(i, (i + 1) % size) for i in range(size if wrap else size - 1)]
    down = [(j, i) for i, j in up]
    lasts, leads = [], []
    for field, width in zip(fields, margins):
        length = field.shape[dim]
        lasts.append(lax.slice_in_dim(field, length - width, length, axis=dim))
        leads.append(lax.slice_in_dim(field, 0, width, axis=dim))
    before = lax.ppermute(jnp.concatenate([p.reshape(-1) for p in lasts]), axis, up)
    after = lax.ppermute(jnp.concatenate([p.reshape(-1) for p in leads]), axis, down)
    joined, at = [], 0
    for field, last, lead in zip(fields, lasts, leads):
        count = last.size
        head = before[at : at + count].reshape(last.shape)
        tail = after[at : at + count].reshape(lead.shape)
        joined.append(jnp.concatenate([head, field, tail], axis=dim))
        at += count
    return joined


def edge(field, width, dim, side):
    if side == 0:
        return field
    length = field.shape[dim]
    start = length - width if side == 1 else 0
    return lax.slice_in_dim(field, start, start + width, axis=dim)


def extend_all(fields, margins):
    lat_count, lon_count = (lax.axis_size("lat"), lax.axis_size("lon"))
    arrived = {}
    for row_side in (1, 0, -1):
        for col_side in (1, 0, -1):
            if row_side == 0 and col_side == 0:
                continue
            pairs = [
                (a * lon_count + o, (a + row_side) * lon_count + (o + col_side) % lon_count)
                for a in range(lat_count)
                for o in range(lon_count)
                if 0 <= a + row_side < lat_count
            ]
            pieces = [
                edge(edge(f, w, 0, row_side), w, 1, col_side) for f, w in zip(fields, margins)
            ]
            flat = jnp.concatenate([p.reshape(-1) for p in pieces])
            got = lax.ppermute(flat, ("lat", "lon"), pairs)
            at, parts = 0, []
            for p in pieces:
                parts.append(got[at : at + p.size].reshape(p.shape))
                at += p.size
            arrived[row_side, col_side] = parts
    joined = []
    for k, field in enumerate(fields):
        bands = []
        for row_side in (1, 0, -1):
            row = [field if (row_side, s) == (0, 0) else arrived[row_side, s][k] for s in (1, 0, -1)]
            bands.append(jnp.concatenate(row, axis=1))
        joined.append(jnp.concatenate(bands, axis=0))
    return joined


def decode(elem_codes, block_exps):
    sign_bit = elem_codes // 128
    exponent = elem_codes // 8 % 16
    mantissa = elem_codes % 8
    magnitude = jnp.exp2((exponent - 7).astype(jnp.float32)) * (
        1.0 + mantissa.astype(jnp.float32) / 8.0
    )
    signed = jnp.where(sign_bit == 1, -magnitude, magnitude)
    factor = jnp.repeat(jnp.exp2(block_exps.astype(jnp.float32)), BLOCK, axis=2)
    return (signed * factor).astype(jnp.bfloat16)


def slope(pre_act):
    plain = pre_act.astype(jnp.float32)
    sigmoid_v = jax.nn.sigmoid(plain)
    return sigmoid_v * (1.0 + plain * (1.0 - sigmoid_v))


def upsample(padded, up_kernel, row_count, col_count):
    halves = []
    for row_par in (1, 0):
        lane_list = []
        for col_par in (1, 0):
            pieces = []
            kernels = []
            for row_tap, row_off in row_taps[row_par]:
                for col_tap, col_off in row_taps[col_par]:
                    row_at = 1 + row_off - row_par
                    col_at = 1 + col_off - col_par
                    pieces.append(
                        padded[row_at : row_at + row_count + 1, col_at : col_at + col_count + 1]
                    )
                    kernels.append(up_kernel[row_tap, col_tap])
            stacked = jnp.concatenate(pieces, axis=2)
            kernel = jnp.concatenate(kernels, axis=0)
            lane_list.append(
                jnp.einsum("rck,kn->rcn", stacked, kernel, preferred_element_type=jnp.float32)
            )
        halves.append(jnp.stack(lane_list, axis=2))
    merged = jnp.stack(halves, axis=1)
    return merged.reshape(2 * row_count + 2, 2 * col_count + 2, merged.shape[-1])


def neighbours(padded, row_count, col_count, flipped):
    pieces = []
    for row_tap in range(3):
        for col_tap in range(3):
            row_at = 2 - row_tap if flipped else row_tap
            col_at = 2 - col_tap if flipped else col_tap
            pieces.append(padded[row_at : row_at + row_count, col_at : col_at + col_count])
    return jnp.concatenate(pieces, axis=2)


def strided(padded, row_count, col_count):
    split = padded.reshape(row_count + 1, 2, col_count + 1, 2, padded.shape[-1])
    pieces = []
    for row_tap in range(4):
        for col_tap in range(4):
            row_at, col_at = (row_tap // 2, col_tap // 2)
            pieces.append(
                split[
                    row_at : row_at + row_count,
                    row_tap % 2,
                    col_at : col_at + col_count,
                    col_tap % 2,
                ]
            )
    return jnp.concatenate(pieces, axis=2)


def shards(elem_codes, block_exps, up_kernel, up_bias, mix_kernel, cotangent):
    inputs = decode(elem_codes, block_exps)
    in_rows, in_cols = (inputs.shape[0], inputs.shape[1])
    out_rows, out_cols = (2 * in_rows, 2 * in_cols)
    lat_count = lax.axis_size("lat")
    lon_count = lax.axis_size("lon")
    back_mix = mix_kernel[::-1, ::-1].transpose(0, 1, 3, 2)
    padded_in, grad_pad = extend_all((inputs, cotangent), (1, 2))
    raw = upsample(padded_in, up_kernel, in_rows, in_cols)
    pre_act = (raw + up_bias).astype(jnp.bfloat16)
    row_at = lax.axis_index("lat") * out_rows - 1 + lax.broadcasted_iota(jnp.int32, (out_rows + 2, 1, 1), 0)
    inside = (row_at >= 0) & (row_at < out_rows * lat_count)
    activated = jax.nn.silu(pre_act.astype(jnp.float32)).astype(jnp.bfloat16)
    act_pad = jnp.where(inside, activated, jnp.zeros_like(activated))
    act_grad = lax.conv_general_dilated(
        grad_pad[None],
        back_mix,
        (1, 1),
        "VALID",
        dimension_numbers=("NHWC", "HWIO", "NHWC"),
        preferred_element_type=jnp.float32,
    )[0]
    pre_grad = (act_grad * slope(pre_act)).astype(jnp.bfloat16)
    pre_grad_pad = jnp.where(inside, pre_grad, jnp.zeros_like(pre_grad))
    patches = neighbours(act_pad, out_rows, out_cols, False)
    mix_flat = mix_kernel.reshape(9 * COUT, COUT)
    section_out = jnp.einsum(
        "rck,kn->rcn", patches, mix_flat, preferred_element_type=jnp.float32
    ).astype(jnp.bfloat16)
    grad_scale = 1.0 / math.sqrt(out_rows * lat_count * out_cols * lon_count)
    mix_span = COUT // lon_count
    mix_owned = jnp.einsum(
        "rctm,rcn->mtn",
        patches.reshape(out_rows, out_cols, 9, COUT),
        cotangent,
        preferred_element_type=jnp.float32,
    ).reshape(lon_count, mix_span, 9, COUT).transpose(0, 2, 1, 3)
    grad_patches = strided(pre_grad_pad, in_rows, in_cols)
    back_up = up_kernel.transpose(0, 1, 3, 2).reshape(16 * COUT, CIN)
    input_grad = jnp.einsum(
        "rck,kn->rcn", grad_patches, back_up, preferred_element_type=jnp.float32
    )
    up_taps = jnp.einsum(
        "rctn,rcm->tmn",
        grad_patches.reshape(in_rows, in_cols, 16, COUT),
        inputs,
        preferred_element_type=jnp.float32,
    )
    up_span = CIN // lon_count
    up_rows = 16 * up_span
    by_owner = [
        up_taps.reshape(16, lon_count, up_span, COUT).transpose(1, 0, 2, 3),
        mix_owned,
    ]
    terms = jnp.concatenate([t.reshape(lon_count, -1, COUT) for t in by_owner], axis=1)
    summed = reduce_terms(terms) * grad_scale
    up_part = summed[:up_rows].reshape(4, 4, up_span, COUT)
    mix_part = summed[up_rows:].reshape(3, 3, mix_span, COUT)
    return (section_out, input_grad, up_part, mix_part)


def exchange(part, axis, step):
    size = lax.axis_size(axis)
    return lax.ppermute(part, axis, [(i, i ^ step) for i in range(size)])


def halve(buffer, axis, step, dim):
    own = lax.axis_index(axis) // step % 2
    keep = lax.dynamic_index_in_dim(buffer, own, dim, keepdims=False)
    send = lax.dynamic_index_in_dim(buffer, 1 - own, dim, keepdims=False)
    return keep + exchange(send.astype(jnp.bfloat16), axis, step).astype(keep.dtype)


def double(part, axis, step):
    own = lax.axis_index(axis) // step % 2
    got = exchange(part, axis, step)
    low = jnp.where(own == 0, part, got)
    high = jnp.where(own == 0, got, part)
    return jnp.concatenate([low, high])


def steps_of(size):
    count = size.bit_length() - 1
    return [1 << k for k in range(count)] if size == 1 << count else None


def scatter_lon(rows, order):
    lon_count = rows.shape[0]
    steps = steps_of(lon_count)
    width = len(steps)
    grid = rows.reshape((2,) * width + rows.shape[1:])
    held = list(reversed(steps))
    for step in order:
        dim = held.index(step)
        grid = halve(grid, "lon", step, dim)
        held.pop(dim)
    return grid


def reduce_lat(flat):
    steps = steps_of(lax.axis_size("lat"))
    if steps is None or flat.shape[0] % 2:
        return lax.psum(flat, "lat")
    pair = flat.reshape((2, flat.shape[0] // 2) + flat.shape[1:])
    part = halve(pair, "lat", steps[0], 0).astype(jnp.bfloat16)
    for step in steps[1:]:
        got = exchange(part, "lat", step)
        part = (part.astype(jnp.float32) + got.astype(jnp.float32)).astype(jnp.bfloat16)
    return double(part, "lat", steps[0]).astype(jnp.float32)


def butterfly(part, steps):
    part = part.astype(jnp.bfloat16)
    for step in steps:
        got = exchange(part, "lat", step)
        part = (part.astype(jnp.float32) + got.astype(jnp.float32)).astype(jnp.bfloat16)
    return part


def reduce_terms(rows):
    lon_count, count = rows.shape[:2]
    steps = steps_of(lon_count)
    lat_steps = steps_of(lax.axis_size("lat"))
    if steps is None or lat_steps is None or count % 4:
        own = lax.axis_index("lon")
        mine = lax.dynamic_index_in_dim(lax.psum(rows, "lon"), own, 0, keepdims=False)
        return reduce_lat(mine)
    pair = rows.reshape((lon_count, 2, count // 2) + rows.shape[2:])
    part = halve(pair, "lat", lat_steps[0], 1)
    half = count // 4
    first = scatter_lon(part[:, :half], steps)
    second = scatter_lon(part[:, half:], list(reversed(steps)))
    joined = jnp.concatenate([butterfly(first, lat_steps[1:]), butterfly(second, lat_steps[1:])])
    return double(joined, "lat", lat_steps[0]).astype(jnp.float32)


def solution(mesh):
    placed = (P("lat", "lon", None), P("lat", "lon", None), P(), P(), P(), P("lat", "lon", None))
    return jax.shard_map(
        shards,
        mesh=mesh,
        in_specs=placed,
        out_specs=(
            P("lat", "lon", None),
            P("lat", "lon", None),
            P(None, None, "lon", None),
            P(None, None, "lon", None),
        ),
        check_vma=False,
    )
```

```python
import math

import jax
import jax.numpy as jnp
from jax import lax
from jax.sharding import PartitionSpec as P

CIN = 256
COUT = 128
BLOCK = 32


row_taps = (((1, 0), (3, -1)), ((0, 1), (2, 0)))


def swap_edges(fields, margins, axis, dim, wrap):
    size = lax.axis_size(axis)
    up = [(i, (i + 1) % size) for i in range(size if wrap else size - 1)]
    down = [(j, i) for i, j in up]
    lasts, leads = [], []
    for field, width in zip(fields, margins):
        length = field.shape[dim]
        lasts.append(lax.slice_in_dim(field, length - width, length, axis=dim))
        leads.append(lax.slice_in_dim(field, 0, width, axis=dim))
    before = lax.ppermute(jnp.concatenate([p.reshape(-1) for p in lasts]), axis, up)
    after = lax.ppermute(jnp.concatenate([p.reshape(-1) for p in leads]), axis, down)
    joined, at = [], 0
    for field, last, lead in zip(fields, lasts, leads):
        count = last.size
        head = before[at : at + count].reshape(last.shape)
        tail = after[at : at + count].reshape(lead.shape)
        joined.append(jnp.concatenate([head, field, tail], axis=dim))
        at += count
    return joined


def extend_all(fields, margins):
    widened = swap_edges(fields, margins, "lon", 1, True)
    return swap_edges(widened, margins, "lat", 0, False)


def decode(elem_codes, block_exps):
    sign_bit = elem_codes // 128
    exponent = elem_codes // 8 % 16
    mantissa = elem_codes % 8
    magnitude = jnp.exp2((exponent - 7).astype(jnp.float32)) * (
        1.0 + mantissa.astype(jnp.float32) / 8.0
    )
    signed = jnp.where(sign_bit == 1, -magnitude, magnitude)
    factor = jnp.repeat(jnp.exp2(block_exps.astype(jnp.float32)), BLOCK, axis=2)
    return (signed * factor).astype(jnp.bfloat16)


def slope(pre_act):
    plain = pre_act.astype(jnp.float32)
    sigmoid_v = jax.nn.sigmoid(plain)
    return sigmoid_v * (1.0 + plain * (1.0 - sigmoid_v))


def upsample(padded, up_kernel, row_count, col_count):
    halves = []
    for row_par in (1, 0):
        lane_list = []
        for col_par in (1, 0):
            pieces = []
            kernels = []
            for row_tap, row_off in row_taps[row_par]:
                for col_tap, col_off in row_taps[col_par]:
                    row_at = 1 + row_off - row_par
                    col_at = 1 + col_off - col_par
                    pieces.append(
                        padded[row_at : row_at + row_count + 1, col_at : col_at + col_count + 1]
                    )
                    kernels.append(up_kernel[row_tap, col_tap])
            stacked = jnp.concatenate(pieces, axis=2)
            kernel = jnp.concatenate(kernels, axis=0)
            lane_list.append(
                jnp.einsum("rck,kn->rcn", stacked, kernel, preferred_element_type=jnp.float32)
            )
        halves.append(jnp.stack(lane_list, axis=2))
    merged = jnp.stack(halves, axis=1)
    return merged.reshape(2 * row_count + 2, 2 * col_count + 2, merged.shape[-1])


def neighbours(padded, row_count, col_count, flipped):
    pieces = []
    for row_tap in range(3):
        for col_tap in range(3):
            row_at = 2 - row_tap if flipped else row_tap
            col_at = 2 - col_tap if flipped else col_tap
            pieces.append(padded[row_at : row_at + row_count, col_at : col_at + col_count])
    return jnp.concatenate(pieces, axis=2)


def strided(padded, row_count, col_count):
    split = padded.reshape(row_count + 1, 2, col_count + 1, 2, padded.shape[-1])
    pieces = []
    for row_tap in range(4):
        for col_tap in range(4):
            row_at, col_at = (row_tap // 2, col_tap // 2)
            pieces.append(
                split[
                    row_at : row_at + row_count,
                    row_tap % 2,
                    col_at : col_at + col_count,
                    col_tap % 2,
                ]
            )
    return jnp.concatenate(pieces, axis=2)


def shards(elem_codes, block_exps, up_kernel, up_bias, mix_kernel, cotangent):
    inputs = decode(elem_codes, block_exps)
    in_rows, in_cols = (inputs.shape[0], inputs.shape[1])
    out_rows, out_cols = (2 * in_rows, 2 * in_cols)
    lat_count = lax.axis_size("lat")
    lon_count = lax.axis_size("lon")
    back_mix = mix_kernel[::-1, ::-1].transpose(0, 1, 3, 2)
    padded_in, grad_pad = extend_all((inputs, cotangent), (1, 2))
    raw = upsample(padded_in, up_kernel, in_rows, in_cols)
    pre_act = (raw + up_bias).astype(jnp.bfloat16)
    row_at = lax.axis_index("lat") * out_rows - 1 + lax.broadcasted_iota(jnp.int32, (out_rows + 2, 1, 1), 0)
    inside = (row_at >= 0) & (row_at < out_rows * lat_count)
    activated = jax.nn.silu(pre_act.astype(jnp.float32)).astype(jnp.bfloat16)
    act_pad = jnp.where(inside, activated, jnp.zeros_like(activated))
    act_grad = lax.conv_general_dilated(
        grad_pad[None],
        back_mix,
        (1, 1),
        "VALID",
        dimension_numbers=("NHWC", "HWIO", "NHWC"),
        preferred_element_type=jnp.float32,
    )[0]
    pre_grad = (act_grad * slope(pre_act)).astype(jnp.bfloat16)
    pre_grad_pad = jnp.where(inside, pre_grad, jnp.zeros_like(pre_grad))
    patches = neighbours(act_pad, out_rows, out_cols, False)
    mix_flat = mix_kernel.reshape(9 * COUT, COUT)
    section_out = jnp.einsum(
        "rck,kn->rcn", patches, mix_flat, preferred_element_type=jnp.float32
    ).astype(jnp.bfloat16)
    grad_scale = 1.0 / math.sqrt(out_rows * lat_count * out_cols * lon_count)
    mix_span = COUT // lon_count
    mix_owned = jnp.einsum(
        "rctm,rcn->mtn",
        patches.reshape(out_rows, out_cols, 9, COUT),
        cotangent,
        preferred_element_type=jnp.float32,
    ).reshape(lon_count, mix_span, 9, COUT).transpose(0, 2, 1, 3)
    grad_patches = strided(pre_grad_pad, in_rows, in_cols)
    back_up = up_kernel.transpose(0, 1, 3, 2).reshape(16 * COUT, CIN)
    input_grad = jnp.einsum(
        "rck,kn->rcn", grad_patches, back_up, preferred_element_type=jnp.float32
    )
    up_taps = jnp.einsum(
        "rctn,rcm->tmn",
        grad_patches.reshape(in_rows, in_cols, 16, COUT),
        inputs,
        preferred_element_type=jnp.float32,
    )
    up_span = CIN // lon_count
    up_rows = 16 * up_span
    by_owner = [
        up_taps.reshape(16, lon_count, up_span, COUT).transpose(1, 0, 2, 3),
        mix_owned,
    ]
    terms = jnp.concatenate([t.reshape(lon_count, -1, COUT) for t in by_owner], axis=1)
    summed = reduce_terms(terms) * grad_scale
    up_part = summed[:up_rows].reshape(4, 4, up_span, COUT)
    mix_part = summed[up_rows:].reshape(3, 3, mix_span, COUT)
    return (section_out, input_grad, up_part, mix_part)


def exchange(part, axis, step):
    size = lax.axis_size(axis)
    return lax.ppermute(part, axis, [(i, i ^ step) for i in range(size)])


def halve(buffer, axis, step, dim):
    own = lax.axis_index(axis) // step % 2
    keep = lax.dynamic_index_in_dim(buffer, own, dim, keepdims=False)
    send = lax.dynamic_index_in_dim(buffer, 1 - own, dim, keepdims=False)
    return keep + exchange(send.astype(jnp.bfloat16), axis, step).astype(keep.dtype)


def double(part, axis, step):
    own = lax.axis_index(axis) // step % 2
    got = exchange(part, axis, step)
    low = jnp.where(own == 0, part, got)
    high = jnp.where(own == 0, got, part)
    return jnp.concatenate([low, high])


def steps_of(size):
    count = size.bit_length() - 1
    return [1 << k for k in range(count)] if size == 1 << count else None


def scatter_lon(rows, order):
    lon_count = rows.shape[0]
    steps = steps_of(lon_count)
    width = len(steps)
    grid = rows.reshape((2,) * width + rows.shape[1:])
    held = list(reversed(steps))
    for step in order:
        dim = held.index(step)
        grid = halve(grid, "lon", step, dim)
        held.pop(dim)
    return grid


def reduce_lat(flat):
    steps = steps_of(lax.axis_size("lat"))
    if steps is None or flat.shape[0] % 2:
        return lax.psum(flat, "lat")
    pair = flat.reshape((2, flat.shape[0] // 2) + flat.shape[1:])
    part = halve(pair, "lat", steps[0], 0).astype(jnp.bfloat16)
    for step in steps[1:]:
        got = exchange(part, "lat", step)
        part = (part.astype(jnp.float32) + got.astype(jnp.float32)).astype(jnp.bfloat16)
    return double(part, "lat", steps[0]).astype(jnp.float32)


def butterfly(part, steps):
    part = part.astype(jnp.bfloat16)
    for step in steps:
        got = exchange(part, "lat", step)
        part = (part.astype(jnp.float32) + got.astype(jnp.float32)).astype(jnp.bfloat16)
    return part


def reduce_terms(rows):
    lon_count, count = rows.shape[:2]
    steps = steps_of(lon_count)
    lat_steps = steps_of(lax.axis_size("lat"))
    if steps is None or lat_steps is None or count % 4:
        own = lax.axis_index("lon")
        mine = lax.dynamic_index_in_dim(lax.psum(rows, "lon"), own, 0, keepdims=False)
        return reduce_lat(mine)
    pair = rows.reshape((lon_count, 2, count // 2) + rows.shape[2:])
    part = halve(pair, "lat", lat_steps[0], 1)
    owned = butterfly(scatter_lon(part, steps), lat_steps[1:])
    return double(owned, "lat", lat_steps[0]).astype(jnp.float32)


def solution(mesh):
    placed = (P("lat", "lon", None), P("lat", "lon", None), P(), P(), P(), P("lat", "lon", None))
    return jax.shard_map(
        shards,
        mesh=mesh,
        in_specs=placed,
        out_specs=(
            P("lat", "lon", None),
            P("lat", "lon", None),
            P(None, None, "lon", None),
            P(None, None, "lon", None),
        ),
        check_vma=False,
    )
```

```python
import math

import jax
import jax.numpy as jnp
from jax import lax
from jax.sharding import PartitionSpec as P

CIN = 256
COUT = 128
BLOCK = 32


row_taps = (((1, 0), (3, -1)), ((0, 1), (2, 0)))


def swap_edges(fields, margins, axis, dim, wrap):
    size = lax.axis_size(axis)
    up = [(i, (i + 1) % size) for i in range(size if wrap else size - 1)]
    down = [(j, i) for i, j in up]
    lasts, leads = [], []
    for field, width in zip(fields, margins):
        length = field.shape[dim]
        lasts.append(lax.slice_in_dim(field, length - width, length, axis=dim))
        leads.append(lax.slice_in_dim(field, 0, width, axis=dim))
    before = lax.ppermute(jnp.concatenate([p.reshape(-1) for p in lasts]), axis, up)
    after = lax.ppermute(jnp.concatenate([p.reshape(-1) for p in leads]), axis, down)
    joined, at = [], 0
    for field, last, lead in zip(fields, lasts, leads):
        count = last.size
        head = before[at : at + count].reshape(last.shape)
        tail = after[at : at + count].reshape(lead.shape)
        joined.append(jnp.concatenate([head, field, tail], axis=dim))
        at += count
    return joined


def extend_all(fields, margins):
    widened = swap_edges(fields, margins, "lon", 1, True)
    return swap_edges(widened, margins, "lat", 0, False)


def decode(elem_codes, block_exps):
    sign_bit = elem_codes // 128
    exponent = elem_codes // 8 % 16
    mantissa = elem_codes % 8
    magnitude = jnp.exp2((exponent - 7).astype(jnp.float32)) * (
        1.0 + mantissa.astype(jnp.float32) / 8.0
    )
    signed = jnp.where(sign_bit == 1, -magnitude, magnitude)
    factor = jnp.repeat(jnp.exp2(block_exps.astype(jnp.float32)), BLOCK, axis=2)
    return (signed * factor).astype(jnp.bfloat16)


def slope(pre_act):
    plain = pre_act.astype(jnp.float32)
    sigmoid_v = jax.nn.sigmoid(plain)
    return sigmoid_v * (1.0 + plain * (1.0 - sigmoid_v))


def upsample(padded, up_kernel, row_count, col_count):
    halves = []
    for row_par in (1, 0):
        lane_list = []
        for col_par in (1, 0):
            pieces = []
            kernels = []
            for row_tap, row_off in row_taps[row_par]:
                for col_tap, col_off in row_taps[col_par]:
                    row_at = 1 + row_off - row_par
                    col_at = 1 + col_off - col_par
                    pieces.append(
                        padded[row_at : row_at + row_count + 1, col_at : col_at + col_count + 1]
                    )
                    kernels.append(up_kernel[row_tap, col_tap])
            stacked = jnp.concatenate(pieces, axis=2)
            kernel = jnp.concatenate(kernels, axis=0)
            lane_list.append(
                jnp.einsum("rck,kn->rcn", stacked, kernel, preferred_element_type=jnp.float32)
            )
        halves.append(jnp.stack(lane_list, axis=2))
    merged = jnp.stack(halves, axis=1)
    return merged.reshape(2 * row_count + 2, 2 * col_count + 2, merged.shape[-1])


def neighbours(padded, row_count, col_count, flipped):
    pieces = []
    for row_tap in range(3):
        for col_tap in range(3):
            row_at = 2 - row_tap if flipped else row_tap
            col_at = 2 - col_tap if flipped else col_tap
            pieces.append(padded[row_at : row_at + row_count, col_at : col_at + col_count])
    return jnp.concatenate(pieces, axis=2)


def strided(padded, row_count, col_count):
    split = padded.reshape(row_count + 1, 2, col_count + 1, 2, padded.shape[-1])
    pieces = []
    for row_tap in range(4):
        for col_tap in range(4):
            row_at, col_at = (row_tap // 2, col_tap // 2)
            pieces.append(
                split[
                    row_at : row_at + row_count,
                    row_tap % 2,
                    col_at : col_at + col_count,
                    col_tap % 2,
                ]
            )
    return jnp.concatenate(pieces, axis=2)


def shards(elem_codes, block_exps, up_kernel, up_bias, mix_kernel, cotangent):
    inputs = decode(elem_codes, block_exps)
    in_rows, in_cols = (inputs.shape[0], inputs.shape[1])
    out_rows, out_cols = (2 * in_rows, 2 * in_cols)
    lat_count = lax.axis_size("lat")
    lon_count = lax.axis_size("lon")
    back_mix = mix_kernel[::-1, ::-1].transpose(0, 1, 3, 2)
    padded_in, grad_pad = extend_all((inputs, cotangent), (1, 2))
    raw = upsample(padded_in, up_kernel, in_rows, in_cols)
    pre_act = (raw + up_bias).astype(jnp.bfloat16)
    row_at = lax.axis_index("lat") * out_rows - 1 + lax.broadcasted_iota(jnp.int32, (out_rows + 2, 1, 1), 0)
    inside = (row_at >= 0) & (row_at < out_rows * lat_count)
    activated = jax.nn.silu(pre_act.astype(jnp.float32)).astype(jnp.bfloat16)
    act_pad = jnp.where(inside, activated, jnp.zeros_like(activated))
    act_grad = lax.conv_general_dilated(
        grad_pad[None],
        back_mix,
        (1, 1),
        "VALID",
        dimension_numbers=("NHWC", "HWIO", "NHWC"),
        preferred_element_type=jnp.float32,
    )[0]
    pre_grad = (act_grad * slope(pre_act)).astype(jnp.bfloat16)
    pre_grad_pad = jnp.where(inside, pre_grad, jnp.zeros_like(pre_grad))
    patches = neighbours(act_pad, out_rows, out_cols, False)
    mix_flat = mix_kernel.reshape(9 * COUT, COUT)
    section_out = jnp.einsum(
        "rck,kn->rcn", patches, mix_flat, preferred_element_type=jnp.float32
    ).astype(jnp.bfloat16)
    grad_scale = 1.0 / math.sqrt(out_rows * lat_count * out_cols * lon_count)
    mix_span = COUT // lon_count
    mix_owned = jnp.einsum(
        "rctm,rcn->mtn",
        patches.reshape(out_rows, out_cols, 9, COUT),
        cotangent,
        preferred_element_type=jnp.float32,
    ).reshape(lon_count, mix_span, 9, COUT).transpose(0, 2, 1, 3)
    grad_patches = strided(pre_grad_pad, in_rows, in_cols)
    input_grad = jnp.einsum(
        "rctn,tmn->rcm",
        grad_patches.reshape(in_rows, in_cols, 16, COUT),
        up_kernel.reshape(16, CIN, COUT),
        preferred_element_type=jnp.float32,
    )
    up_taps = jnp.einsum(
        "rctn,rcm->tmn",
        grad_patches.reshape(in_rows, in_cols, 16, COUT),
        inputs,
        preferred_element_type=jnp.float32,
    )
    up_span = CIN // lon_count
    up_rows = 16 * up_span
    by_owner = [
        up_taps.reshape(16, lon_count, up_span, COUT).transpose(1, 0, 2, 3),
        mix_owned,
    ]
    terms = jnp.concatenate([t.reshape(lon_count, -1, COUT) for t in by_owner], axis=1)
    summed = reduce_terms(terms) * grad_scale
    up_part = summed[:up_rows].reshape(4, 4, up_span, COUT)
    mix_part = summed[up_rows:].reshape(3, 3, mix_span, COUT)
    return (section_out, input_grad, up_part, mix_part)


def exchange(part, axis, step):
    size = lax.axis_size(axis)
    return lax.ppermute(part, axis, [(i, i ^ step) for i in range(size)])


def halve(buffer, axis, step, dim):
    own = lax.axis_index(axis) // step % 2
    keep = lax.dynamic_index_in_dim(buffer, own, dim, keepdims=False)
    send = lax.dynamic_index_in_dim(buffer, 1 - own, dim, keepdims=False)
    return keep + exchange(send.astype(jnp.bfloat16), axis, step).astype(keep.dtype)


def double(part, axis, step):
    own = lax.axis_index(axis) // step % 2
    got = exchange(part, axis, step)
    low = jnp.where(own == 0, part, got)
    high = jnp.where(own == 0, got, part)
    return jnp.concatenate([low, high])


def steps_of(size):
    count = size.bit_length() - 1
    return [1 << k for k in range(count)] if size == 1 << count else None


def scatter_lon(rows, order):
    lon_count = rows.shape[0]
    steps = steps_of(lon_count)
    width = len(steps)
    grid = rows.reshape((2,) * width + rows.shape[1:])
    held = list(reversed(steps))
    for step in order:
        dim = held.index(step)
        grid = halve(grid, "lon", step, dim)
        held.pop(dim)
    return grid


def reduce_lat(flat):
    steps = steps_of(lax.axis_size("lat"))
    if steps is None or flat.shape[0] % 2:
        return lax.psum(flat, "lat")
    pair = flat.reshape((2, flat.shape[0] // 2) + flat.shape[1:])
    part = halve(pair, "lat", steps[0], 0).astype(jnp.bfloat16)
    for step in steps[1:]:
        got = exchange(part, "lat", step)
        part = (part.astype(jnp.float32) + got.astype(jnp.float32)).astype(jnp.bfloat16)
    return double(part, "lat", steps[0]).astype(jnp.float32)


def butterfly(part, steps):
    part = part.astype(jnp.bfloat16)
    for step in steps:
        got = exchange(part, "lat", step)
        part = (part.astype(jnp.float32) + got.astype(jnp.float32)).astype(jnp.bfloat16)
    return part


def reduce_terms(rows):
    lon_count, count = rows.shape[:2]
    steps = steps_of(lon_count)
    lat_steps = steps_of(lax.axis_size("lat"))
    if steps is None or lat_steps is None or count % 4:
        own = lax.axis_index("lon")
        mine = lax.dynamic_index_in_dim(lax.psum(rows, "lon"), own, 0, keepdims=False)
        return reduce_lat(mine)
    pair = rows.reshape((lon_count, 2, count // 2) + rows.shape[2:])
    part = halve(pair, "lat", lat_steps[0], 1)
    half = count // 4
    first = scatter_lon(part[:, :half], steps)
    second = scatter_lon(part[:, half:], list(reversed(steps)))
    joined = jnp.concatenate([butterfly(first, lat_steps[1:]), butterfly(second, lat_steps[1:])])
    return double(joined, "lat", lat_steps[0]).astype(jnp.float32)


def solution(mesh):
    placed = (P("lat", "lon", None), P("lat", "lon", None), P(), P(), P(), P("lat", "lon", None))
    return jax.shard_map(
        shards,
        mesh=mesh,
        in_specs=placed,
        out_specs=(
            P("lat", "lon", None),
            P("lat", "lon", None),
            P(None, None, "lon", None),
            P(None, None, "lon", None),
        ),
        check_vma=False,
    )
```

```python
import math

import jax
import jax.numpy as jnp
from jax import lax
from jax.sharding import PartitionSpec as P

CIN = 256
COUT = 128
BLOCK = 32


row_taps = (((1, 0), (3, -1)), ((0, 1), (2, 0)))


def swap_edges(fields, margins, axis, dim, wrap):
    size = lax.axis_size(axis)
    up = [(i, (i + 1) % size) for i in range(size if wrap else size - 1)]
    down = [(j, i) for i, j in up]
    lasts, leads = [], []
    for field, width in zip(fields, margins):
        length = field.shape[dim]
        lasts.append(lax.slice_in_dim(field, length - width, length, axis=dim))
        leads.append(lax.slice_in_dim(field, 0, width, axis=dim))
    before = lax.ppermute(jnp.concatenate([p.reshape(-1) for p in lasts]), axis, up)
    after = lax.ppermute(jnp.concatenate([p.reshape(-1) for p in leads]), axis, down)
    joined, at = [], 0
    for field, last, lead in zip(fields, lasts, leads):
        count = last.size
        head = before[at : at + count].reshape(last.shape)
        tail = after[at : at + count].reshape(lead.shape)
        joined.append(jnp.concatenate([head, field, tail], axis=dim))
        at += count
    return joined


def extend_all(fields, margins):
    widened = swap_edges(fields, margins, "lat", 0, False)
    return swap_edges(widened, margins, "lon", 1, True)


def decode(elem_codes, block_exps):
    sign_bit = elem_codes // 128
    exponent = elem_codes // 8 % 16
    mantissa = elem_codes % 8
    magnitude = jnp.exp2((exponent - 7).astype(jnp.float32)) * (
        1.0 + mantissa.astype(jnp.float32) / 8.0
    )
    signed = jnp.where(sign_bit == 1, -magnitude, magnitude)
    factor = jnp.repeat(jnp.exp2(block_exps.astype(jnp.float32)), BLOCK, axis=2)
    return (signed * factor).astype(jnp.bfloat16)


def slope(pre_act):
    plain = pre_act.astype(jnp.float32)
    sigmoid_v = jax.nn.sigmoid(plain)
    return sigmoid_v * (1.0 + plain * (1.0 - sigmoid_v))


def upsample(padded, up_kernel, row_count, col_count):
    halves = []
    for row_par in (1, 0):
        lane_list = []
        for col_par in (1, 0):
            pieces = []
            kernels = []
            for row_tap, row_off in row_taps[row_par]:
                for col_tap, col_off in row_taps[col_par]:
                    row_at = 1 + row_off - row_par
                    col_at = 1 + col_off - col_par
                    pieces.append(
                        padded[row_at : row_at + row_count + 1, col_at : col_at + col_count + 1]
                    )
                    kernels.append(up_kernel[row_tap, col_tap])
            stacked = jnp.concatenate(pieces, axis=2)
            kernel = jnp.concatenate(kernels, axis=0)
            lane_list.append(
                jnp.einsum("rck,kn->rcn", stacked, kernel, preferred_element_type=jnp.float32)
            )
        halves.append(jnp.stack(lane_list, axis=2))
    merged = jnp.stack(halves, axis=1)
    return merged.reshape(2 * row_count + 2, 2 * col_count + 2, merged.shape[-1])


def neighbours(padded, row_count, col_count, flipped):
    pieces = []
    for row_tap in range(3):
        for col_tap in range(3):
            row_at = 2 - row_tap if flipped else row_tap
            col_at = 2 - col_tap if flipped else col_tap
            pieces.append(padded[row_at : row_at + row_count, col_at : col_at + col_count])
    return jnp.concatenate(pieces, axis=2)


def strided(padded, row_count, col_count):
    split = padded.reshape(row_count + 1, 2, col_count + 1, 2, padded.shape[-1])
    pieces = []
    for row_tap in range(4):
        for col_tap in range(4):
            row_at, col_at = (row_tap // 2, col_tap // 2)
            pieces.append(
                split[
                    row_at : row_at + row_count,
                    row_tap % 2,
                    col_at : col_at + col_count,
                    col_tap % 2,
                ]
            )
    return jnp.concatenate(pieces, axis=2)


def shards(elem_codes, block_exps, up_kernel, up_bias, mix_kernel, cotangent):
    inputs = decode(elem_codes, block_exps)
    in_rows, in_cols = (inputs.shape[0], inputs.shape[1])
    out_rows, out_cols = (2 * in_rows, 2 * in_cols)
    lat_count = lax.axis_size("lat")
    lon_count = lax.axis_size("lon")
    back_mix = mix_kernel[::-1, ::-1].transpose(0, 1, 3, 2)
    padded_in, grad_pad = extend_all((inputs, cotangent), (1, 2))
    raw = upsample(padded_in, up_kernel, in_rows, in_cols)
    pre_act = (raw + up_bias).astype(jnp.bfloat16)
    row_at = lax.axis_index("lat") * out_rows - 1 + lax.broadcasted_iota(jnp.int32, (out_rows + 2, 1, 1), 0)
    inside = (row_at >= 0) & (row_at < out_rows * lat_count)
    activated = jax.nn.silu(pre_act.astype(jnp.float32)).astype(jnp.bfloat16)
    act_pad = jnp.where(inside, activated, jnp.zeros_like(activated))
    act_grad = lax.conv_general_dilated(
        grad_pad[None],
        back_mix,
        (1, 1),
        "VALID",
        dimension_numbers=("NHWC", "HWIO", "NHWC"),
        preferred_element_type=jnp.float32,
    )[0]
    pre_grad = (act_grad * slope(pre_act)).astype(jnp.bfloat16)
    pre_grad_pad = jnp.where(inside, pre_grad, jnp.zeros_like(pre_grad))
    patches = neighbours(act_pad, out_rows, out_cols, False)
    mix_flat = mix_kernel.reshape(9 * COUT, COUT)
    section_out = jnp.einsum(
        "rck,kn->rcn", patches, mix_flat, preferred_element_type=jnp.float32
    ).astype(jnp.bfloat16)
    grad_scale = 1.0 / math.sqrt(out_rows * lat_count * out_cols * lon_count)
    mix_span = COUT // lon_count
    mix_owned = jnp.einsum(
        "rctm,rcn->mtn",
        patches.reshape(out_rows, out_cols, 9, COUT),
        cotangent,
        preferred_element_type=jnp.float32,
    ).reshape(lon_count, mix_span, 9, COUT).transpose(0, 2, 1, 3)
    grad_patches = strided(pre_grad_pad, in_rows, in_cols)
    input_grad = jnp.einsum(
        "rctn,tmn->rcm",
        grad_patches.reshape(in_rows, in_cols, 16, COUT),
        up_kernel.reshape(16, CIN, COUT),
        preferred_element_type=jnp.float32,
    )
    up_taps = jnp.einsum(
        "rctn,rcm->tmn",
        grad_patches.reshape(in_rows, in_cols, 16, COUT),
        inputs,
        preferred_element_type=jnp.float32,
    )
    up_span = CIN // lon_count
    up_rows = 16 * up_span
    by_owner = [
        up_taps.reshape(16, lon_count, up_span, COUT).transpose(1, 0, 2, 3),
        mix_owned,
    ]
    terms = jnp.concatenate([t.reshape(lon_count, -1, COUT) for t in by_owner], axis=1)
    summed = reduce_terms(terms) * grad_scale
    up_part = summed[:up_rows].reshape(4, 4, up_span, COUT)
    mix_part = summed[up_rows:].reshape(3, 3, mix_span, COUT)
    return (section_out, input_grad, up_part, mix_part)


def exchange(part, axis, step):
    size = lax.axis_size(axis)
    return lax.ppermute(part, axis, [(i, i ^ step) for i in range(size)])


def halve(buffer, axis, step, dim):
    own = lax.axis_index(axis) // step % 2
    keep = lax.dynamic_index_in_dim(buffer, own, dim, keepdims=False)
    send = lax.dynamic_index_in_dim(buffer, 1 - own, dim, keepdims=False)
    return keep + exchange(send.astype(jnp.bfloat16), axis, step).astype(keep.dtype)


def double(part, axis, step):
    own = lax.axis_index(axis) // step % 2
    got = exchange(part, axis, step)
    low = jnp.where(own == 0, part, got)
    high = jnp.where(own == 0, got, part)
    return jnp.concatenate([low, high])


def steps_of(size):
    count = size.bit_length() - 1
    return [1 << k for k in range(count)] if size == 1 << count else None


def scatter_lon(rows, order):
    lon_count = rows.shape[0]
    steps = steps_of(lon_count)
    width = len(steps)
    grid = rows.reshape((2,) * width + rows.shape[1:])
    held = list(reversed(steps))
    for step in order:
        dim = held.index(step)
        grid = halve(grid, "lon", step, dim)
        held.pop(dim)
    return grid


def reduce_lat(flat):
    steps = steps_of(lax.axis_size("lat"))
    if steps is None or flat.shape[0] % 2:
        return lax.psum(flat, "lat")
    pair = flat.reshape((2, flat.shape[0] // 2) + flat.shape[1:])
    part = halve(pair, "lat", steps[0], 0).astype(jnp.bfloat16)
    for step in steps[1:]:
        got = exchange(part, "lat", step)
        part = (part.astype(jnp.float32) + got.astype(jnp.float32)).astype(jnp.bfloat16)
    return double(part, "lat", steps[0]).astype(jnp.float32)


def butterfly(part, steps):
    part = part.astype(jnp.bfloat16)
    for step in steps:
        got = exchange(part, "lat", step)
        part = (part.astype(jnp.float32) + got.astype(jnp.float32)).astype(jnp.bfloat16)
    return part


def reduce_terms(rows):
    lon_count, count = rows.shape[:2]
    steps = steps_of(lon_count)
    lat_steps = steps_of(lax.axis_size("lat"))
    if steps is None or lat_steps is None or count % 4:
        own = lax.axis_index("lon")
        mine = lax.dynamic_index_in_dim(lax.psum(rows, "lon"), own, 0, keepdims=False)
        return reduce_lat(mine)
    pair = rows.reshape((lon_count, 2, count // 2) + rows.shape[2:])
    part = halve(pair, "lat", lat_steps[0], 1)
    half = count // 4
    first = scatter_lon(part[:, :half], steps)
    second = scatter_lon(part[:, half:], list(reversed(steps)))
    joined = jnp.concatenate([butterfly(first, lat_steps[1:]), butterfly(second, lat_steps[1:])])
    return double(joined, "lat", lat_steps[0]).astype(jnp.float32)


def solution(mesh):
    placed = (P("lat", "lon", None), P("lat", "lon", None), P(), P(), P(), P("lat", "lon", None))
    return jax.shard_map(
        shards,
        mesh=mesh,
        in_specs=placed,
        out_specs=(
            P("lat", "lon", None),
            P("lat", "lon", None),
            P(None, None, "lon", None),
            P(None, None, "lon", None),
        ),
        check_vma=False,
    )
```

```python
import math

import jax
import jax.numpy as jnp
from jax import lax
from jax.sharding import PartitionSpec as P

CIN = 256
COUT = 128
BLOCK = 32


row_taps = (((1, 0), (3, -1)), ((0, 1), (2, 0)))


def swap_edges(fields, margins, axis, dim, wrap):
    size = lax.axis_size(axis)
    up = [(i, (i + 1) % size) for i in range(size if wrap else size - 1)]
    down = [(j, i) for i, j in up]
    lasts, leads = [], []
    for field, width in zip(fields, margins):
        length = field.shape[dim]
        lasts.append(lax.slice_in_dim(field, length - width, length, axis=dim))
        leads.append(lax.slice_in_dim(field, 0, width, axis=dim))
    before = lax.ppermute(jnp.concatenate([p.reshape(-1) for p in lasts]), axis, up)
    after = lax.ppermute(jnp.concatenate([p.reshape(-1) for p in leads]), axis, down)
    joined, at = [], 0
    for field, last, lead in zip(fields, lasts, leads):
        count = last.size
        head = before[at : at + count].reshape(last.shape)
        tail = after[at : at + count].reshape(lead.shape)
        joined.append(jnp.concatenate([head, field, tail], axis=dim))
        at += count
    return joined


def extend_all(fields, margins):
    widened = swap_edges(fields, margins, "lon", 1, True)
    return swap_edges(widened, margins, "lat", 0, False)


def decode(elem_codes, block_exps):
    sign_bit = elem_codes // 128
    exponent = elem_codes // 8 % 16
    mantissa = elem_codes % 8
    magnitude = jnp.exp2((exponent - 7).astype(jnp.float32)) * (
        1.0 + mantissa.astype(jnp.float32) / 8.0
    )
    signed = jnp.where(sign_bit == 1, -magnitude, magnitude)
    factor = jnp.repeat(jnp.exp2(block_exps.astype(jnp.float32)), BLOCK, axis=2)
    return (signed * factor).astype(jnp.bfloat16)


def slope(pre_act):
    plain = pre_act.astype(jnp.float32)
    sigmoid_v = jax.nn.sigmoid(plain)
    return sigmoid_v * (1.0 + plain * (1.0 - sigmoid_v))


def upsample(padded, up_kernel, row_count, col_count):
    halves = []
    for row_par in (1, 0):
        lane_list = []
        for col_par in (1, 0):
            pieces = []
            kernels = []
            for row_tap, row_off in row_taps[row_par]:
                for col_tap, col_off in row_taps[col_par]:
                    row_at = 1 + row_off - row_par
                    col_at = 1 + col_off - col_par
                    pieces.append(
                        padded[row_at : row_at + row_count + 1, col_at : col_at + col_count + 1]
                    )
                    kernels.append(up_kernel[row_tap, col_tap])
            stacked = jnp.concatenate(pieces, axis=2)
            kernel = jnp.concatenate(kernels, axis=0)
            lane_list.append(
                jnp.einsum("rck,kn->rcn", stacked, kernel, preferred_element_type=jnp.float32)
            )
        halves.append(jnp.stack(lane_list, axis=2))
    merged = jnp.stack(halves, axis=1)
    return merged.reshape(2 * row_count + 2, 2 * col_count + 2, merged.shape[-1])


def neighbours(padded, row_count, col_count, flipped):
    pieces = []
    for row_tap in range(3):
        for col_tap in range(3):
            row_at = 2 - row_tap if flipped else row_tap
            col_at = 2 - col_tap if flipped else col_tap
            pieces.append(padded[row_at : row_at + row_count, col_at : col_at + col_count])
    return jnp.concatenate(pieces, axis=2)


def strided(padded, row_count, col_count):
    split = padded.reshape(row_count + 1, 2, col_count + 1, 2, padded.shape[-1])
    pieces = []
    for row_tap in range(4):
        for col_tap in range(4):
            row_at, col_at = (row_tap // 2, col_tap // 2)
            pieces.append(
                split[
                    row_at : row_at + row_count,
                    row_tap % 2,
                    col_at : col_at + col_count,
                    col_tap % 2,
                ]
            )
    return jnp.concatenate(pieces, axis=2)


def shards(elem_codes, block_exps, up_kernel, up_bias, mix_kernel, cotangent):
    inputs = decode(elem_codes, block_exps)
    in_rows, in_cols = (inputs.shape[0], inputs.shape[1])
    out_rows, out_cols = (2 * in_rows, 2 * in_cols)
    lat_count = lax.axis_size("lat")
    lon_count = lax.axis_size("lon")
    back_mix = mix_kernel[::-1, ::-1].transpose(0, 1, 3, 2)
    padded_in, grad_pad = extend_all((inputs, cotangent), (1, 2))
    raw = upsample(padded_in, up_kernel, in_rows, in_cols)
    pre_act = (raw + up_bias).astype(jnp.bfloat16)
    row_at = lax.axis_index("lat") * out_rows - 1 + lax.broadcasted_iota(jnp.int32, (out_rows + 2, 1, 1), 0)
    inside = (row_at >= 0) & (row_at < out_rows * lat_count)
    activated = jax.nn.silu(pre_act.astype(jnp.float32)).astype(jnp.bfloat16)
    act_pad = jnp.where(inside, activated, jnp.zeros_like(activated))
    act_grad = lax.conv_general_dilated(
        grad_pad[None],
        back_mix,
        (1, 1),
        "VALID",
        dimension_numbers=("NHWC", "HWIO", "NHWC"),
        preferred_element_type=jnp.float32,
    )[0]
    pre_grad = (act_grad * slope(pre_act)).astype(jnp.bfloat16)
    pre_grad_pad = jnp.where(inside, pre_grad, jnp.zeros_like(pre_grad))
    patches = neighbours(act_pad, out_rows, out_cols, False)
    mix_flat = mix_kernel.reshape(9 * COUT, COUT)
    section_out = jnp.einsum(
        "rck,kn->rcn", patches, mix_flat, preferred_element_type=jnp.float32
    ).astype(jnp.bfloat16)
    grad_scale = 1.0 / math.sqrt(out_rows * lat_count * out_cols * lon_count)
    mix_span = COUT // lon_count
    mix_owned = jnp.einsum(
        "rctm,rcn->mtn",
        patches.reshape(out_rows, out_cols, 9, COUT),
        cotangent,
        preferred_element_type=jnp.float32,
    ).reshape(lon_count, mix_span, 9, COUT).transpose(0, 2, 1, 3)
    grad_patches = strided(pre_grad_pad, in_rows, in_cols)
    input_grad = jnp.einsum(
        "rctn,tmn->rcm",
        grad_patches.reshape(in_rows, in_cols, 16, COUT),
        up_kernel.reshape(16, CIN, COUT),
        preferred_element_type=jnp.float32,
    )
    up_taps = jnp.einsum(
        "rctn,rcm->tmn",
        grad_patches.reshape(in_rows, in_cols, 16, COUT),
        inputs,
        preferred_element_type=jnp.float32,
    )
    up_span = CIN // lon_count
    up_rows = 16 * up_span
    by_owner = [
        up_taps.reshape(16, lon_count, up_span, COUT).transpose(1, 0, 2, 3),
        mix_owned,
    ]
    terms = jnp.concatenate([t.reshape(lon_count, -1, COUT) for t in by_owner], axis=1)
    summed = reduce_terms(terms) * grad_scale
    up_part = summed[:up_rows].reshape(4, 4, up_span, COUT)
    mix_part = summed[up_rows:].reshape(3, 3, mix_span, COUT)
    return (section_out, input_grad, up_part, mix_part)


def exchange(part, axis, step):
    size = lax.axis_size(axis)
    return lax.ppermute(part, axis, [(i, i ^ step) for i in range(size)])


def halve(buffer, axis, step, dim):
    own = lax.axis_index(axis) // step % 2
    keep = lax.dynamic_index_in_dim(buffer, own, dim, keepdims=False)
    send = lax.dynamic_index_in_dim(buffer, 1 - own, dim, keepdims=False)
    return keep + exchange(send.astype(jnp.bfloat16), axis, step).astype(keep.dtype)


def double(part, axis, step):
    own = lax.axis_index(axis) // step % 2
    got = exchange(part, axis, step)
    low = jnp.where(own == 0, part, got)
    high = jnp.where(own == 0, got, part)
    return jnp.concatenate([low, high])


def steps_of(size):
    count = size.bit_length() - 1
    return [1 << k for k in range(count)] if size == 1 << count else None


def scatter_lon(rows, order):
    lon_count = rows.shape[0]
    steps = steps_of(lon_count)
    width = len(steps)
    grid = rows.reshape((2,) * width + rows.shape[1:])
    held = list(reversed(steps))
    for step in order:
        dim = held.index(step)
        grid = halve(grid, "lon", step, dim)
        held.pop(dim)
    return grid


def reduce_lat(flat):
    steps = steps_of(lax.axis_size("lat"))
    if steps is None or flat.shape[0] % 2:
        return lax.psum(flat, "lat")
    pair = flat.reshape((2, flat.shape[0] // 2) + flat.shape[1:])
    part = halve(pair, "lat", steps[0], 0).astype(jnp.bfloat16)
    for step in steps[1:]:
        got = exchange(part, "lat", step)
        part = (part.astype(jnp.float32) + got.astype(jnp.float32)).astype(jnp.bfloat16)
    return double(part, "lat", steps[0]).astype(jnp.float32)


def butterfly(part, steps):
    part = part.astype(jnp.bfloat16)
    for step in steps:
        got = exchange(part, "lat", step)
        part = (part.astype(jnp.float32) + got.astype(jnp.float32)).astype(jnp.bfloat16)
    return part


def reduce_terms(rows):
    lon_count, count = rows.shape[:2]
    steps = steps_of(lon_count)
    lat_steps = steps_of(lax.axis_size("lat"))
    if steps is None or lat_steps is None or count % 4:
        own = lax.axis_index("lon")
        mine = lax.dynamic_index_in_dim(lax.psum(rows, "lon"), own, 0, keepdims=False)
        return reduce_lat(mine)
    pair = rows.reshape((lon_count, 2, count // 2) + rows.shape[2:])
    part = halve(pair, "lat", lat_steps[0], 1)
    half = count // 6 // 8 * 8
    first = scatter_lon(part[:, :half], steps)
    second = scatter_lon(part[:, half:], list(reversed(steps)))
    joined = jnp.concatenate([butterfly(first, lat_steps[1:]), butterfly(second, lat_steps[1:])])
    return double(joined, "lat", lat_steps[0]).astype(jnp.float32)


def solution(mesh):
    placed = (P("lat", "lon", None), P("lat", "lon", None), P(), P(), P(), P("lat", "lon", None))
    return jax.shard_map(
        shards,
        mesh=mesh,
        in_specs=placed,
        out_specs=(
            P("lat", "lon", None),
            P("lat", "lon", None),
            P(None, None, "lon", None),
            P(None, None, "lon", None),
        ),
        check_vma=False,
    )
```

```python
import math

import jax
import jax.numpy as jnp
from jax import lax
from jax.sharding import PartitionSpec as P

CIN = 256
COUT = 128
BLOCK = 32


row_taps = (((1, 0), (3, -1)), ((0, 1), (2, 0)))


def swap_edges(fields, margins, axis, dim, wrap):
    size = lax.axis_size(axis)
    up = [(i, (i + 1) % size) for i in range(size if wrap else size - 1)]
    down = [(j, i) for i, j in up]
    lasts, leads = [], []
    for field, width in zip(fields, margins):
        length = field.shape[dim]
        lasts.append(lax.slice_in_dim(field, length - width, length, axis=dim))
        leads.append(lax.slice_in_dim(field, 0, width, axis=dim))
    before = lax.ppermute(jnp.concatenate([p.reshape(-1) for p in lasts]), axis, up)
    after = lax.ppermute(jnp.concatenate([p.reshape(-1) for p in leads]), axis, down)
    joined, at = [], 0
    for field, last, lead in zip(fields, lasts, leads):
        count = last.size
        head = before[at : at + count].reshape(last.shape)
        tail = after[at : at + count].reshape(lead.shape)
        joined.append(jnp.concatenate([head, field, tail], axis=dim))
        at += count
    return joined


def extend_all(fields, margins):
    widened = swap_edges(fields, margins, "lon", 1, True)
    return swap_edges(widened, margins, "lat", 0, False)


def decode(elem_codes, block_exps):
    sign_bit = elem_codes // 128
    exponent = elem_codes // 8 % 16
    mantissa = elem_codes % 8
    magnitude = jnp.exp2((exponent - 7).astype(jnp.float32)) * (
        1.0 + mantissa.astype(jnp.float32) / 8.0
    )
    signed = jnp.where(sign_bit == 1, -magnitude, magnitude)
    factor = jnp.repeat(jnp.exp2(block_exps.astype(jnp.float32)), BLOCK, axis=2)
    return (signed * factor).astype(jnp.bfloat16)


def slope(pre_act):
    plain = pre_act.astype(jnp.float32)
    sigmoid_v = jax.nn.sigmoid(plain)
    return sigmoid_v * (1.0 + plain * (1.0 - sigmoid_v))


def upsample(padded, up_kernel, row_count, col_count):
    halves = []
    for row_par in (1, 0):
        lane_list = []
        for col_par in (1, 0):
            pieces = []
            kernels = []
            for row_tap, row_off in row_taps[row_par]:
                for col_tap, col_off in row_taps[col_par]:
                    row_at = 1 + row_off - row_par
                    col_at = 1 + col_off - col_par
                    pieces.append(
                        padded[row_at : row_at + row_count + 1, col_at : col_at + col_count + 1]
                    )
                    kernels.append(up_kernel[row_tap, col_tap])
            stacked = jnp.concatenate(pieces, axis=2)
            kernel = jnp.concatenate(kernels, axis=0)
            lane_list.append(
                jnp.einsum("rck,kn->rcn", stacked, kernel, preferred_element_type=jnp.float32)
            )
        halves.append(jnp.stack(lane_list, axis=2))
    merged = jnp.stack(halves, axis=1)
    return merged.reshape(2 * row_count + 2, 2 * col_count + 2, merged.shape[-1])


def neighbours(padded, row_count, col_count, flipped):
    pieces = []
    for row_tap in range(3):
        for col_tap in range(3):
            row_at = 2 - row_tap if flipped else row_tap
            col_at = 2 - col_tap if flipped else col_tap
            pieces.append(padded[row_at : row_at + row_count, col_at : col_at + col_count])
    return jnp.concatenate(pieces, axis=2)


def strided(padded, row_count, col_count):
    split = padded.reshape(row_count + 1, 2, col_count + 1, 2, padded.shape[-1])
    pieces = []
    for row_tap in range(4):
        for col_tap in range(4):
            row_at, col_at = (row_tap // 2, col_tap // 2)
            pieces.append(
                split[
                    row_at : row_at + row_count,
                    row_tap % 2,
                    col_at : col_at + col_count,
                    col_tap % 2,
                ]
            )
    return jnp.concatenate(pieces, axis=2)


def shards(elem_codes, block_exps, up_kernel, up_bias, mix_kernel, cotangent):
    inputs = decode(elem_codes, block_exps)
    in_rows, in_cols = (inputs.shape[0], inputs.shape[1])
    out_rows, out_cols = (2 * in_rows, 2 * in_cols)
    lat_count = lax.axis_size("lat")
    lon_count = lax.axis_size("lon")
    back_mix = mix_kernel[::-1, ::-1].transpose(0, 1, 3, 2)
    padded_in, grad_pad = extend_all((inputs, cotangent), (1, 2))
    raw = upsample(padded_in, up_kernel, in_rows, in_cols)
    pre_act = (raw + up_bias).astype(jnp.bfloat16)
    row_at = lax.axis_index("lat") * out_rows - 1 + lax.broadcasted_iota(jnp.int32, (out_rows + 2, 1, 1), 0)
    inside = (row_at >= 0) & (row_at < out_rows * lat_count)
    activated = jax.nn.silu(pre_act.astype(jnp.float32)).astype(jnp.bfloat16)
    act_pad = jnp.where(inside, activated, jnp.zeros_like(activated))
    act_grad = lax.conv_general_dilated(
        grad_pad[None],
        back_mix,
        (1, 1),
        "VALID",
        dimension_numbers=("NHWC", "HWIO", "NHWC"),
        preferred_element_type=jnp.float32,
    )[0]
    pre_grad = (act_grad * slope(pre_act)).astype(jnp.bfloat16)
    pre_grad_pad = jnp.where(inside, pre_grad, jnp.zeros_like(pre_grad))
    patches = neighbours(act_pad, out_rows, out_cols, False)
    mix_flat = mix_kernel.reshape(9 * COUT, COUT)
    section_out = jnp.einsum(
        "rck,kn->rcn", patches, mix_flat, preferred_element_type=jnp.float32
    ).astype(jnp.bfloat16)
    grad_scale = 1.0 / math.sqrt(out_rows * lat_count * out_cols * lon_count)
    mix_span = COUT // lon_count
    mix_owned = jnp.einsum(
        "rctm,rcn->mtn",
        patches.reshape(out_rows, out_cols, 9, COUT),
        cotangent,
        preferred_element_type=jnp.float32,
    ).reshape(lon_count, mix_span, 9, COUT).transpose(0, 2, 1, 3)
    grad_patches = strided(pre_grad_pad, in_rows, in_cols)
    input_grad = jnp.einsum(
        "rctn,tmn->rcm",
        grad_patches.reshape(in_rows, in_cols, 16, COUT),
        up_kernel.reshape(16, CIN, COUT),
        preferred_element_type=jnp.float32,
    )
    up_taps = jnp.einsum(
        "rctn,rcm->tmn",
        grad_patches.reshape(in_rows, in_cols, 16, COUT),
        inputs,
        preferred_element_type=jnp.float32,
    )
    up_span = CIN // lon_count
    up_rows = 16 * up_span
    by_owner = [
        up_taps.reshape(16, lon_count, up_span, COUT).transpose(1, 0, 2, 3),
        mix_owned,
    ]
    terms = jnp.concatenate([t.reshape(lon_count, -1, COUT) for t in by_owner], axis=1)
    summed = reduce_terms(terms) * grad_scale
    up_part = summed[:up_rows].reshape(4, 4, up_span, COUT)
    mix_part = summed[up_rows:].reshape(3, 3, mix_span, COUT)
    return (section_out, input_grad, up_part, mix_part)


def exchange(part, axis, step):
    size = lax.axis_size(axis)
    return lax.ppermute(part, axis, [(i, i ^ step) for i in range(size)])


def halve(buffer, axis, step, dim):
    own = lax.axis_index(axis) // step % 2
    keep = lax.dynamic_index_in_dim(buffer, own, dim, keepdims=False)
    send = lax.dynamic_index_in_dim(buffer, 1 - own, dim, keepdims=False)
    return keep + exchange(send.astype(jnp.bfloat16), axis, step).astype(keep.dtype)


def double(part, axis, step):
    own = lax.axis_index(axis) // step % 2
    got = exchange(part, axis, step)
    low = jnp.where(own == 0, part, got)
    high = jnp.where(own == 0, got, part)
    return jnp.concatenate([low, high])


def steps_of(size):
    count = size.bit_length() - 1
    return [1 << k for k in range(count)] if size == 1 << count else None


def scatter_lon(rows, order):
    lon_count = rows.shape[0]
    steps = steps_of(lon_count)
    width = len(steps)
    grid = rows.reshape((2,) * width + rows.shape[1:])
    held = list(reversed(steps))
    for step in order:
        dim = held.index(step)
        grid = halve(grid, "lon", step, dim)
        held.pop(dim)
    return grid


def reduce_lat(flat):
    steps = steps_of(lax.axis_size("lat"))
    if steps is None or flat.shape[0] % 2:
        return lax.psum(flat, "lat")
    pair = flat.reshape((2, flat.shape[0] // 2) + flat.shape[1:])
    part = halve(pair, "lat", steps[0], 0).astype(jnp.bfloat16)
    for step in steps[1:]:
        got = exchange(part, "lat", step)
        part = (part.astype(jnp.float32) + got.astype(jnp.float32)).astype(jnp.bfloat16)
    return double(part, "lat", steps[0]).astype(jnp.float32)


def butterfly(part, steps):
    for step in steps:
        part = halve(part.reshape((2, part.shape[0] // 2) + part.shape[1:]), "lat", step, 0)
    part = part.astype(jnp.bfloat16)
    for step in reversed(steps):
        part = double(part, "lat", step)
    return part


def reduce_terms(rows):
    lon_count, count = rows.shape[:2]
    steps = steps_of(lon_count)
    lat_steps = steps_of(lax.axis_size("lat"))
    if steps is None or lat_steps is None or count % (4 << len(lat_steps)):
        own = lax.axis_index("lon")
        mine = lax.dynamic_index_in_dim(lax.psum(rows, "lon"), own, 0, keepdims=False)
        return reduce_lat(mine)
    pair = rows.reshape((lon_count, 2, count // 2) + rows.shape[2:])
    part = halve(pair, "lat", lat_steps[0], 1)
    half = count // 4
    first = scatter_lon(part[:, :half], steps)
    second = scatter_lon(part[:, half:], list(reversed(steps)))
    joined = jnp.concatenate([butterfly(first, lat_steps[1:]), butterfly(second, lat_steps[1:])])
    return double(joined, "lat", lat_steps[0]).astype(jnp.float32)


def solution(mesh):
    placed = (P("lat", "lon", None), P("lat", "lon", None), P(), P(), P(), P("lat", "lon", None))
    return jax.shard_map(
        shards,
        mesh=mesh,
        in_specs=placed,
        out_specs=(
            P("lat", "lon", None),
            P("lat", "lon", None),
            P(None, None, "lon", None),
            P(None, None, "lon", None),
        ),
        check_vma=False,
    )
```

```python
import math

import jax
import jax.numpy as jnp
from jax import lax
from jax.sharding import PartitionSpec as P

CIN = 256
COUT = 128
BLOCK = 32


row_taps = (((1, 0), (3, -1)), ((0, 1), (2, 0)))


def swap_edges(fields, margins, axis, dim, wrap):
    size = lax.axis_size(axis)
    up = [(i, (i + 1) % size) for i in range(size if wrap else size - 1)]
    down = [(j, i) for i, j in up]
    lasts, leads = [], []
    for field, width in zip(fields, margins):
        length = field.shape[dim]
        lasts.append(lax.slice_in_dim(field, length - width, length, axis=dim))
        leads.append(lax.slice_in_dim(field, 0, width, axis=dim))
    before = lax.ppermute(jnp.concatenate([p.reshape(-1) for p in lasts]), axis, up)
    after = lax.ppermute(jnp.concatenate([p.reshape(-1) for p in leads]), axis, down)
    joined, at = [], 0
    for field, last, lead in zip(fields, lasts, leads):
        count = last.size
        head = before[at : at + count].reshape(last.shape)
        tail = after[at : at + count].reshape(lead.shape)
        joined.append(jnp.concatenate([head, field, tail], axis=dim))
        at += count
    return joined


def extend_all(fields, margins):
    widened = swap_edges(fields, margins, "lon", 1, True)
    return swap_edges(widened, margins, "lat", 0, False)


def decode(elem_codes, block_exps):
    sign_bit = elem_codes // 128
    exponent = elem_codes // 8 % 16
    mantissa = elem_codes % 8
    magnitude = jnp.exp2((exponent - 7).astype(jnp.float32)) * (
        1.0 + mantissa.astype(jnp.float32) / 8.0
    )
    signed = jnp.where(sign_bit == 1, -magnitude, magnitude)
    factor = jnp.exp2(block_exps.astype(jnp.float32))[..., None]
    blocks = signed.reshape(block_exps.shape + (BLOCK,))
    return (blocks * factor).reshape(signed.shape).astype(jnp.bfloat16)


def slope(pre_act):
    plain = pre_act.astype(jnp.float32)
    sigmoid_v = jax.nn.sigmoid(plain)
    return sigmoid_v * (1.0 + plain * (1.0 - sigmoid_v))


def upsample(padded, up_kernel, row_count, col_count):
    halves = []
    for row_par in (1, 0):
        lane_list = []
        for col_par in (1, 0):
            pieces = []
            kernels = []
            for row_tap, row_off in row_taps[row_par]:
                for col_tap, col_off in row_taps[col_par]:
                    row_at = 1 + row_off - row_par
                    col_at = 1 + col_off - col_par
                    pieces.append(
                        padded[row_at : row_at + row_count + 1, col_at : col_at + col_count + 1]
                    )
                    kernels.append(up_kernel[row_tap, col_tap])
            stacked = jnp.concatenate(pieces, axis=2)
            kernel = jnp.concatenate(kernels, axis=0)
            lane_list.append(
                jnp.einsum("rck,kn->rcn", stacked, kernel, preferred_element_type=jnp.float32)
            )
        halves.append(jnp.stack(lane_list, axis=2))
    merged = jnp.stack(halves, axis=1)
    return merged.reshape(2 * row_count + 2, 2 * col_count + 2, merged.shape[-1])


def neighbours(padded, row_count, col_count, flipped):
    pieces = []
    for row_tap in range(3):
        for col_tap in range(3):
            row_at = 2 - row_tap if flipped else row_tap
            col_at = 2 - col_tap if flipped else col_tap
            pieces.append(padded[row_at : row_at + row_count, col_at : col_at + col_count])
    return jnp.concatenate(pieces, axis=2)


def strided(padded, row_count, col_count):
    split = padded.reshape(row_count + 1, 2, col_count + 1, 2, padded.shape[-1])
    pieces = []
    for row_tap in range(4):
        for col_tap in range(4):
            row_at, col_at = (row_tap // 2, col_tap // 2)
            pieces.append(
                split[
                    row_at : row_at + row_count,
                    row_tap % 2,
                    col_at : col_at + col_count,
                    col_tap % 2,
                ]
            )
    return jnp.concatenate(pieces, axis=2)


def shards(elem_codes, block_exps, up_kernel, up_bias, mix_kernel, cotangent):
    inputs = decode(elem_codes, block_exps)
    in_rows, in_cols = (inputs.shape[0], inputs.shape[1])
    out_rows, out_cols = (2 * in_rows, 2 * in_cols)
    lat_count = lax.axis_size("lat")
    lon_count = lax.axis_size("lon")
    back_mix = mix_kernel[::-1, ::-1].transpose(0, 1, 3, 2)
    padded_in, grad_pad = extend_all((inputs, cotangent), (1, 2))
    raw = upsample(padded_in, up_kernel, in_rows, in_cols)
    pre_act = (raw + up_bias).astype(jnp.bfloat16)
    row_at = lax.axis_index("lat") * out_rows - 1 + lax.broadcasted_iota(jnp.int32, (out_rows + 2, 1, 1), 0)
    inside = (row_at >= 0) & (row_at < out_rows * lat_count)
    activated = jax.nn.silu(pre_act.astype(jnp.float32)).astype(jnp.bfloat16)
    act_pad = jnp.where(inside, activated, jnp.zeros_like(activated))
    act_grad = lax.conv_general_dilated(
        grad_pad[None],
        back_mix,
        (1, 1),
        "VALID",
        dimension_numbers=("NHWC", "HWIO", "NHWC"),
        preferred_element_type=jnp.float32,
    )[0]
    pre_grad = (act_grad * slope(pre_act)).astype(jnp.bfloat16)
    pre_grad_pad = jnp.where(inside, pre_grad, jnp.zeros_like(pre_grad))
    patches = neighbours(act_pad, out_rows, out_cols, False)
    mix_flat = mix_kernel.reshape(9 * COUT, COUT)
    section_out = jnp.einsum(
        "rck,kn->rcn", patches, mix_flat, preferred_element_type=jnp.float32
    ).astype(jnp.bfloat16)
    grad_scale = 1.0 / math.sqrt(out_rows * lat_count * out_cols * lon_count)
    mix_span = COUT // lon_count
    mix_owned = jnp.einsum(
        "rctm,rcn->mtn",
        patches.reshape(out_rows, out_cols, 9, COUT),
        cotangent,
        preferred_element_type=jnp.float32,
    ).reshape(lon_count, mix_span, 9, COUT).transpose(0, 2, 1, 3)
    grad_patches = strided(pre_grad_pad, in_rows, in_cols)
    input_grad = jnp.einsum(
        "rctn,tmn->rcm",
        grad_patches.reshape(in_rows, in_cols, 16, COUT),
        up_kernel.reshape(16, CIN, COUT),
        preferred_element_type=jnp.float32,
    )
    up_taps = jnp.einsum(
        "rctn,rcm->tmn",
        grad_patches.reshape(in_rows, in_cols, 16, COUT),
        inputs,
        preferred_element_type=jnp.float32,
    )
    up_span = CIN // lon_count
    up_rows = 16 * up_span
    by_owner = [
        up_taps.reshape(16, lon_count, up_span, COUT).transpose(1, 0, 2, 3),
        mix_owned,
    ]
    terms = jnp.concatenate([t.reshape(lon_count, -1, COUT) for t in by_owner], axis=1)
    summed = reduce_terms(terms) * grad_scale
    up_part = summed[:up_rows].reshape(4, 4, up_span, COUT)
    mix_part = summed[up_rows:].reshape(3, 3, mix_span, COUT)
    return (section_out, input_grad, up_part, mix_part)


def exchange(part, axis, step):
    size = lax.axis_size(axis)
    return lax.ppermute(part, axis, [(i, i ^ step) for i in range(size)])


def halve(buffer, axis, step, dim):
    own = lax.axis_index(axis) // step % 2
    keep = lax.dynamic_index_in_dim(buffer, own, dim, keepdims=False)
    send = lax.dynamic_index_in_dim(buffer, 1 - own, dim, keepdims=False)
    return keep + exchange(send.astype(jnp.bfloat16), axis, step).astype(keep.dtype)


def double(part, axis, step):
    own = lax.axis_index(axis) // step % 2
    got = exchange(part, axis, step)
    low = jnp.where(own == 0, part, got)
    high = jnp.where(own == 0, got, part)
    return jnp.concatenate([low, high])


def steps_of(size):
    count = size.bit_length() - 1
    return [1 << k for k in range(count)] if size == 1 << count else None


def scatter_lon(rows, order):
    lon_count = rows.shape[0]
    steps = steps_of(lon_count)
    width = len(steps)
    grid = rows.reshape((2,) * width + rows.shape[1:])
    held = list(reversed(steps))
    for step in order:
        dim = held.index(step)
        grid = halve(grid, "lon", step, dim)
        held.pop(dim)
    return grid


def reduce_lat(flat):
    steps = steps_of(lax.axis_size("lat"))
    if steps is None or flat.shape[0] % 2:
        return lax.psum(flat, "lat")
    pair = flat.reshape((2, flat.shape[0] // 2) + flat.shape[1:])
    part = halve(pair, "lat", steps[0], 0).astype(jnp.bfloat16)
    for step in steps[1:]:
        got = exchange(part, "lat", step)
        part = (part.astype(jnp.float32) + got.astype(jnp.float32)).astype(jnp.bfloat16)
    return double(part, "lat", steps[0]).astype(jnp.float32)


def butterfly(part, steps):
    part = part.astype(jnp.bfloat16)
    for step in steps:
        got = exchange(part, "lat", step)
        part = (part.astype(jnp.float32) + got.astype(jnp.float32)).astype(jnp.bfloat16)
    return part


def reduce_terms(rows):
    lon_count, count = rows.shape[:2]
    steps = steps_of(lon_count)
    lat_steps = steps_of(lax.axis_size("lat"))
    if steps is None or lat_steps is None or count % 4:
        own = lax.axis_index("lon")
        mine = lax.dynamic_index_in_dim(lax.psum(rows, "lon"), own, 0, keepdims=False)
        return reduce_lat(mine)
    pair = rows.reshape((lon_count, 2, count // 2) + rows.shape[2:])
    part = halve(pair, "lat", lat_steps[0], 1)
    half = count // 4
    first = scatter_lon(part[:, :half], steps)
    second = scatter_lon(part[:, half:], list(reversed(steps)))
    joined = jnp.concatenate([butterfly(first, lat_steps[1:]), butterfly(second, lat_steps[1:])])
    return double(joined, "lat", lat_steps[0]).astype(jnp.float32)


def solution(mesh):
    placed = (P("lat", "lon", None), P("lat", "lon", None), P(), P(), P(), P("lat", "lon", None))
    return jax.shard_map(
        shards,
        mesh=mesh,
        in_specs=placed,
        out_specs=(
            P("lat", "lon", None),
            P("lat", "lon", None),
            P(None, None, "lon", None),
            P(None, None, "lon", None),
        ),
        check_vma=False,
    )
```

```python
import math

import jax
import jax.numpy as jnp
from jax import lax
from jax.sharding import PartitionSpec as P

CIN = 256
COUT = 128
BLOCK = 32


row_taps = (((1, 0), (3, -1)), ((0, 1), (2, 0)))


def swap_edges(fields, margins, axis, dim, wrap):
    size = lax.axis_size(axis)
    up = [(i, (i + 1) % size) for i in range(size if wrap else size - 1)]
    down = [(j, i) for i, j in up]
    lasts, leads = [], []
    for field, width in zip(fields, margins):
        length = field.shape[dim]
        lasts.append(lax.slice_in_dim(field, length - width, length, axis=dim))
        leads.append(lax.slice_in_dim(field, 0, width, axis=dim))
    before = lax.ppermute(jnp.concatenate([p.reshape(-1) for p in lasts]), axis, up)
    after = lax.ppermute(jnp.concatenate([p.reshape(-1) for p in leads]), axis, down)
    joined, at = [], 0
    for field, last, lead in zip(fields, lasts, leads):
        count = last.size
        head = before[at : at + count].reshape(last.shape)
        tail = after[at : at + count].reshape(lead.shape)
        joined.append(jnp.concatenate([head, field, tail], axis=dim))
        at += count
    return joined


def extend_all(fields, margins):
    widened = swap_edges(fields, margins, "lon", 1, True)
    return swap_edges(widened, margins, "lat", 0, False)


def decode(elem_codes, block_exps):
    sign_bit = elem_codes // 128
    exponent = elem_codes // 8 % 16
    mantissa = elem_codes % 8
    magnitude = jnp.exp2((exponent - 7).astype(jnp.float32)) * (
        1.0 + mantissa.astype(jnp.float32) / 8.0
    )
    signed = jnp.where(sign_bit == 1, -magnitude, magnitude)
    factor = jnp.repeat(jnp.exp2(block_exps.astype(jnp.float32)), BLOCK, axis=2)
    return (signed * factor).astype(jnp.bfloat16)


def slope(pre_act):
    plain = pre_act.astype(jnp.float32)
    sigmoid_v = jax.nn.sigmoid(plain)
    return sigmoid_v * (1.0 + plain * (1.0 - sigmoid_v))


def upsample(padded, up_kernel, row_count, col_count):
    halves = []
    for row_par in (1, 0):
        lane_list = []
        for col_par in (1, 0):
            pieces = []
            kernels = []
            for row_tap, row_off in row_taps[row_par]:
                for col_tap, col_off in row_taps[col_par]:
                    row_at = 1 + row_off - row_par
                    col_at = 1 + col_off - col_par
                    pieces.append(
                        padded[row_at : row_at + row_count + 1, col_at : col_at + col_count + 1]
                    )
                    kernels.append(up_kernel[row_tap, col_tap])
            stacked = jnp.concatenate(pieces, axis=2)
            kernel = jnp.concatenate(kernels, axis=0)
            lane_list.append(
                jnp.einsum("rck,kn->rcn", stacked, kernel, preferred_element_type=jnp.float32)
            )
        halves.append(jnp.stack(lane_list, axis=2))
    merged = jnp.stack(halves, axis=1)
    return merged.reshape(2 * row_count + 2, 2 * col_count + 2, merged.shape[-1])


def neighbours(padded, row_count, col_count, flipped):
    pieces = []
    for row_tap in range(3):
        for col_tap in range(3):
            row_at = 2 - row_tap if flipped else row_tap
            col_at = 2 - col_tap if flipped else col_tap
            pieces.append(padded[row_at : row_at + row_count, col_at : col_at + col_count])
    return jnp.concatenate(pieces, axis=2)


def strided(padded, row_count, col_count):
    split = padded.reshape(row_count + 1, 2, col_count + 1, 2, padded.shape[-1])
    pieces = []
    for row_tap in range(4):
        for col_tap in range(4):
            row_at, col_at = (row_tap // 2, col_tap // 2)
            pieces.append(
                split[
                    row_at : row_at + row_count,
                    row_tap % 2,
                    col_at : col_at + col_count,
                    col_tap % 2,
                ]
            )
    return jnp.concatenate(pieces, axis=2)


def shards(elem_codes, block_exps, up_kernel, up_bias, mix_kernel, cotangent):
    inputs = decode(elem_codes, block_exps)
    in_rows, in_cols = (inputs.shape[0], inputs.shape[1])
    out_rows, out_cols = (2 * in_rows, 2 * in_cols)
    lat_count = lax.axis_size("lat")
    lon_count = lax.axis_size("lon")
    back_mix = mix_kernel[::-1, ::-1].transpose(0, 1, 3, 2)
    coded = (elem_codes.astype(jnp.bfloat16), block_exps.astype(jnp.bfloat16), cotangent)
    codes_wide, exps_wide, grad_wide = swap_edges(coded, (1, 1, 2), "lon", 1, True)
    inputs_wide = decode(codes_wide.astype(jnp.int32), exps_wide.astype(jnp.int32))
    padded_in, grad_pad = swap_edges((inputs_wide, grad_wide), (1, 2), "lat", 0, False)
    raw = upsample(padded_in, up_kernel, in_rows, in_cols)
    pre_act = (raw + up_bias).astype(jnp.bfloat16)
    row_at = lax.axis_index("lat") * out_rows - 1 + lax.broadcasted_iota(jnp.int32, (out_rows + 2, 1, 1), 0)
    inside = (row_at >= 0) & (row_at < out_rows * lat_count)
    activated = jax.nn.silu(pre_act.astype(jnp.float32)).astype(jnp.bfloat16)
    act_pad = jnp.where(inside, activated, jnp.zeros_like(activated))
    act_grad = lax.conv_general_dilated(
        grad_pad[None],
        back_mix,
        (1, 1),
        "VALID",
        dimension_numbers=("NHWC", "HWIO", "NHWC"),
        preferred_element_type=jnp.float32,
    )[0]
    pre_grad = (act_grad * slope(pre_act)).astype(jnp.bfloat16)
    pre_grad_pad = jnp.where(inside, pre_grad, jnp.zeros_like(pre_grad))
    patches = neighbours(act_pad, out_rows, out_cols, False)
    mix_flat = mix_kernel.reshape(9 * COUT, COUT)
    section_out = jnp.einsum(
        "rck,kn->rcn", patches, mix_flat, preferred_element_type=jnp.float32
    ).astype(jnp.bfloat16)
    grad_scale = 1.0 / math.sqrt(out_rows * lat_count * out_cols * lon_count)
    mix_span = COUT // lon_count
    mix_owned = jnp.einsum(
        "rctm,rcn->mtn",
        patches.reshape(out_rows, out_cols, 9, COUT),
        cotangent,
        preferred_element_type=jnp.float32,
    ).reshape(lon_count, mix_span, 9, COUT).transpose(0, 2, 1, 3)
    grad_patches = strided(pre_grad_pad, in_rows, in_cols)
    input_grad = jnp.einsum(
        "rctn,tmn->rcm",
        grad_patches.reshape(in_rows, in_cols, 16, COUT),
        up_kernel.reshape(16, CIN, COUT),
        preferred_element_type=jnp.float32,
    )
    up_taps = jnp.einsum(
        "rctn,rcm->tmn",
        grad_patches.reshape(in_rows, in_cols, 16, COUT),
        inputs,
        preferred_element_type=jnp.float32,
    )
    up_span = CIN // lon_count
    up_rows = 16 * up_span
    by_owner = [
        up_taps.reshape(16, lon_count, up_span, COUT).transpose(1, 0, 2, 3),
        mix_owned,
    ]
    terms = jnp.concatenate([t.reshape(lon_count, -1, COUT) for t in by_owner], axis=1)
    summed = reduce_terms(terms) * grad_scale
    up_part = summed[:up_rows].reshape(4, 4, up_span, COUT)
    mix_part = summed[up_rows:].reshape(3, 3, mix_span, COUT)
    return (section_out, input_grad, up_part, mix_part)


def exchange(part, axis, step):
    size = lax.axis_size(axis)
    return lax.ppermute(part, axis, [(i, i ^ step) for i in range(size)])


def halve(buffer, axis, step, dim):
    own = lax.axis_index(axis) // step % 2
    keep = lax.dynamic_index_in_dim(buffer, own, dim, keepdims=False)
    send = lax.dynamic_index_in_dim(buffer, 1 - own, dim, keepdims=False)
    return keep + exchange(send.astype(jnp.bfloat16), axis, step).astype(keep.dtype)


def double(part, axis, step):
    own = lax.axis_index(axis) // step % 2
    got = exchange(part, axis, step)
    low = jnp.where(own == 0, part, got)
    high = jnp.where(own == 0, got, part)
    return jnp.concatenate([low, high])


def steps_of(size):
    count = size.bit_length() - 1
    return [1 << k for k in range(count)] if size == 1 << count else None


def scatter_lon(rows, order):
    lon_count = rows.shape[0]
    steps = steps_of(lon_count)
    width = len(steps)
    grid = rows.reshape((2,) * width + rows.shape[1:])
    held = list(reversed(steps))
    for step in order:
        dim = held.index(step)
        grid = halve(grid, "lon", step, dim)
        held.pop(dim)
    return grid


def reduce_lat(flat):
    steps = steps_of(lax.axis_size("lat"))
    if steps is None or flat.shape[0] % 2:
        return lax.psum(flat, "lat")
    pair = flat.reshape((2, flat.shape[0] // 2) + flat.shape[1:])
    part = halve(pair, "lat", steps[0], 0).astype(jnp.bfloat16)
    for step in steps[1:]:
        got = exchange(part, "lat", step)
        part = (part.astype(jnp.float32) + got.astype(jnp.float32)).astype(jnp.bfloat16)
    return double(part, "lat", steps[0]).astype(jnp.float32)


def butterfly(part, steps):
    part = part.astype(jnp.bfloat16)
    for step in steps:
        got = exchange(part, "lat", step)
        part = (part.astype(jnp.float32) + got.astype(jnp.float32)).astype(jnp.bfloat16)
    return part


def reduce_terms(rows):
    lon_count, count = rows.shape[:2]
    steps = steps_of(lon_count)
    lat_steps = steps_of(lax.axis_size("lat"))
    if steps is None or lat_steps is None or count % 4:
        own = lax.axis_index("lon")
        mine = lax.dynamic_index_in_dim(lax.psum(rows, "lon"), own, 0, keepdims=False)
        return reduce_lat(mine)
    pair = rows.reshape((lon_count, 2, count // 2) + rows.shape[2:])
    part = halve(pair, "lat", lat_steps[0], 1)
    half = count // 4
    first = scatter_lon(part[:, :half], steps)
    second = scatter_lon(part[:, half:], list(reversed(steps)))
    joined = jnp.concatenate([butterfly(first, lat_steps[1:]), butterfly(second, lat_steps[1:])])
    return double(joined, "lat", lat_steps[0]).astype(jnp.float32)


def solution(mesh):
    placed = (P("lat", "lon", None), P("lat", "lon", None), P(), P(), P(), P("lat", "lon", None))
    return jax.shard_map(
        shards,
        mesh=mesh,
        in_specs=placed,
        out_specs=(
            P("lat", "lon", None),
            P("lat", "lon", None),
            P(None, None, "lon", None),
            P(None, None, "lon", None),
        ),
        check_vma=False,
    )
```

```python
import math

import jax
import jax.numpy as jnp
from jax import lax
from jax.sharding import PartitionSpec as P

CIN = 256
COUT = 128
BLOCK = 32


row_taps = (((1, 0), (3, -1)), ((0, 1), (2, 0)))


def swap_edges(fields, margins, axis, dim, wrap):
    size = lax.axis_size(axis)
    up = [(i, (i + 1) % size) for i in range(size if wrap else size - 1)]
    down = [(j, i) for i, j in up]
    lasts, leads = [], []
    for field, width in zip(fields, margins):
        length = field.shape[dim]
        lasts.append(lax.slice_in_dim(field, length - width, length, axis=dim))
        leads.append(lax.slice_in_dim(field, 0, width, axis=dim))
    before = lax.ppermute(jnp.concatenate([p.reshape(-1) for p in lasts]), axis, up)
    after = lax.ppermute(jnp.concatenate([p.reshape(-1) for p in leads]), axis, down)
    joined, at = [], 0
    for field, last, lead in zip(fields, lasts, leads):
        count = last.size
        head = before[at : at + count].reshape(last.shape)
        tail = after[at : at + count].reshape(lead.shape)
        joined.append(jnp.concatenate([head, field, tail], axis=dim))
        at += count
    return joined


def extend_all(fields, margins):
    widened = swap_edges(fields, margins, "lon", 1, True)
    return swap_edges(widened, margins, "lat", 0, False)


def decode(elem_codes, block_exps):
    sign_bit = elem_codes // 128
    exponent = elem_codes // 8 % 16
    mantissa = elem_codes % 8
    magnitude = jnp.exp2((exponent - 7).astype(jnp.float32)) * (
        1.0 + mantissa.astype(jnp.float32) / 8.0
    )
    signed = jnp.where(sign_bit == 1, -magnitude, magnitude)
    factor = jnp.repeat(jnp.exp2(block_exps.astype(jnp.float32)), BLOCK, axis=2)
    return (signed * factor).astype(jnp.bfloat16)


def slope(pre_act):
    plain = pre_act.astype(jnp.float32)
    sigmoid_v = jax.nn.sigmoid(plain)
    return sigmoid_v * (1.0 + plain * (1.0 - sigmoid_v))


def upsample(padded, up_kernel, row_count, col_count):
    halves = []
    for row_par in (1, 0):
        lane_list = []
        for col_par in (1, 0):
            pieces = []
            kernels = []
            for row_tap, row_off in row_taps[row_par]:
                for col_tap, col_off in row_taps[col_par]:
                    row_at = 1 + row_off - row_par
                    col_at = 1 + col_off - col_par
                    pieces.append(
                        padded[row_at : row_at + row_count + 1, col_at : col_at + col_count + 1]
                    )
                    kernels.append(up_kernel[row_tap, col_tap])
            stacked = jnp.concatenate(pieces, axis=2)
            kernel = jnp.concatenate(kernels, axis=0)
            lane_list.append(
                jnp.einsum("rck,kn->rcn", stacked, kernel, preferred_element_type=jnp.float32)
            )
        halves.append(jnp.stack(lane_list, axis=2))
    merged = jnp.stack(halves, axis=1)
    return merged.reshape(2 * row_count + 2, 2 * col_count + 2, merged.shape[-1])


def neighbours(padded, row_count, col_count, flipped):
    pieces = []
    for row_tap in range(3):
        for col_tap in range(3):
            row_at = 2 - row_tap if flipped else row_tap
            col_at = 2 - col_tap if flipped else col_tap
            pieces.append(padded[row_at : row_at + row_count, col_at : col_at + col_count])
    return jnp.concatenate(pieces, axis=2)


def strided(padded, row_count, col_count):
    split = padded.reshape(row_count + 1, 2, col_count + 1, 2, padded.shape[-1])
    pieces = []
    for row_tap in range(4):
        for col_tap in range(4):
            row_at, col_at = (row_tap // 2, col_tap // 2)
            pieces.append(
                split[
                    row_at : row_at + row_count,
                    row_tap % 2,
                    col_at : col_at + col_count,
                    col_tap % 2,
                ]
            )
    return jnp.concatenate(pieces, axis=2)


def shards(elem_codes, block_exps, up_kernel, up_bias, mix_kernel, cotangent):
    inputs = decode(elem_codes, block_exps)
    in_rows, in_cols = (inputs.shape[0], inputs.shape[1])
    out_rows, out_cols = (2 * in_rows, 2 * in_cols)
    lat_count = lax.axis_size("lat")
    lon_count = lax.axis_size("lon")
    back_mix = mix_kernel[::-1, ::-1].transpose(0, 1, 3, 2)
    padded_in, grad_pad = extend_all((inputs, cotangent), (1, 2))
    raw = upsample(padded_in, up_kernel, in_rows, in_cols)
    pre_act = (raw + up_bias).astype(jnp.bfloat16)
    row_at = lax.axis_index("lat") * out_rows - 1 + lax.broadcasted_iota(jnp.int32, (out_rows + 2, 1, 1), 0)
    inside = (row_at >= 0) & (row_at < out_rows * lat_count)
    activated = jax.nn.silu(pre_act.astype(jnp.float32)).astype(jnp.bfloat16)
    act_pad = jnp.where(inside, activated, jnp.zeros_like(activated))
    act_grad = lax.conv_general_dilated(
        grad_pad[None],
        back_mix,
        (1, 1),
        "VALID",
        dimension_numbers=("NHWC", "HWIO", "NHWC"),
        preferred_element_type=jnp.float32,
    )[0]
    pre_grad = (act_grad * slope(pre_act)).astype(jnp.bfloat16)
    pre_grad_pad = jnp.where(inside, pre_grad, jnp.zeros_like(pre_grad))
    patches = neighbours(act_pad, out_rows, out_cols, False)
    mix_flat = mix_kernel.reshape(9 * COUT, COUT)
    section_out = jnp.einsum(
        "rck,kn->rcn", patches, mix_flat, preferred_element_type=jnp.float32
    ).astype(jnp.bfloat16)
    grad_scale = 1.0 / math.sqrt(out_rows * lat_count * out_cols * lon_count)
    mix_span = COUT // lon_count
    mix_owned = jnp.einsum(
        "rctm,rcn->mtn",
        patches.reshape(out_rows, out_cols, 9, COUT),
        cotangent,
        preferred_element_type=jnp.float32,
    ).reshape(lon_count, mix_span, 9, COUT).transpose(0, 2, 1, 3)
    grad_patches = strided(pre_grad_pad, in_rows, in_cols)
    input_grad = jnp.einsum(
        "rctn,tmn->rcm",
        grad_patches.reshape(in_rows, in_cols, 16, COUT),
        up_kernel.reshape(16, CIN, COUT),
        preferred_element_type=jnp.float32,
    )
    up_taps = jnp.einsum(
        "rctn,rcm->tmn",
        grad_patches.reshape(in_rows, in_cols, 16, COUT),
        inputs,
        preferred_element_type=jnp.float32,
    )
    up_span = CIN // lon_count
    by_owner = [
        up_taps.reshape(16, lon_count, up_span, COUT).transpose(1, 0, 2, 3),
        mix_owned,
    ]
    up_sum, mix_sum = reduce_terms([t.reshape(lon_count, -1, COUT) for t in by_owner])
    up_part = (up_sum * grad_scale).reshape(4, 4, up_span, COUT)
    mix_part = (mix_sum * grad_scale).reshape(3, 3, mix_span, COUT)
    return (section_out, input_grad, up_part, mix_part)


def exchange(part, axis, step):
    size = lax.axis_size(axis)
    return lax.ppermute(part, axis, [(i, i ^ step) for i in range(size)])


def halve(buffer, axis, step, dim):
    own = lax.axis_index(axis) // step % 2
    keep = lax.dynamic_index_in_dim(buffer, own, dim, keepdims=False)
    send = lax.dynamic_index_in_dim(buffer, 1 - own, dim, keepdims=False)
    return keep + exchange(send.astype(jnp.bfloat16), axis, step).astype(keep.dtype)


def double(part, axis, step):
    own = lax.axis_index(axis) // step % 2
    got = exchange(part, axis, step)
    low = jnp.where(own == 0, part, got)
    high = jnp.where(own == 0, got, part)
    return jnp.concatenate([low, high])


def steps_of(size):
    count = size.bit_length() - 1
    return [1 << k for k in range(count)] if size == 1 << count else None


def scatter_lon(rows, order):
    lon_count = rows.shape[0]
    steps = steps_of(lon_count)
    width = len(steps)
    grid = rows.reshape((2,) * width + rows.shape[1:])
    held = list(reversed(steps))
    for step in order:
        dim = held.index(step)
        grid = halve(grid, "lon", step, dim)
        held.pop(dim)
    return grid


def reduce_lat(flat):
    steps = steps_of(lax.axis_size("lat"))
    if steps is None or flat.shape[0] % 2:
        return lax.psum(flat, "lat")
    pair = flat.reshape((2, flat.shape[0] // 2) + flat.shape[1:])
    part = halve(pair, "lat", steps[0], 0).astype(jnp.bfloat16)
    for step in steps[1:]:
        got = exchange(part, "lat", step)
        part = (part.astype(jnp.float32) + got.astype(jnp.float32)).astype(jnp.bfloat16)
    return double(part, "lat", steps[0]).astype(jnp.float32)


def butterfly(part, steps):
    part = part.astype(jnp.bfloat16)
    for step in steps:
        got = exchange(part, "lat", step)
        part = (part.astype(jnp.float32) + got.astype(jnp.float32)).astype(jnp.bfloat16)
    return part


def reduce_terms(terms):
    lon_count = terms[0].shape[0]
    sizes = [t.shape[1] for t in terms]
    steps = steps_of(lon_count)
    lat_steps = steps_of(lax.axis_size("lat"))
    if steps is None or lat_steps is None or any(n % 2 for n in sizes) or sum(sizes) % 32:
        rows = jnp.concatenate(terms, axis=1)
        own = lax.axis_index("lon")
        mine = lax.dynamic_index_in_dim(lax.psum(rows, "lon"), own, 0, keepdims=False)
        summed = reduce_lat(mine)
        return summed[: sizes[0]], summed[sizes[0] :]
    kept = [
        halve(t.reshape((lon_count, 2, t.shape[1] // 2) + t.shape[2:]), "lat", lat_steps[0], 1)
        for t in terms
    ]
    part = jnp.concatenate(kept, axis=1)
    half = part.shape[1] // 2
    first = scatter_lon(part[:, :half], steps)
    second = scatter_lon(part[:, half:], list(reversed(steps)))
    joined = jnp.concatenate([butterfly(first, lat_steps[1:]), butterfly(second, lat_steps[1:])])
    low, high = jnp.split(double(joined, "lat", lat_steps[0]).astype(jnp.float32), 2)
    cut = sizes[0] // 2
    return (jnp.concatenate([low[:cut], high[:cut]]), jnp.concatenate([low[cut:], high[cut:]]))


def solution(mesh):
    placed = (P("lat", "lon", None), P("lat", "lon", None), P(), P(), P(), P("lat", "lon", None))
    return jax.shard_map(
        shards,
        mesh=mesh,
        in_specs=placed,
        out_specs=(
            P("lat", "lon", None),
            P("lat", "lon", None),
            P(None, None, "lon", None),
            P(None, None, "lon", None),
        ),
        check_vma=False,
    )
```

```python
import math

import jax
import jax.numpy as jnp
from jax import lax
from jax.sharding import PartitionSpec as P

CIN = 256
COUT = 128
BLOCK = 32


row_taps = (((1, 0), (3, -1)), ((0, 1), (2, 0)))


def swap_edges(fields, margins, axis, dim, wrap):
    size = lax.axis_size(axis)
    up = [(i, (i + 1) % size) for i in range(size if wrap else size - 1)]
    down = [(j, i) for i, j in up]
    lasts, leads = [], []
    for field, width in zip(fields, margins):
        length = field.shape[dim]
        lasts.append(lax.slice_in_dim(field, length - width, length, axis=dim))
        leads.append(lax.slice_in_dim(field, 0, width, axis=dim))
    before = lax.ppermute(jnp.concatenate([p.reshape(-1) for p in lasts]), axis, up)
    after = lax.ppermute(jnp.concatenate([p.reshape(-1) for p in leads]), axis, down)
    joined, at = [], 0
    for field, last, lead in zip(fields, lasts, leads):
        count = last.size
        head = before[at : at + count].reshape(last.shape)
        tail = after[at : at + count].reshape(lead.shape)
        joined.append(jnp.concatenate([head, field, tail], axis=dim))
        at += count
    return joined


def extend_all(fields, margins):
    widened = swap_edges(fields, margins, "lon", 1, True)
    return swap_edges(widened, margins, "lat", 0, False)


def decode(elem_codes, block_exps):
    sign_bit = elem_codes // 128
    exponent = elem_codes // 8 % 16
    mantissa = elem_codes % 8
    magnitude = jnp.exp2((exponent - 7).astype(jnp.float32)) * (
        1.0 + mantissa.astype(jnp.float32) / 8.0
    )
    signed = jnp.where(sign_bit == 1, -magnitude, magnitude)
    factor = jnp.repeat(jnp.exp2(block_exps.astype(jnp.float32)), BLOCK, axis=2)
    return (signed * factor).astype(jnp.bfloat16)


def slope(pre_act):
    plain = pre_act.astype(jnp.float32)
    sigmoid_v = jax.nn.sigmoid(plain)
    return sigmoid_v * (1.0 + plain * (1.0 - sigmoid_v))


def upsample(padded, up_kernel, row_count, col_count):
    halves = []
    for row_par in (1, 0):
        lane_list = []
        for col_par in (1, 0):
            pieces = []
            kernels = []
            for row_tap, row_off in row_taps[row_par]:
                for col_tap, col_off in row_taps[col_par]:
                    row_at = 1 + row_off - row_par
                    col_at = 1 + col_off - col_par
                    pieces.append(
                        padded[row_at : row_at + row_count + 1, col_at : col_at + col_count + 1]
                    )
                    kernels.append(up_kernel[row_tap, col_tap])
            stacked = jnp.concatenate(pieces, axis=2)
            kernel = jnp.concatenate(kernels, axis=0)
            lane_list.append(
                jnp.einsum("rck,kn->rcn", stacked, kernel, preferred_element_type=jnp.float32)
            )
        halves.append(jnp.stack(lane_list, axis=2))
    merged = jnp.stack(halves, axis=1)
    return merged.reshape(2 * row_count + 2, 2 * col_count + 2, merged.shape[-1])


def neighbours(padded, row_count, col_count, flipped):
    pieces = []
    for row_tap in range(3):
        for col_tap in range(3):
            row_at = 2 - row_tap if flipped else row_tap
            col_at = 2 - col_tap if flipped else col_tap
            pieces.append(padded[row_at : row_at + row_count, col_at : col_at + col_count])
    return jnp.concatenate(pieces, axis=2)


def strided(padded, row_count, col_count):
    split = padded.reshape(row_count + 1, 2, col_count + 1, 2, padded.shape[-1])
    pieces = []
    for row_tap in range(4):
        for col_tap in range(4):
            row_at, col_at = (row_tap // 2, col_tap // 2)
            pieces.append(
                split[
                    row_at : row_at + row_count,
                    row_tap % 2,
                    col_at : col_at + col_count,
                    col_tap % 2,
                ]
            )
    return jnp.concatenate(pieces, axis=2)


def shards(elem_codes, block_exps, up_kernel, up_bias, mix_kernel, cotangent):
    inputs = decode(elem_codes, block_exps)
    in_rows, in_cols = (inputs.shape[0], inputs.shape[1])
    out_rows, out_cols = (2 * in_rows, 2 * in_cols)
    lat_count = lax.axis_size("lat")
    lon_count = lax.axis_size("lon")
    back_mix = mix_kernel[::-1, ::-1].transpose(0, 1, 3, 2)
    padded_in, grad_pad = extend_all((inputs, cotangent), (1, 2))
    raw = upsample(padded_in, up_kernel, in_rows, in_cols)
    pre_act = (raw + up_bias).astype(jnp.bfloat16)
    row_at = lax.axis_index("lat") * out_rows - 1 + lax.broadcasted_iota(jnp.int32, (out_rows + 2, 1, 1), 0)
    inside = (row_at >= 0) & (row_at < out_rows * lat_count)
    activated = jax.nn.silu(pre_act.astype(jnp.float32)).astype(jnp.bfloat16)
    act_pad = jnp.where(inside, activated, jnp.zeros_like(activated))
    act_grad = lax.conv_general_dilated(
        grad_pad[None],
        back_mix,
        (1, 1),
        "VALID",
        dimension_numbers=("NHWC", "HWIO", "NHWC"),
        preferred_element_type=jnp.float32,
    )[0]
    pre_grad = (act_grad * slope(pre_act)).astype(jnp.bfloat16)
    pre_grad_pad = jnp.where(inside, pre_grad, jnp.zeros_like(pre_grad))
    patches = neighbours(act_pad, out_rows, out_cols, False)
    mix_flat = mix_kernel.reshape(9 * COUT, COUT)
    section_out = jnp.einsum(
        "rck,kn->rcn", patches, mix_flat, preferred_element_type=jnp.float32
    ).astype(jnp.bfloat16)
    grad_scale = 1.0 / math.sqrt(out_rows * lat_count * out_cols * lon_count)
    mix_span = COUT // lon_count
    mix_owned = jnp.einsum(
        "rctm,rcn->mtn",
        patches.reshape(out_rows, out_cols, 9, COUT),
        cotangent,
        preferred_element_type=jnp.float32,
    ).reshape(lon_count, mix_span, 9, COUT).transpose(0, 2, 1, 3)
    grad_patches = strided(pre_grad_pad, in_rows, in_cols)
    input_grad = jnp.einsum(
        "rctn,tmn->rcm",
        grad_patches.reshape(in_rows, in_cols, 16, COUT),
        up_kernel.reshape(16, CIN, COUT),
        preferred_element_type=jnp.float32,
    )
    up_owned = jnp.einsum(
        "rctn,rcom->otmn",
        grad_patches.reshape(in_rows, in_cols, 16, COUT),
        inputs.reshape(in_rows, in_cols, lon_count, CIN // lon_count),
        preferred_element_type=jnp.float32,
    )
    up_span = CIN // lon_count
    up_rows = 16 * up_span
    by_owner = [
        up_owned,
        mix_owned,
    ]
    terms = jnp.concatenate([t.reshape(lon_count, -1, COUT) for t in by_owner], axis=1)
    summed = reduce_terms(terms) * grad_scale
    up_part = summed[:up_rows].reshape(4, 4, up_span, COUT)
    mix_part = summed[up_rows:].reshape(3, 3, mix_span, COUT)
    return (section_out, input_grad, up_part, mix_part)


def exchange(part, axis, step):
    size = lax.axis_size(axis)
    return lax.ppermute(part, axis, [(i, i ^ step) for i in range(size)])


def halve(buffer, axis, step, dim):
    own = lax.axis_index(axis) // step % 2
    keep = lax.dynamic_index_in_dim(buffer, own, dim, keepdims=False)
    send = lax.dynamic_index_in_dim(buffer, 1 - own, dim, keepdims=False)
    return keep + exchange(send.astype(jnp.bfloat16), axis, step).astype(keep.dtype)


def double(part, axis, step):
    own = lax.axis_index(axis) // step % 2
    got = exchange(part, axis, step)
    low = jnp.where(own == 0, part, got)
    high = jnp.where(own == 0, got, part)
    return jnp.concatenate([low, high])


def steps_of(size):
    count = size.bit_length() - 1
    return [1 << k for k in range(count)] if size == 1 << count else None


def scatter_lon(rows, order):
    lon_count = rows.shape[0]
    steps = steps_of(lon_count)
    width = len(steps)
    grid = rows.reshape((2,) * width + rows.shape[1:])
    held = list(reversed(steps))
    for step in order:
        dim = held.index(step)
        grid = halve(grid, "lon", step, dim)
        held.pop(dim)
    return grid


def reduce_lat(flat):
    steps = steps_of(lax.axis_size("lat"))
    if steps is None or flat.shape[0] % 2:
        return lax.psum(flat, "lat")
    pair = flat.reshape((2, flat.shape[0] // 2) + flat.shape[1:])
    part = halve(pair, "lat", steps[0], 0).astype(jnp.bfloat16)
    for step in steps[1:]:
        got = exchange(part, "lat", step)
        part = (part.astype(jnp.float32) + got.astype(jnp.float32)).astype(jnp.bfloat16)
    return double(part, "lat", steps[0]).astype(jnp.float32)


def butterfly(part, steps):
    part = part.astype(jnp.bfloat16)
    for step in steps:
        got = exchange(part, "lat", step)
        part = (part.astype(jnp.float32) + got.astype(jnp.float32)).astype(jnp.bfloat16)
    return part


def reduce_terms(rows):
    lon_count, count = rows.shape[:2]
    steps = steps_of(lon_count)
    lat_steps = steps_of(lax.axis_size("lat"))
    if steps is None or lat_steps is None or count % 4:
        own = lax.axis_index("lon")
        mine = lax.dynamic_index_in_dim(lax.psum(rows, "lon"), own, 0, keepdims=False)
        return reduce_lat(mine)
    pair = rows.reshape((lon_count, 2, count // 2) + rows.shape[2:])
    part = halve(pair, "lat", lat_steps[0], 1)
    half = count // 4
    first = scatter_lon(part[:, :half], steps)
    second = scatter_lon(part[:, half:], list(reversed(steps)))
    joined = jnp.concatenate([butterfly(first, lat_steps[1:]), butterfly(second, lat_steps[1:])])
    return double(joined, "lat", lat_steps[0]).astype(jnp.float32)


def solution(mesh):
    placed = (P("lat", "lon", None), P("lat", "lon", None), P(), P(), P(), P("lat", "lon", None))
    return jax.shard_map(
        shards,
        mesh=mesh,
        in_specs=placed,
        out_specs=(
            P("lat", "lon", None),
            P("lat", "lon", None),
            P(None, None, "lon", None),
            P(None, None, "lon", None),
        ),
        check_vma=False,
    )
```

```python
import math

import jax
import jax.numpy as jnp
from jax import lax
from jax.sharding import PartitionSpec as P

CIN = 256
COUT = 128
BLOCK = 32


row_taps = (((1, 0), (3, -1)), ((0, 1), (2, 0)))


def swap_edges(fields, margins, axis, dim, wrap):
    size = lax.axis_size(axis)
    up = [(i, (i + 1) % size) for i in range(size if wrap else size - 1)]
    down = [(j, i) for i, j in up]
    lasts, leads = [], []
    for field, width in zip(fields, margins):
        length = field.shape[dim]
        lasts.append(lax.slice_in_dim(field, length - width, length, axis=dim))
        leads.append(lax.slice_in_dim(field, 0, width, axis=dim))
    before = lax.ppermute(jnp.concatenate([p.reshape(-1) for p in lasts]), axis, up)
    after = lax.ppermute(jnp.concatenate([p.reshape(-1) for p in leads]), axis, down)
    joined, at = [], 0
    for field, last, lead in zip(fields, lasts, leads):
        count = last.size
        head = before[at : at + count].reshape(last.shape)
        tail = after[at : at + count].reshape(lead.shape)
        joined.append(jnp.concatenate([head, field, tail], axis=dim))
        at += count
    return joined


def extend_all(fields, margins):
    widened = swap_edges(fields, margins, "lon", 1, True)
    return swap_edges(widened, margins, "lat", 0, False)


def decode(elem_codes, block_exps):
    sign_bit = elem_codes // 128
    exponent = elem_codes // 8 % 16
    mantissa = elem_codes % 8
    magnitude = jnp.exp2((exponent - 7).astype(jnp.float32)) * (
        1.0 + mantissa.astype(jnp.float32) / 8.0
    )
    signed = jnp.where(sign_bit == 1, -magnitude, magnitude)
    factor = jnp.repeat(jnp.exp2(block_exps.astype(jnp.float32)), BLOCK, axis=2)
    return (signed * factor).astype(jnp.bfloat16)


def slope(pre_act):
    plain = pre_act.astype(jnp.float32)
    sigmoid_v = jax.nn.sigmoid(plain)
    return sigmoid_v * (1.0 + plain * (1.0 - sigmoid_v))


def upsample(padded, up_kernel, row_count, col_count):
    halves = []
    for row_par in (1, 0):
        lane_list = []
        for col_par in (1, 0):
            pieces = []
            kernels = []
            for row_tap, row_off in row_taps[row_par]:
                for col_tap, col_off in row_taps[col_par]:
                    row_at = 1 + row_off - row_par
                    col_at = 1 + col_off - col_par
                    pieces.append(
                        padded[row_at : row_at + row_count + 1, col_at : col_at + col_count + 1]
                    )
                    kernels.append(up_kernel[row_tap, col_tap])
            stacked = jnp.concatenate(pieces, axis=2)
            kernel = jnp.concatenate(kernels, axis=0)
            lane_list.append(
                jnp.einsum("rck,kn->rcn", stacked, kernel, preferred_element_type=jnp.float32)
            )
        halves.append(jnp.stack(lane_list, axis=2))
    merged = jnp.stack(halves, axis=1)
    return merged.reshape(2 * row_count + 2, 2 * col_count + 2, merged.shape[-1])


def neighbours(padded, row_count, col_count, flipped):
    pieces = []
    for row_tap in range(3):
        for col_tap in range(3):
            row_at = 2 - row_tap if flipped else row_tap
            col_at = 2 - col_tap if flipped else col_tap
            pieces.append(padded[row_at : row_at + row_count, col_at : col_at + col_count])
    return jnp.concatenate(pieces, axis=2)


def strided(padded, row_count, col_count):
    split = padded.reshape(row_count + 1, 2, col_count + 1, 2, padded.shape[-1])
    pieces = []
    for row_tap in range(4):
        for col_tap in range(4):
            row_at, col_at = (row_tap // 2, col_tap // 2)
            pieces.append(
                split[
                    row_at : row_at + row_count,
                    row_tap % 2,
                    col_at : col_at + col_count,
                    col_tap % 2,
                ]
            )
    return jnp.concatenate(pieces, axis=2)


def shards(elem_codes, block_exps, up_kernel, up_bias, mix_kernel, cotangent):
    inputs = decode(elem_codes, block_exps)
    in_rows, in_cols = (inputs.shape[0], inputs.shape[1])
    out_rows, out_cols = (2 * in_rows, 2 * in_cols)
    lat_count = lax.axis_size("lat")
    lon_count = lax.axis_size("lon")
    back_mix = mix_kernel[::-1, ::-1].transpose(0, 1, 3, 2)
    padded_in, grad_pad = extend_all((inputs, cotangent), (1, 2))
    raw = upsample(padded_in, up_kernel, in_rows, in_cols)
    pre_act = (raw + up_bias).astype(jnp.bfloat16)
    row_at = lax.axis_index("lat") * out_rows - 1 + lax.broadcasted_iota(jnp.int32, (out_rows + 2, 1, 1), 0)
    inside = (row_at >= 0) & (row_at < out_rows * lat_count)
    activated = jax.nn.silu(pre_act.astype(jnp.float32)).astype(jnp.bfloat16)
    act_pad = jnp.where(inside, activated, jnp.zeros_like(activated))
    act_grad = lax.conv_general_dilated(
        grad_pad[None],
        back_mix,
        (1, 1),
        "VALID",
        dimension_numbers=("NHWC", "HWIO", "NHWC"),
        preferred_element_type=jnp.float32,
    )[0]
    pre_grad = (act_grad * slope(pre_act)).astype(jnp.bfloat16)
    pre_grad_pad = jnp.where(inside, pre_grad, jnp.zeros_like(pre_grad))
    patches = neighbours(act_pad, out_rows, out_cols, False)
    mix_flat = mix_kernel.reshape(9 * COUT, COUT)
    section_out = jnp.einsum(
        "rck,kn->rcn", patches, mix_flat, preferred_element_type=jnp.float32
    ).astype(jnp.bfloat16)
    grad_scale = 1.0 / math.sqrt(out_rows * lat_count * out_cols * lon_count)
    mix_span = COUT // lon_count
    mix_owned = jnp.einsum(
        "rctm,rcn->mtn",
        patches.reshape(out_rows, out_cols, 9, COUT),
        cotangent,
        preferred_element_type=jnp.float32,
    ).reshape(lon_count, mix_span, 9, COUT).transpose(0, 2, 1, 3)
    grad_patches = strided(pre_grad_pad, in_rows, in_cols)
    input_grad = jnp.einsum(
        "rctn,tmn->rcm",
        grad_patches.reshape(in_rows, in_cols, 16, COUT),
        up_kernel.reshape(16, CIN, COUT),
        preferred_element_type=jnp.float32,
    )
    up_taps = jnp.einsum(
        "rctn,rcm->tmn",
        grad_patches.reshape(in_rows, in_cols, 16, COUT),
        inputs,
        preferred_element_type=jnp.float32,
    )
    up_span = CIN // lon_count
    up_rows = 16 * up_span
    by_owner = [
        up_taps.reshape(16, lon_count, up_span, COUT).transpose(1, 0, 2, 3),
        mix_owned,
    ]
    terms = jnp.concatenate([t.reshape(lon_count, -1, COUT) for t in by_owner], axis=1)
    summed = reduce_terms(terms) * grad_scale
    up_part = summed[:up_rows].reshape(4, 4, up_span, COUT)
    mix_part = summed[up_rows:].reshape(3, 3, mix_span, COUT)
    return (section_out, input_grad, up_part, mix_part)


def exchange(part, axis, step):
    size = lax.axis_size(axis)
    return lax.ppermute(part, axis, [(i, i ^ step) for i in range(size)])


def halve(buffer, axis, step, dim):
    own = lax.axis_index(axis) // step % 2
    keep = lax.dynamic_index_in_dim(buffer, own, dim, keepdims=False)
    send = lax.dynamic_index_in_dim(buffer, 1 - own, dim, keepdims=False)
    return keep + exchange(send.astype(jnp.bfloat16), axis, step).astype(keep.dtype)


def double(part, axis, step):
    own = lax.axis_index(axis) // step % 2
    got = exchange(part, axis, step)
    low = jnp.where(own == 0, part, got)
    high = jnp.where(own == 0, got, part)
    return jnp.concatenate([low, high])


def steps_of(size):
    count = size.bit_length() - 1
    return [1 << k for k in range(count)] if size == 1 << count else None


def scatter_lon(rows, order):
    lon_count = rows.shape[0]
    steps = steps_of(lon_count)
    width = len(steps)
    grid = rows.reshape((2,) * width + rows.shape[1:])
    held = list(reversed(steps))
    for step in order:
        dim = held.index(step)
        grid = halve(grid, "lon", step, dim)
        held.pop(dim)
    return grid


def reduce_lat(flat):
    steps = steps_of(lax.axis_size("lat"))
    if steps is None or flat.shape[0] % 2:
        return lax.psum(flat, "lat")
    pair = flat.reshape((2, flat.shape[0] // 2) + flat.shape[1:])
    part = halve(pair, "lat", steps[0], 0).astype(jnp.bfloat16)
    for step in steps[1:]:
        got = exchange(part, "lat", step)
        part = (part.astype(jnp.float32) + got.astype(jnp.float32)).astype(jnp.bfloat16)
    return double(part, "lat", steps[0]).astype(jnp.float32)


def butterfly(part, steps):
    part = part.astype(jnp.bfloat16)
    for step in steps:
        got = exchange(part, "lat", step)
        part = (part.astype(jnp.float32) + got.astype(jnp.float32)).astype(jnp.bfloat16)
    return part


def reduce_terms(rows):
    lon_count, count = rows.shape[:2]
    steps = steps_of(lon_count)
    lat_steps = steps_of(lax.axis_size("lat"))
    if steps is None or lat_steps is None or count % 4:
        own = lax.axis_index("lon")
        mine = lax.dynamic_index_in_dim(lax.psum(rows, "lon"), own, 0, keepdims=False)
        return reduce_lat(mine)
    pair = rows.reshape((lon_count, 2, count // 2) + rows.shape[2:])
    part = halve(pair, "lat", lat_steps[0], 1)
    half = count // 4
    first = scatter_lon(part[:, :half], steps)
    second = scatter_lon(part[:, half:], list(reversed(steps)))
    order = list(reversed(lat_steps[1:]))
    joined = jnp.concatenate([butterfly(first, order), butterfly(second, order)])
    return double(joined, "lat", lat_steps[0]).astype(jnp.float32)


def solution(mesh):
    placed = (P("lat", "lon", None), P("lat", "lon", None), P(), P(), P(), P("lat", "lon", None))
    return jax.shard_map(
        shards,
        mesh=mesh,
        in_specs=placed,
        out_specs=(
            P("lat", "lon", None),
            P("lat", "lon", None),
            P(None, None, "lon", None),
            P(None, None, "lon", None),
        ),
        check_vma=False,
    )
```

```python
import math

import jax
import jax.numpy as jnp
from jax import lax
from jax.sharding import PartitionSpec as P

CIN = 256
COUT = 128
BLOCK = 32


row_taps = (((1, 0), (3, -1)), ((0, 1), (2, 0)))


def swap_edges(fields, margins, axis, dim, wrap):
    size = lax.axis_size(axis)
    up = [(i, (i + 1) % size) for i in range(size if wrap else size - 1)]
    down = [(j, i) for i, j in up]
    lasts, leads = [], []
    for field, width in zip(fields, margins):
        length = field.shape[dim]
        lasts.append(lax.slice_in_dim(field, length - width, length, axis=dim))
        leads.append(lax.slice_in_dim(field, 0, width, axis=dim))
    before = lax.ppermute(jnp.concatenate([p.reshape(-1) for p in lasts]), axis, up)
    after = lax.ppermute(jnp.concatenate([p.reshape(-1) for p in leads]), axis, down)
    joined, at = [], 0
    for field, last, lead in zip(fields, lasts, leads):
        count = last.size
        head = before[at : at + count].reshape(last.shape)
        tail = after[at : at + count].reshape(lead.shape)
        joined.append(jnp.concatenate([head, field, tail], axis=dim))
        at += count
    return joined


def extend_all(fields, margins):
    widened = swap_edges(fields, margins, "lon", 1, True)
    return swap_edges(widened, margins, "lat", 0, False)


def decode(elem_codes, block_exps):
    sign_bit = elem_codes // 128
    exponent = elem_codes // 8 % 16
    mantissa = elem_codes % 8
    magnitude = jnp.exp2((exponent - 7).astype(jnp.float32)) * (
        1.0 + mantissa.astype(jnp.float32) / 8.0
    )
    signed = jnp.where(sign_bit == 1, -magnitude, magnitude)
    factor = jnp.repeat(jnp.exp2(block_exps.astype(jnp.float32)), BLOCK, axis=2)
    return (signed * factor).astype(jnp.bfloat16)


def slope(pre_act):
    plain = pre_act.astype(jnp.float32)
    sigmoid_v = jax.nn.sigmoid(plain)
    return sigmoid_v * (1.0 + plain * (1.0 - sigmoid_v))


def upsample(padded, up_kernel, row_count, col_count):
    halves = []
    for row_par in (1, 0):
        lane_list = []
        for col_par in (1, 0):
            pieces = []
            kernels = []
            for row_tap, row_off in row_taps[row_par]:
                for col_tap, col_off in row_taps[col_par]:
                    row_at = 1 + row_off - row_par
                    col_at = 1 + col_off - col_par
                    pieces.append(
                        padded[row_at : row_at + row_count + 1, col_at : col_at + col_count + 1]
                    )
                    kernels.append(up_kernel[row_tap, col_tap])
            stacked = jnp.concatenate(pieces, axis=2)
            kernel = jnp.concatenate(kernels, axis=0)
            lane_list.append(
                jnp.einsum("rck,kn->rcn", stacked, kernel, preferred_element_type=jnp.float32)
            )
        halves.append(jnp.stack(lane_list, axis=2))
    merged = jnp.stack(halves, axis=1)
    return merged.reshape(2 * row_count + 2, 2 * col_count + 2, merged.shape[-1])


def neighbours(padded, row_count, col_count, flipped):
    pieces = []
    for row_tap in range(3):
        for col_tap in range(3):
            row_at = 2 - row_tap if flipped else row_tap
            col_at = 2 - col_tap if flipped else col_tap
            pieces.append(padded[row_at : row_at + row_count, col_at : col_at + col_count])
    return jnp.concatenate(pieces, axis=2)


def strided(padded, row_count, col_count):
    split = padded.reshape(row_count + 1, 2, col_count + 1, 2, padded.shape[-1])
    pieces = []
    for row_tap in range(4):
        for col_tap in range(4):
            row_at, col_at = (row_tap // 2, col_tap // 2)
            pieces.append(
                split[
                    row_at : row_at + row_count,
                    row_tap % 2,
                    col_at : col_at + col_count,
                    col_tap % 2,
                ]
            )
    return jnp.concatenate(pieces, axis=2)


def shards(elem_codes, block_exps, up_kernel, up_bias, mix_kernel, cotangent):
    inputs = decode(elem_codes, block_exps)
    in_rows, in_cols = (inputs.shape[0], inputs.shape[1])
    out_rows, out_cols = (2 * in_rows, 2 * in_cols)
    lat_count = lax.axis_size("lat")
    lon_count = lax.axis_size("lon")
    back_mix = mix_kernel[::-1, ::-1].transpose(0, 1, 3, 2)
    padded_in, grad_pad = extend_all((inputs, cotangent), (1, 2))
    raw = upsample(padded_in, up_kernel, in_rows, in_cols)
    pre_act = (raw + up_bias).astype(jnp.bfloat16)
    row_at = lax.axis_index("lat") * out_rows - 1 + lax.broadcasted_iota(jnp.int32, (out_rows + 2, 1, 1), 0)
    inside = (row_at >= 0) & (row_at < out_rows * lat_count)
    activated = jax.nn.silu(pre_act.astype(jnp.float32)).astype(jnp.bfloat16)
    act_pad = jnp.where(inside, activated, jnp.zeros_like(activated))
    act_grad = lax.conv_general_dilated(
        grad_pad[None],
        back_mix,
        (1, 1),
        "VALID",
        dimension_numbers=("NHWC", "HWIO", "NHWC"),
        preferred_element_type=jnp.float32,
    )[0]
    pre_grad = (act_grad * slope(pre_act)).astype(jnp.bfloat16)
    pre_grad_pad = jnp.where(inside, pre_grad, jnp.zeros_like(pre_grad))
    patches = neighbours(act_pad, out_rows, out_cols, False)
    mix_flat = mix_kernel.reshape(9 * COUT, COUT)
    section_out = jnp.einsum(
        "rck,kn->rcn", patches, mix_flat, preferred_element_type=jnp.float32
    ).astype(jnp.bfloat16)
    grad_scale = 1.0 / math.sqrt(out_rows * lat_count * out_cols * lon_count)
    mix_span = COUT // lon_count
    mix_owned = jnp.einsum(
        "rctm,rcn->mtn",
        patches.reshape(out_rows, out_cols, 9, COUT),
        cotangent,
        preferred_element_type=jnp.float32,
    ).reshape(lon_count, mix_span, 9, COUT).transpose(0, 2, 1, 3)
    grad_patches = strided(pre_grad_pad, in_rows, in_cols)
    input_grad = jnp.einsum(
        "rctn,tmn->rcm",
        grad_patches.reshape(in_rows, in_cols, 16, COUT),
        up_kernel.reshape(16, CIN, COUT),
        preferred_element_type=jnp.float32,
    )
    up_taps = jnp.einsum(
        "rctn,rcm->tmn",
        grad_patches.reshape(in_rows, in_cols, 16, COUT),
        inputs,
        preferred_element_type=jnp.float32,
    )
    up_span = CIN // lon_count
    up_rows = 16 * up_span
    by_owner = [
        up_taps.reshape(16, lon_count, up_span, COUT).transpose(1, 0, 2, 3),
        mix_owned,
    ]
    terms = jnp.concatenate([t.reshape(lon_count, -1, COUT) for t in by_owner], axis=1)
    summed = reduce_terms(terms) * grad_scale
    up_part = summed[:up_rows].reshape(4, 4, up_span, COUT)
    mix_part = summed[up_rows:].reshape(3, 3, mix_span, COUT)
    return (section_out, input_grad, up_part, mix_part)


def exchange(part, axis, step):
    size = lax.axis_size(axis)
    return lax.ppermute(part, axis, [(i, i ^ step) for i in range(size)])


def halve(buffer, axis, step, dim):
    own = lax.axis_index(axis) // step % 2
    keep = lax.dynamic_index_in_dim(buffer, own, dim, keepdims=False)
    send = lax.dynamic_index_in_dim(buffer, 1 - own, dim, keepdims=False)
    return keep + exchange(send.astype(jnp.bfloat16), axis, step).astype(keep.dtype)


def double(part, axis, step):
    own = lax.axis_index(axis) // step % 2
    got = exchange(part, axis, step)
    low = jnp.where(own == 0, part, got)
    high = jnp.where(own == 0, got, part)
    return jnp.concatenate([low, high])


def steps_of(size):
    count = size.bit_length() - 1
    return [1 << k for k in range(count)] if size == 1 << count else None


def scatter_lon(rows, order):
    lon_count = rows.shape[0]
    steps = steps_of(lon_count)
    width = len(steps)
    grid = rows.reshape((2,) * width + rows.shape[1:])
    held = list(reversed(steps))
    for step in order:
        dim = held.index(step)
        grid = halve(grid, "lon", step, dim)
        held.pop(dim)
    return grid


def reduce_lat(flat):
    steps = steps_of(lax.axis_size("lat"))
    if steps is None or flat.shape[0] % 2:
        return lax.psum(flat, "lat")
    pair = flat.reshape((2, flat.shape[0] // 2) + flat.shape[1:])
    part = halve(pair, "lat", steps[0], 0).astype(jnp.bfloat16)
    for step in steps[1:]:
        got = exchange(part, "lat", step)
        part = (part.astype(jnp.float32) + got.astype(jnp.float32)).astype(jnp.bfloat16)
    return double(part, "lat", steps[0]).astype(jnp.float32)


def butterfly(part, steps):
    part = part.astype(jnp.bfloat16)
    for step in steps:
        got = exchange(part, "lat", step)
        part = (part.astype(jnp.float32) + got.astype(jnp.float32)).astype(jnp.bfloat16)
    return part


def reduce_terms(rows):
    lon_count, count = rows.shape[:2]
    steps = steps_of(lon_count)
    lat_steps = steps_of(lax.axis_size("lat"))
    if steps is None or lat_steps is None or count % 4:
        own = lax.axis_index("lon")
        mine = lax.dynamic_index_in_dim(lax.psum(rows, "lon"), own, 0, keepdims=False)
        return reduce_lat(mine)
    pair = rows.reshape((lon_count, 2, count // 2) + rows.shape[2:])
    part = halve(pair, "lat", lat_steps[0], 1)
    half = count // 4
    first = scatter_lon(part[:, :half], steps)
    second = scatter_lon(part[:, half:], list(reversed(steps)))
    order = list(reversed(lat_steps[1:]))
    joined = jnp.concatenate([butterfly(first, order), butterfly(second, order[::-1])])
    return double(joined, "lat", lat_steps[0]).astype(jnp.float32)


def solution(mesh):
    placed = (P("lat", "lon", None), P("lat", "lon", None), P(), P(), P(), P("lat", "lon", None))
    return jax.shard_map(
        shards,
        mesh=mesh,
        in_specs=placed,
        out_specs=(
            P("lat", "lon", None),
            P("lat", "lon", None),
            P(None, None, "lon", None),
            P(None, None, "lon", None),
        ),
        check_vma=False,
    )
```
